128 devices in a mesh: gx: 16 (over y, z_hi, core), gy: 8 (over x, z_lo).
Axes of the slice: x: 4, y: 4, z: 4 (z_hi: 2, z_lo: 2; z = z_hi * 2 + z_lo), core: 2. Of those that a mesh axis runs over, the one named last changes fastest.
Arguments:
- theta: float32 [60, 512, 4096], P(None, 'gx', 'gy'), may hold values from -6 to 6
- winds: float32 [2, 60, 512, 4096], P(None, None, 'gx', 'gy'), may hold values from -4 to 4
- theta_bar: float32 [60, 512, 4096], P(None, 'gx', 'gy'), may hold values from -6 to 6
- press_bar: float32 [60, 512, 4096], P(None, 'gx', 'gy'), may hold values from -6 to 6
- urban_frac: float32 [512, 4096], P('gx', 'gy'), may hold values from 0.1 to 0.9
- wall_temp: float32 [512, 4096], P('gx', 'gy'), may hold values from -6 to 6
- urban_class: int32 [512, 4096], P('gx', 'gy'), may hold values from 0 to 10
- canopy_layers: int32 [512, 4096], P('gx', 'gy'), may hold values from 1 to 8
- height_bin: int32 [512, 4096], P('gx', 'gy'), may hold values from 0 to 14
- class_drag: float32 [11], replicated, may hold values from 0.05 to 0.5
- bin_profile: float32 [15, 60], replicated, may hold values from 0.2 to 1
- sound_coef: float32 [60], replicated, may hold values from 0.2 to 2
Outputs:
- theta_grad: float32 [60, 512, 4096], P(None, 'gx', 'gy')
- press_grad: float32 [60, 512, 4096], P(None, 'gx', 'gy')
- frac_grad: float32 [512, 4096], P('gx', 'gy')
- wall_grad: float32 [512, 4096], P('gx', 'gy')
The draws below stay inside these ranges and needn't reach their ends.
All inputs are finite; a program needn't handle non-finite values.
Results may differ from the reference program's by a relative error of at most 0.00016.
Values sent between devices are 32-bit elements; how exact they have to be, the bound alone decides.
No kernel may reach another device: no remote copies, remote signals or barrier semaphores. Data moves between devices by JAX's collectives and lax.ppermute only.
A program may use at most 256 MiB of HBM per device.

```python
import math
import jax
import jax.numpy as jnp
from jax import lax

NZ = 60
NCLASS = 11
NBIN = 15
NLMAX = 8
NX = 512
NY = 4096


def with_ends(drawn, own_key, smallest, largest):
    longest = drawn.shape.index(max(drawn.shape))
    spots = []
    for shift in (0, 1):
        where = [jax.random.randint(jax.random.fold_in(own_key, axis), (), 0, length) for axis, length in enumerate(drawn.shape)]
        where[longest] = (where[longest] + shift) % drawn.shape[longest]
        spots.append(tuple(where))
    return drawn.at[spots[0]].set(smallest).at[spots[1]].set(largest)


def block_scale(key, dims, pieces, smallest, largest):
    factor_of = 1.0
    for dim, blocks in pieces:
        steps = jax.random.uniform(jax.random.fold_in(jax.random.fold_in(key, 6), dim), (blocks,), jnp.float32, smallest / len(pieces), largest / len(pieces))
        factor_of = factor_of * jnp.repeat(jnp.exp(steps), dims[dim] // blocks).reshape((-1,) + (1,) * (len(dims) - 1 - dim))
    return factor_of


def centred(stream_key, extent, scale, most, split=(), kind=jnp.bfloat16):
    level = block_scale(stream_key, extent, split, -0.22, 0.18) if split else 1.0
    values = jax.random.normal(stream_key, extent, jnp.float32) * scale * level
    return jnp.minimum(jnp.maximum(values, -most), most).astype(kind)


def setup_inputs(seed: int = 0) -> dict:
    key_list = jax.random.split(jax.random.key(seed), 13)
    return {
        "theta": centred(key_list[0], (NZ, NX, NY), 1.0, 6.0, ((1, 16), (2, 8)), jnp.float32),
        "winds": centred(key_list[1], (2, NZ, NX, NY), 1.0, 4.0, ((2, 16), (3, 8)), jnp.float32),
        "theta_bar": centred(key_list[2], (NZ, NX, NY), 1.0, 6.0, ((1, 16), (2, 8)), jnp.float32),
        "press_bar": centred(key_list[3], (NZ, NX, NY), 1.0, 6.0, ((1, 16), (2, 8)), jnp.float32),
        "urban_frac": jnp.clip(0.1 + 0.79999997 * jax.random.uniform(key_list[4], (NX, NY), jnp.float32) ** block_scale(key_list[4], (NX, NY), ((0, 16), (1, 8)), -0.2, 0.2), 0.1, 0.9),
        "wall_temp": centred(key_list[5], (NX, NY), 1.0, 6.0, ((0, 16), (1, 8)), jnp.float32),
        "urban_class": with_ends(jax.random.randint(key_list[6], (NX, NY), 0, NCLASS), jax.random.fold_in(key_list[6], 1), 0, NCLASS - 1).astype(jnp.int32),
        "canopy_layers": with_ends(jax.random.randint(key_list[7], (NX, NY), 1, NLMAX + 1), jax.random.fold_in(key_list[7], 1), 1, NLMAX).astype(jnp.int32),
        "height_bin": with_ends(jax.random.randint(key_list[8], (NX, NY), 0, NBIN), jax.random.fold_in(key_list[8], 1), 0, NBIN - 1).astype(jnp.int32),
        "class_drag": jnp.clip(jnp.exp(jax.random.uniform(key_list[9], (NCLASS,), jnp.float32, math.log(0.05), math.log(0.5))), 0.05, 0.5),
        "bin_profile": jnp.clip(jax.random.uniform(key_list[10], (NBIN, NZ), jnp.float32, 0.2, 1.0), 0.2, 1.0),
        "sound_coef": jnp.clip(jnp.exp(jax.random.uniform(key_list[11], (NZ,), jnp.float32, math.log(0.2), math.log(2.0))), 0.2, 2.0),
    }


courant = 0.3
diffusion = 0.1
buoyancy = 0.5
upwind_table = ((1.0, 1.0), (-8.0, -5.0), (37.0, 10.0), (37.0, -10.0), (-8.0, 5.0), (1.0, -1.0))

def take_part(array, start, count, axis):
    return lax.slice_in_dim(array, start, start + count, axis=axis)

def pad_three(field, axis):
    widths = [(0, 0)] * field.ndim
    widths[axis] = (3, 3)
    return jnp.pad(field, widths)

def forward_tend(padded, wind_pad, axis):
    count = padded.shape[axis] - 6
    speed = take_part(wind_pad, 2, count + 1, axis)
    magnitude = jnp.abs(speed)
    flux = jnp.zeros_like(speed)
    for offset, pair in enumerate(upwind_table):
        flux = flux + (pair[0] * speed + pair[1] * magnitude) / 60.0 * take_part(padded, offset, count + 1, axis)
    return -courant * (take_part(flux, 1, count, axis) - take_part(flux, 0, count, axis))

def adjoint_tend(padded, wind_pad, axis):
    count = padded.shape[axis] - 6
    face_bar = courant * (take_part(padded, 1, count + 5, axis) - take_part(padded, 0, count + 5, axis))
    speed = take_part(wind_pad, 0, count + 5, axis)
    magnitude = jnp.abs(speed)
    result = jnp.zeros_like(take_part(padded, 3, count, axis))
    for offset, pair in enumerate(upwind_table):
        weighted = (pair[0] * speed + pair[1] * magnitude) / 60.0 * face_bar
        result = result + take_part(weighted, 5 - offset, count, axis)
    return result

def level_forward(items):
    field, east, north = items
    return forward_tend(pad_three(field, 0), pad_three(east, 0), 0) + forward_tend(pad_three(field, 1), pad_three(north, 1), 1)

def level_adjoint(items):
    field, east, north = items
    return adjoint_tend(pad_three(field, 0), pad_three(east, 0), 0) + adjoint_tend(pad_three(field, 1), pad_three(north, 1), 1)

def laplace(field):
    padded = jnp.pad(field, ((0, 0), (1, 1), (1, 1)))
    return padded[:, 2:, 1:-1] + padded[:, :-2, 1:-1] + padded[:, 1:-1, 2:] + padded[:, 1:-1, :-2] - 4.0 * field

def solve_transposed(field, sound_coef):
    levels, rows, columns = field.shape
    zero_one = jnp.zeros((1,), sound_coef.dtype)
    lower = jnp.concatenate([zero_one, -sound_coef[:-1]])
    upper = jnp.concatenate([-sound_coef[1:], zero_one])
    middle = 1.0 + 2.0 * sound_coef
    flat = field.reshape(levels, rows * columns)
    solved = lax.linalg.tridiagonal_solve(lower, middle, upper, flat)
    return solved.reshape(levels, rows, columns)

def reference(theta, winds, theta_bar, press_bar, urban_frac, wall_temp, urban_class, canopy_layers, height_bin, class_drag, bin_profile, sound_coef):
    drag_col = class_drag[urban_class]
    profile = jnp.transpose(bin_profile[height_bin], (2, 0, 1))
    levels = jnp.arange(theta.shape[0], dtype=jnp.int32)[:, None, None]
    active = (levels < canopy_layers[None]).astype(theta.dtype)
    amount = urban_frac[None] * drag_col[None] * profile * active
    first = theta + lax.map(level_forward, (theta, winds[0], winds[1]))
    press_back = press_bar
    stacked_q = jnp.zeros_like(theta)
    for substep in range(2):
        solved = solve_transposed(press_back, sound_coef)
        stacked_q = stacked_q + solved
        press_back = solved + diffusion * laplace(solved)
    press_grad = press_back
    second_bar = theta_bar + buoyancy * stacked_q
    first_bar = (1.0 - amount) * second_bar
    theta_grad = first_bar + lax.map(level_adjoint, (first_bar, winds[0], winds[1]))
    frac_grad = jnp.sum(drag_col[None] * profile * active * (wall_temp[None] - first) * second_bar, axis=0)
    wall_grad = jnp.sum(amount * second_bar, axis=0)
    return (theta_grad, press_grad, frac_grad, wall_grad)
```

```python
import functools

import jax
import jax.numpy as jnp
from jax import lax
from jax.experimental import pallas as pl
from jax.experimental.pallas import tpu as pltpu
from jax.sharding import PartitionSpec as P

courant = 0.3
diffusion = 0.1
buoyancy = 0.5
canopy_levels = 8
halo_rows = 8
strip = 128
block_levels = 12


def from_side(x, axis, delta):
    n = lax.axis_size(axis)
    if delta > 0:
        pairs = [(i + delta, i) for i in range(n - delta)]
    else:
        pairs = [(i, i - delta) for i in range(n + delta)]
    return lax.ppermute(x, axis, pairs)


def from_corner(x, dx, dy):
    nx, ny = lax.axis_size("gx"), lax.axis_size("gy")
    pairs = []
    for ix in range(nx):
        for iy in range(ny):
            sx, sy = ix + dx, iy + dy
            if 0 <= sx < nx and 0 <= sy < ny:
                pairs.append((sx * ny + sy, ix * ny + iy))
    return lax.ppermute(x, ("gx", "gy"), pairs)


def row_halo(f, lo, hi):
    levels, rows, cols = f.shape
    parts = []
    if hi:
        parts.append(from_side(f[:, :hi, :], "gx", 1))
    parts.append(jnp.zeros((levels, halo_rows - hi - lo, cols), f.dtype))
    if lo:
        parts.append(from_side(f[:, rows - lo :, :], "gx", -1))
    return jnp.concatenate(parts, axis=1)


def col_halo(f, lo, hi):
    levels, rows, cols = f.shape
    parts = []
    if hi:
        parts.append(from_side(f[:, :, :hi], "gy", 1))
    parts.append(jnp.zeros((levels, rows, strip - hi - lo), f.dtype))
    if lo:
        parts.append(from_side(f[:, :, cols - lo :], "gy", -1))
    return jnp.concatenate(parts, axis=2)


def corner_rows(f, w):
    levels, rows, cols = f.shape
    mid = jnp.zeros((levels, w, strip - 2 * w), f.dtype)
    gap = jnp.zeros((levels, halo_rows - 2 * w, strip), f.dtype)
    top = jnp.concatenate(
        [from_corner(f[:, :w, :w], 1, 1), mid, from_corner(f[:, :w, cols - w :], 1, -1)], axis=2
    )
    bottom = jnp.concatenate(
        [from_corner(f[:, rows - w :, :w], -1, 1), mid, from_corner(f[:, rows - w :, cols - w :], -1, -1)],
        axis=2,
    )
    return jnp.concatenate([top, gap, bottom], axis=1)


def ahead(x, k, axis):
    if k == 0:
        return x
    n = x.shape[axis]
    return pltpu.roll(x, (-k) % n, axis)


def forward_tend(f, u, axis):
    fm2, fm1, f0, f1, f2, f3 = [ahead(f, k, axis) for k in (-2, -1, 0, 1, 2, 3)]
    a_sum = (fm2 + f3) - 8.0 * (fm1 + f2) + 37.0 * (f0 + f1)
    b_sum = (fm2 - f3) - 5.0 * (fm1 - f2) + 10.0 * (f0 - f1)
    flux = (u * a_sum + jnp.abs(u) * b_sum) * (1.0 / 60.0)
    return -courant * (flux - ahead(flux, -1, axis))


def adjoint_tend(f, u, axis):
    g = courant * (ahead(f, 1, axis) - f)
    pu = u * g
    qu = jnp.abs(u) * g
    total = (
        ahead(pu + qu, 2, axis)
        + ahead(-8.0 * pu - 5.0 * qu, 1, axis)
        + (37.0 * pu + 10.0 * qu)
        + ahead(37.0 * pu - 10.0 * qu, -1, axis)
        + ahead(-8.0 * pu + 5.0 * qu, -2, axis)
        + ahead(pu - qu, -3, axis)
    )
    return total * (1.0 / 60.0)


def laplace(q):
    return ahead(q, 1, 0) + ahead(q, -1, 0) + ahead(q, 1, 1) + ahead(q, -1, 1) - 4.0 * q


def extend(main, rows, cols):
    return jnp.concatenate([jnp.concatenate([main, rows], axis=0), cols], axis=1)


def kernel(
    lo_ref, mid_ref, up_ref,
    pbm, pbx, pby, tbm, tbx, tby, u0m, u1m, u0x, u1y, thm, thx, thy, amt, dpa, wall, mask,
    tg_out, pg_out, fg_out, wg_out,
    dd, qa, car_a, car_b, cpc, cp1, cq2,
):
    phase = pl.program_id(0)
    blk = pl.program_id(1)
    nblk = pl.num_programs(1)
    lz = pbm.shape[0]
    rows, cols = pbm.shape[1], pbm.shape[2]
    wide = cpc.shape[1]

    def coef(ref, k):
        return jnp.full((1, wide), ref[k], jnp.float32)

    @pl.when(phase == 0)
    def _():
        @pl.when(blk == 0)
        def _():
            car_a[...] = jnp.zeros(car_a.shape, jnp.float32)
            cpc[...] = jnp.zeros(cpc.shape, jnp.float32)

        def body(j, c):
            k = blk * lz + j
            ak = coef(lo_ref, k)
            r = 1.0 / (coef(mid_ref, k) - ak * cpc[...])
            cp = coef(up_ref, k) * r
            cpc[...] = cp
            cp1[k] = cp
            d = extend(pbm[j], pbx[j], pby[j])
            dn = (d - ak * car_a[...]) * r
            car_a[...] = dn
            dd[k] = dn
            return c

        lax.fori_loop(0, lz, body, 0)

    @pl.when(phase == 1)
    def _():
        @pl.when(blk == 0)
        def _():
            car_a[...] = jnp.zeros(car_a.shape, jnp.float32)
            car_b[...] = jnp.zeros(car_b.shape, jnp.float32)
            cpc[...] = jnp.zeros(cpc.shape, jnp.float32)

        def body(j, c):
            k = (nblk - 1 - blk) * lz + (lz - 1 - j)
            x = dd[k] - cp1[k] * car_a[...]
            car_a[...] = x
            qa[k] = x
            pb1 = (x + diffusion * laplace(x)) * mask[...]
            ck = coef(up_ref, k)
            s = 1.0 / (coef(mid_ref, k) - ck * cpc[...])
            cq = coef(lo_ref, k) * s
            cpc[...] = cq
            cq2[k] = cq
            e = (pb1 - ck * car_b[...]) * s
            car_b[...] = e
            dd[k] = e
            return c

        lax.fori_loop(0, lz, body, 0)

    @pl.when(phase == 2)
    def _():
        @pl.when(blk == 0)
        def _():
            car_a[...] = jnp.zeros(car_a.shape, jnp.float32)

        def level(j, canopy, acc):
            k = blk * lz + j
            qb = dd[k] - cq2[k] * car_a[...]
            car_a[...] = qb
            pg = qb + diffusion * laplace(qb)
            pg_out[j] = pg[:rows, :cols]
            th2b = extend(tbm[j], tbx[j], tby[j]) + buoyancy * (qa[k] + qb)
            if canopy:
                am = amt[j]
                th1b = (1.0 - am) * th2b
            else:
                th1b = th2b
            u0e = jnp.concatenate([u0m[j], u0x[j]], axis=0)
            u1e = jnp.concatenate([u1m[j], u1y[j]], axis=1)
            adv = adjoint_tend(th1b[:, :cols], u0e, 0)[:rows, :] + adjoint_tend(th1b[:rows, :], u1e, 1)[:, :cols]
            tg_out[j] = th1b[:rows, :cols] + adv
            if canopy:
                th = thm[j]
                fx = forward_tend(jnp.concatenate([th, thx[j]], axis=0), u0e, 0)[:rows, :]
                fy = forward_tend(jnp.concatenate([th, thy[j]], axis=1), u1e, 1)[:, :cols]
                first = th + (fx + fy)
                sb = th2b[:rows, :cols]
                fg, wg = acc
                fg = fg + dpa[j] * (wall[...] - first) * sb
                wg = wg + am[:rows, :cols] * sb
                acc = (fg, wg)
            return acc

        @pl.when(blk == 0)
        def _():
            zero = jnp.zeros((rows, cols), jnp.float32)
            fg, wg = lax.fori_loop(0, canopy_levels, lambda j, a: level(j, True, a), (zero, zero))
            fg_out[...] = fg
            wg_out[...] = wg
            lax.fori_loop(canopy_levels, lz, lambda j, a: level(j, False, a), 0)

        @pl.when(blk > 0)
        def _():
            lax.fori_loop(0, lz, lambda j, a: level(j, False, a), 0)


def per_device(
    theta, winds, theta_bar, press_bar, urban_frac, wall_temp, urban_class, canopy_layers,
    height_bin, class_drag, bin_profile, sound_coef,
):
    levels, rows, cols = theta.shape
    rext, cext = rows + halo_rows, cols + strip
    lz = block_levels
    nblk = levels // lz
    kc = canopy_levels

    drag = jnp.zeros((rows, cols), jnp.float32)
    for c in range(class_drag.shape[0]):
        drag = jnp.where(urban_class == c, class_drag[c], drag)
    prof = jnp.zeros((kc, rows, cols), jnp.float32)
    for bb in range(bin_profile.shape[0]):
        prof = jnp.where(height_bin[None] == bb, bin_profile[bb, :kc][:, None, None], prof)
    active = (jnp.arange(kc, dtype=jnp.int32)[:, None, None] < canopy_layers[None]).astype(jnp.float32)
    amount8 = urban_frac[None] * drag[None] * prof * active
    dpa8 = drag[None] * prof * active
    amt_ext = extend_xla(amount8, row_halo(amount8, 3, 3), col_halo(amount8, 3, 3), None)

    ix = lax.axis_index("gx")
    iy = lax.axis_index("gy")
    nx, ny = lax.axis_size("gx"), lax.axis_size("gy")
    r = jnp.arange(rext, dtype=jnp.int32)[:, None]
    cc = jnp.arange(cext, dtype=jnp.int32)[None, :]
    row_ok = (r < rows) | ((r < rows + 4) & (ix < nx - 1)) | ((r >= rext - 4) & (ix > 0))
    col_ok = (cc < cols) | ((cc < cols + 4) & (iy < ny - 1)) | ((cc >= cext - 4) & (iy > 0))
    mask = (row_ok & col_ok).astype(jnp.float32)

    pbx = row_halo(press_bar, 4, 4)
    pby = jnp.concatenate([col_halo(press_bar, 4, 4), corner_rows(press_bar, 4)], axis=1)
    tbx = row_halo(theta_bar, 3, 3)
    tby = jnp.concatenate(
        [col_halo(theta_bar, 3, 3), jnp.zeros((levels, halo_rows, strip), jnp.float32)], axis=1
    )
    u0x = row_halo(winds[0], 3, 2)
    u1y = col_halo(winds[1], 3, 2)
    th8 = theta[:kc]
    thx = row_halo(th8, 3, 3)
    thy = col_halo(th8, 3, 3)

    zero1 = jnp.zeros((1,), jnp.float32)
    lower = jnp.concatenate([zero1, -sound_coef[:-1]])
    upper = jnp.concatenate([-sound_coef[1:], zero1])
    middle = 1.0 + 2.0 * sound_coef

    def lvl(which):
        if which == 0:
            return lambda p, b: (jnp.where(p == 0, b, nblk - 1), 0, 0)
        return lambda p, b: (jnp.where(p == 2, b, 0), 0, 0)

    const3 = lambda p, b: (0, 0, 0)
    const2 = lambda p, b: (0, 0)
    smem = pl.BlockSpec(memory_space=pltpu.SMEM)
    in_specs = [
        smem, smem, smem,
        pl.BlockSpec((lz, rows, cols), lvl(0)),
        pl.BlockSpec((lz, halo_rows, cols), lvl(0)),
        pl.BlockSpec((lz, rext, strip), lvl(0)),
        pl.BlockSpec((lz, rows, cols), lvl(2)),
        pl.BlockSpec((lz, halo_rows, cols), lvl(2)),
        pl.BlockSpec((lz, rext, strip), lvl(2)),
        pl.BlockSpec((None, lz, rows, cols), lambda p, b: (0, jnp.where(p == 2, b, 0), 0, 0)),
        pl.BlockSpec((None, lz, rows, cols), lambda p, b: (1, jnp.where(p == 2, b, 0), 0, 0)),
        pl.BlockSpec((lz, halo_rows, cols), lvl(2)),
        pl.BlockSpec((lz, rows, strip), lvl(2)),
        pl.BlockSpec((kc, rows, cols), const3),
        pl.BlockSpec((kc, halo_rows, cols), const3),
        pl.BlockSpec((kc, rows, strip), const3),
        pl.BlockSpec((kc, rext, cext), const3),
        pl.BlockSpec((kc, rows, cols), const3),
        pl.BlockSpec((rows, cols), const2),
        pl.BlockSpec((rext, cext), const2),
    ]
    out_specs = [
        pl.BlockSpec((lz, rows, cols), lvl(2)),
        pl.BlockSpec((lz, rows, cols), lvl(2)),
        pl.BlockSpec((rows, cols), const2),
        pl.BlockSpec((rows, cols), const2),
    ]
    out_shape = [
        jax.ShapeDtypeStruct((levels, rows, cols), jnp.float32),
        jax.ShapeDtypeStruct((levels, rows, cols), jnp.float32),
        jax.ShapeDtypeStruct((rows, cols), jnp.float32),
        jax.ShapeDtypeStruct((rows, cols), jnp.float32),
    ]
    scratch = [
        pltpu.VMEM((levels, rext, cext), jnp.float32),
        pltpu.VMEM((levels, rext, cext), jnp.float32),
        pltpu.VMEM((rext, cext), jnp.float32),
        pltpu.VMEM((rext, cext), jnp.float32),
        pltpu.VMEM((1, cext), jnp.float32),
        pltpu.VMEM((levels, 1, cext), jnp.float32),
        pltpu.VMEM((levels, 1, cext), jnp.float32),
    ]
    call = pl.pallas_call(
        kernel,
        grid=(3, nblk),
        in_specs=in_specs,
        out_specs=out_specs,
        out_shape=out_shape,
        scratch_shapes=scratch,
        compiler_params=pltpu.CompilerParams(
            dimension_semantics=("arbitrary", "arbitrary"),
            vmem_limit_bytes=56 * 1024 * 1024,
        ),
    )
    tg, pg, fg, wg = call(
        lower, middle, upper,
        press_bar, pbx, pby, theta_bar, tbx, tby, winds, winds, u0x, u1y,
        theta, thx, thy, amt_ext, dpa8, wall_temp, mask,
    )
    return tg, pg, fg, wg


def extend_xla(main, rows, cols, corner):
    levels = main.shape[0]
    if corner is None:
        corner = jnp.zeros((levels, rows.shape[1], cols.shape[2]), main.dtype)
    return jnp.concatenate(
        [jnp.concatenate([main, rows], axis=1), jnp.concatenate([cols, corner], axis=1)], axis=2
    )


def solution(mesh):
    in_specs = (
        P(None, "gx", "gy"),
        P(None, None, "gx", "gy"),
        P(None, "gx", "gy"),
        P(None, "gx", "gy"),
        P("gx", "gy"),
        P("gx", "gy"),
        P("gx", "gy"),
        P("gx", "gy"),
        P("gx", "gy"),
        P(),
        P(),
        P(),
    )
    out_specs = (P(None, "gx", "gy"), P(None, "gx", "gy"), P("gx", "gy"), P("gx", "gy"))
    return jax.shard_map(
        per_device, mesh=mesh, in_specs=in_specs, out_specs=out_specs, check_vma=False
    )
```

```python
import functools

import jax
import jax.numpy as jnp
from jax import lax
from jax.experimental import pallas as pl
from jax.experimental.pallas import tpu as pltpu
from jax.sharding import PartitionSpec as P

courant = 0.3
diffusion = 0.1
buoyancy = 0.5
canopy_levels = 8
halo_rows = 8
strip = 128
block_levels = 12


def from_side(x, axis, delta):
    n = lax.axis_size(axis)
    if delta > 0:
        pairs = [(i + delta, i) for i in range(n - delta)]
    else:
        pairs = [(i, i - delta) for i in range(n + delta)]
    return lax.ppermute(x, axis, pairs)


def from_corner(x, dx, dy):
    nx, ny = lax.axis_size("gx"), lax.axis_size("gy")
    pairs = []
    for ix in range(nx):
        for iy in range(ny):
            sx, sy = ix + dx, iy + dy
            if 0 <= sx < nx and 0 <= sy < ny:
                pairs.append((sx * ny + sy, ix * ny + iy))
    return lax.ppermute(x, ("gx", "gy"), pairs)


def row_halo(f, lo, hi):
    levels, rows, cols = f.shape
    parts = []
    if hi:
        parts.append(from_side(f[:, :hi, :], "gx", 1))
    parts.append(jnp.zeros((levels, halo_rows - hi - lo, cols), f.dtype))
    if lo:
        parts.append(from_side(f[:, rows - lo :, :], "gx", -1))
    return jnp.concatenate(parts, axis=1)


def col_halo(f, lo, hi):
    levels, rows, cols = f.shape
    parts = []
    if hi:
        parts.append(from_side(f[:, :, :hi], "gy", 1))
    parts.append(jnp.zeros((levels, rows, strip - hi - lo), f.dtype))
    if lo:
        parts.append(from_side(f[:, :, cols - lo :], "gy", -1))
    return jnp.concatenate(parts, axis=2)


def corner_rows(f, w):
    levels, rows, cols = f.shape
    mid = jnp.zeros((levels, w, strip - 2 * w), f.dtype)
    gap = jnp.zeros((levels, halo_rows - 2 * w, strip), f.dtype)
    top = jnp.concatenate(
        [from_corner(f[:, :w, :w], 1, 1), mid, from_corner(f[:, :w, cols - w :], 1, -1)], axis=2
    )
    bottom = jnp.concatenate(
        [from_corner(f[:, rows - w :, :w], -1, 1), mid, from_corner(f[:, rows - w :, cols - w :], -1, -1)],
        axis=2,
    )
    return jnp.concatenate([top, gap, bottom], axis=1)


def ahead(x, k, axis):
    if k == 0:
        return x
    n = x.shape[axis]
    return pltpu.roll(x, (-k) % n, axis)


def forward_tend(f, u, axis):
    fm2, fm1, f0, f1, f2, f3 = [ahead(f, k, axis) for k in (-2, -1, 0, 1, 2, 3)]
    a_sum = (fm2 + f3) - 8.0 * (fm1 + f2) + 37.0 * (f0 + f1)
    b_sum = (fm2 - f3) - 5.0 * (fm1 - f2) + 10.0 * (f0 - f1)
    flux = (u * a_sum + jnp.abs(u) * b_sum) * (1.0 / 60.0)
    return -courant * (flux - ahead(flux, -1, axis))


def adjoint_tend(f, u, axis):
    g = courant * (ahead(f, 1, axis) - f)
    pu = u * g
    qu = jnp.abs(u) * g
    total = (
        ahead(pu + qu, 2, axis)
        + ahead(-8.0 * pu - 5.0 * qu, 1, axis)
        + (37.0 * pu + 10.0 * qu)
        + ahead(37.0 * pu - 10.0 * qu, -1, axis)
        + ahead(-8.0 * pu + 5.0 * qu, -2, axis)
        + ahead(pu - qu, -3, axis)
    )
    return total * (1.0 / 60.0)


def laplace(q):
    return ahead(q, 1, 0) + ahead(q, -1, 0) + ahead(q, 1, 1) + ahead(q, -1, 1) - 4.0 * q


def extend(main, rows, cols):
    return jnp.concatenate([jnp.concatenate([main, rows], axis=0), cols], axis=1)


def kernel(
    lo_ref, mid_ref, up_ref, bp_ref,
    pbm, pbx, pby, tbm, tbx, tby, u0m, u1m, u0x, u1y, thm, thx, thy, f2e, drag, wall, mask,
    tg_out, pg_out, fg_out, wg_out,
    dd, qa, car_a, car_b, cpc, cp1, cq2,
):
    phase = pl.program_id(0)
    blk = pl.program_id(1)
    nblk = pl.num_programs(1)
    lz = pbm.shape[0]
    rows, cols = pbm.shape[1], pbm.shape[2]
    wide = cpc.shape[1]

    def coef(ref, k):
        return jnp.full((1, wide), ref[k], jnp.float32)

    @pl.when(phase == 0)
    def _():
        @pl.when(blk == 0)
        def _():
            car_a[...] = jnp.zeros(car_a.shape, jnp.float32)
            cpc[...] = jnp.zeros(cpc.shape, jnp.float32)

        def body(j, c):
            k = blk * lz + j
            ak = coef(lo_ref, k)
            r = 1.0 / (coef(mid_ref, k) - ak * cpc[...])
            cp = coef(up_ref, k) * r
            cpc[...] = cp
            cp1[k] = cp
            d = extend(pbm[j], pbx[j], pby[j])
            dn = (d - ak * car_a[...]) * r
            car_a[...] = dn
            dd[k] = dn
            return c

        lax.fori_loop(0, lz, body, 0)

    @pl.when(phase == 1)
    def _():
        @pl.when(blk == 0)
        def _():
            car_a[...] = jnp.zeros(car_a.shape, jnp.float32)
            car_b[...] = jnp.zeros(car_b.shape, jnp.float32)
            cpc[...] = jnp.zeros(cpc.shape, jnp.float32)

        def body(j, c):
            k = (nblk - 1 - blk) * lz + (lz - 1 - j)
            x = dd[k] - cp1[k] * car_a[...]
            car_a[...] = x
            qa[k] = x
            pb1 = (x + diffusion * laplace(x)) * mask[...]
            ck = coef(up_ref, k)
            s = 1.0 / (coef(mid_ref, k) - ck * cpc[...])
            cq = coef(lo_ref, k) * s
            cpc[...] = cq
            cq2[k] = cq
            e = (pb1 - ck * car_b[...]) * s
            car_b[...] = e
            dd[k] = e
            return c

        lax.fori_loop(0, lz, body, 0)

    @pl.when(phase == 2)
    def _():
        @pl.when(blk == 0)
        def _():
            car_a[...] = jnp.zeros(car_a.shape, jnp.float32)

        def level(j, canopy, acc):
            k = blk * lz + j
            qb = dd[k] - cq2[k] * car_a[...]
            car_a[...] = qb
            pg = qb + diffusion * laplace(qb)
            pg_out[j] = pg[:rows, :cols]
            th2b = extend(tbm[j], tbx[j], tby[j]) + buoyancy * (qa[k] + qb)
            if canopy:
                hb = f2e[1]
                prof = jnp.zeros(hb.shape, jnp.float32)
                for bb in range(bp_ref.shape[0] // canopy_levels):
                    prof = jnp.where(hb == float(bb), bp_ref[bb * canopy_levels + j], prof)
                act = jnp.where(f2e[2] > j.astype(jnp.float32), 1.0, 0.0)
                am = f2e[0] * prof * act
                th1b = (1.0 - am) * th2b
            else:
                th1b = th2b
            u0e = jnp.concatenate([u0m[j], u0x[j]], axis=0)
            u1e = jnp.concatenate([u1m[j], u1y[j]], axis=1)
            adv = adjoint_tend(th1b[:, :cols], u0e, 0)[:rows, :] + adjoint_tend(th1b[:rows, :], u1e, 1)[:, :cols]
            tg_out[j] = th1b[:rows, :cols] + adv
            if canopy:
                th = thm[j]
                fx = forward_tend(jnp.concatenate([th, thx[j]], axis=0), u0e, 0)[:rows, :]
                fy = forward_tend(jnp.concatenate([th, thy[j]], axis=1), u1e, 1)[:, :cols]
                first = th + (fx + fy)
                sb = th2b[:rows, :cols]
                fg, wg = acc
                dpa = drag[...] * prof[:rows, :cols] * act[:rows, :cols]
                fg = fg + dpa * (wall[...] - first) * sb
                wg = wg + am[:rows, :cols] * sb
                acc = (fg, wg)
            return acc

        @pl.when(blk == 0)
        def _():
            zero = jnp.zeros((rows, cols), jnp.float32)
            fg, wg = lax.fori_loop(0, canopy_levels, lambda j, a: level(j, True, a), (zero, zero))
            fg_out[...] = fg
            wg_out[...] = wg
            lax.fori_loop(canopy_levels, lz, lambda j, a: level(j, False, a), 0)

        @pl.when(blk > 0)
        def _():
            lax.fori_loop(0, lz, lambda j, a: level(j, False, a), 0)


def per_device(
    theta, winds, theta_bar, press_bar, urban_frac, wall_temp, urban_class, canopy_layers,
    height_bin, class_drag, bin_profile, sound_coef,
):
    levels, rows, cols = theta.shape
    rext, cext = rows + halo_rows, cols + strip
    lz = block_levels
    nblk = levels // lz
    kc = canopy_levels

    drag = jnp.zeros((rows, cols), jnp.float32)
    for c in range(class_drag.shape[0]):
        drag = jnp.where(urban_class == c, class_drag[c], drag)
    fields2d = jnp.stack(
        [urban_frac * drag, height_bin.astype(jnp.float32), canopy_layers.astype(jnp.float32)]
    )
    nf = fields2d.shape[0]
    th8 = theta[:kc]
    u0, u1 = winds[0], winds[1]

    def extra_rows(sel):
        e = jnp.concatenate([th8[:, sel, :].reshape(-1, cols), fields2d[:, sel, :].reshape(-1, cols)], axis=0)
        return jnp.pad(e, ((0, levels - e.shape[0]), (0, 0)))[:, None, :]

    def extra_cols(sel):
        t = jnp.swapaxes(th8[:, :, sel], 1, 2).reshape(-1, rows)
        f = jnp.swapaxes(fields2d[:, :, sel], 1, 2).reshape(-1, rows)
        e = jnp.concatenate([t, f], axis=0)
        return jnp.pad(e, ((0, levels - e.shape[0]), (0, 0)))[:, :, None]

    z = lambda *shape: jnp.zeros(shape, jnp.float32)
    nt, n2 = kc * 3, nf * 3
    first = jnp.concatenate(
        [press_bar[:, :4], theta_bar[:, :3], u0[:, :2], extra_rows(slice(0, 3))], axis=1
    )
    last = jnp.concatenate(
        [press_bar[:, rows - 4 :], theta_bar[:, rows - 3 :], u0[:, rows - 3 :], extra_rows(slice(rows - 3, rows))],
        axis=1,
    )
    nxt = from_side(first, "gx", 1)
    prv = from_side(last, "gx", -1)
    pbx = jnp.concatenate([nxt[:, 0:4], prv[:, 0:4]], axis=1)
    tbx = jnp.concatenate([nxt[:, 4:7], z(levels, 2, cols), prv[:, 4:7]], axis=1)
    u0x = jnp.concatenate([nxt[:, 7:9], z(levels, 3, cols), prv[:, 7:10]], axis=1)
    en, ep = nxt[:, 9, :], prv[:, 10, :]
    thx = jnp.concatenate(
        [en[:nt].reshape(kc, 3, cols), z(kc, 2, cols), ep[:nt].reshape(kc, 3, cols)], axis=1
    )
    f2x = jnp.concatenate(
        [en[nt : nt + n2].reshape(nf, 3, cols), z(nf, 2, cols), ep[nt : nt + n2].reshape(nf, 3, cols)], axis=1
    )

    firsty = jnp.concatenate(
        [press_bar[:, :, :4], theta_bar[:, :, :3], u1[:, :, :2], extra_cols(slice(0, 3))], axis=2
    )
    lasty = jnp.concatenate(
        [press_bar[:, :, cols - 4 :], theta_bar[:, :, cols - 3 :], u1[:, :, cols - 3 :], extra_cols(slice(cols - 3, cols))],
        axis=2,
    )
    nyt = from_side(firsty, "gy", 1)
    pyv = from_side(lasty, "gy", -1)
    pby = jnp.concatenate(
        [
            jnp.concatenate([nyt[..., 0:4], z(levels, rows, strip - 8), pyv[..., 0:4]], axis=2),
            corner_rows(press_bar, 4),
        ],
        axis=1,
    )
    tby = jnp.concatenate(
        [
            jnp.concatenate([nyt[..., 4:7], z(levels, rows, strip - 6), pyv[..., 4:7]], axis=2),
            z(levels, halo_rows, strip),
        ],
        axis=1,
    )
    u1y = jnp.concatenate([nyt[..., 7:9], z(levels, rows, strip - 5), pyv[..., 7:10]], axis=2)
    eyn, eyp = nyt[:, :, 9], pyv[:, :, 10]
    thy = jnp.concatenate(
        [
            jnp.swapaxes(eyn[:nt].reshape(kc, 3, rows), 1, 2),
            z(kc, rows, strip - 6),
            jnp.swapaxes(eyp[:nt].reshape(kc, 3, rows), 1, 2),
        ],
        axis=2,
    )
    f2y = jnp.concatenate(
        [
            jnp.swapaxes(eyn[nt : nt + n2].reshape(nf, 3, rows), 1, 2),
            z(nf, rows, strip - 6),
            jnp.swapaxes(eyp[nt : nt + n2].reshape(nf, 3, rows), 1, 2),
        ],
        axis=2,
    )
    f2e = extend_xla(fields2d, f2x, f2y, None)

    ix = lax.axis_index("gx")
    iy = lax.axis_index("gy")
    nx, ny = lax.axis_size("gx"), lax.axis_size("gy")
    r = jnp.arange(rext, dtype=jnp.int32)[:, None]
    cc = jnp.arange(cext, dtype=jnp.int32)[None, :]
    row_ok = (r < rows) | ((r < rows + 4) & (ix < nx - 1)) | ((r >= rext - 4) & (ix > 0))
    col_ok = (cc < cols) | ((cc < cols + 4) & (iy < ny - 1)) | ((cc >= cext - 4) & (iy > 0))
    mask = (row_ok & col_ok).astype(jnp.float32)
    bp8 = bin_profile[:, :kc].reshape(-1)

    zero1 = jnp.zeros((1,), jnp.float32)
    lower = jnp.concatenate([zero1, -sound_coef[:-1]])
    upper = jnp.concatenate([-sound_coef[1:], zero1])
    middle = 1.0 + 2.0 * sound_coef

    def lvl(which):
        if which == 0:
            return lambda p, b: (jnp.where(p == 0, b, nblk - 1), 0, 0)
        return lambda p, b: (jnp.where(p == 2, b, 0), 0, 0)

    const3 = lambda p, b: (0, 0, 0)
    const2 = lambda p, b: (0, 0)
    smem = pl.BlockSpec(memory_space=pltpu.SMEM)
    in_specs = [
        smem, smem, smem, smem,
        pl.BlockSpec((lz, rows, cols), lvl(0)),
        pl.BlockSpec((lz, halo_rows, cols), lvl(0)),
        pl.BlockSpec((lz, rext, strip), lvl(0)),
        pl.BlockSpec((lz, rows, cols), lvl(2)),
        pl.BlockSpec((lz, halo_rows, cols), lvl(2)),
        pl.BlockSpec((lz, rext, strip), lvl(2)),
        pl.BlockSpec((None, lz, rows, cols), lambda p, b: (0, jnp.where(p == 2, b, 0), 0, 0)),
        pl.BlockSpec((None, lz, rows, cols), lambda p, b: (1, jnp.where(p == 2, b, 0), 0, 0)),
        pl.BlockSpec((lz, halo_rows, cols), lvl(2)),
        pl.BlockSpec((lz, rows, strip), lvl(2)),
        pl.BlockSpec((kc, rows, cols), const3),
        pl.BlockSpec((kc, halo_rows, cols), const3),
        pl.BlockSpec((kc, rows, strip), const3),
        pl.BlockSpec((nf, rext, cext), const3),
        pl.BlockSpec((rows, cols), const2),
        pl.BlockSpec((rows, cols), const2),
        pl.BlockSpec((rext, cext), const2),
    ]
    out_specs = [
        pl.BlockSpec((lz, rows, cols), lvl(2)),
        pl.BlockSpec((lz, rows, cols), lvl(2)),
        pl.BlockSpec((rows, cols), const2),
        pl.BlockSpec((rows, cols), const2),
    ]
    out_shape = [
        jax.ShapeDtypeStruct((levels, rows, cols), jnp.float32),
        jax.ShapeDtypeStruct((levels, rows, cols), jnp.float32),
        jax.ShapeDtypeStruct((rows, cols), jnp.float32),
        jax.ShapeDtypeStruct((rows, cols), jnp.float32),
    ]
    scratch = [
        pltpu.VMEM((levels, rext, cext), jnp.float32),
        pltpu.VMEM((levels, rext, cext), jnp.float32),
        pltpu.VMEM((rext, cext), jnp.float32),
        pltpu.VMEM((rext, cext), jnp.float32),
        pltpu.VMEM((1, cext), jnp.float32),
        pltpu.VMEM((levels, 1, cext), jnp.float32),
        pltpu.VMEM((levels, 1, cext), jnp.float32),
    ]
    call = pl.pallas_call(
        kernel,
        grid=(3, nblk),
        in_specs=in_specs,
        out_specs=out_specs,
        out_shape=out_shape,
        scratch_shapes=scratch,
        compiler_params=pltpu.CompilerParams(
            dimension_semantics=("arbitrary", "arbitrary"),
            vmem_limit_bytes=56 * 1024 * 1024,
        ),
    )
    tg, pg, fg, wg = call(
        lower, middle, upper, bp8,
        press_bar, pbx, pby, theta_bar, tbx, tby, winds, winds, u0x, u1y,
        theta, thx, thy, f2e, drag, wall_temp, mask,
    )
    return tg, pg, fg, wg


def extend_xla(main, rows, cols, corner):
    levels = main.shape[0]
    if corner is None:
        corner = jnp.zeros((levels, rows.shape[1], cols.shape[2]), main.dtype)
    return jnp.concatenate(
        [jnp.concatenate([main, rows], axis=1), jnp.concatenate([cols, corner], axis=1)], axis=2
    )


def solution(mesh):
    in_specs = (
        P(None, "gx", "gy"),
        P(None, None, "gx", "gy"),
        P(None, "gx", "gy"),
        P(None, "gx", "gy"),
        P("gx", "gy"),
        P("gx", "gy"),
        P("gx", "gy"),
        P("gx", "gy"),
        P("gx", "gy"),
        P(),
        P(),
        P(),
    )
    out_specs = (P(None, "gx", "gy"), P(None, "gx", "gy"), P("gx", "gy"), P("gx", "gy"))
    return jax.shard_map(
        per_device, mesh=mesh, in_specs=in_specs, out_specs=out_specs, check_vma=False
    )
```

```python
import functools

import jax
import jax.numpy as jnp
from jax import lax
from jax.experimental import pallas as pl
from jax.experimental.pallas import tpu as pltpu
from jax.sharding import PartitionSpec as P

courant = 0.3
diffusion = 0.1
buoyancy = 0.5
canopy_levels = 8
halo_rows = 8
strip = 128
block_levels = 12


def from_side(x, axis, delta):
    n = lax.axis_size(axis)
    if delta > 0:
        pairs = [(i + delta, i) for i in range(n - delta)]
    else:
        pairs = [(i, i - delta) for i in range(n + delta)]
    return lax.ppermute(x, axis, pairs)


def from_corner(x, dx, dy):
    nx, ny = lax.axis_size("gx"), lax.axis_size("gy")
    pairs = []
    for ix in range(nx):
        for iy in range(ny):
            sx, sy = ix + dx, iy + dy
            if 0 <= sx < nx and 0 <= sy < ny:
                pairs.append((sx * ny + sy, ix * ny + iy))
    return lax.ppermute(x, ("gx", "gy"), pairs)


def row_halo(f, lo, hi):
    levels, rows, cols = f.shape
    parts = []
    if hi:
        parts.append(from_side(f[:, :hi, :], "gx", 1))
    parts.append(jnp.zeros((levels, halo_rows - hi - lo, cols), f.dtype))
    if lo:
        parts.append(from_side(f[:, rows - lo :, :], "gx", -1))
    return jnp.concatenate(parts, axis=1)


def col_halo(f, lo, hi):
    levels, rows, cols = f.shape
    parts = []
    if hi:
        parts.append(from_side(f[:, :, :hi], "gy", 1))
    parts.append(jnp.zeros((levels, rows, strip - hi - lo), f.dtype))
    if lo:
        parts.append(from_side(f[:, :, cols - lo :], "gy", -1))
    return jnp.concatenate(parts, axis=2)


def corner_rows(f, w):
    levels, rows, cols = f.shape
    mid = jnp.zeros((levels, w, strip - 2 * w), f.dtype)
    gap = jnp.zeros((levels, halo_rows - 2 * w, strip), f.dtype)
    top = jnp.concatenate(
        [from_corner(f[:, :w, :w], 1, 1), mid, from_corner(f[:, :w, cols - w :], 1, -1)], axis=2
    )
    bottom = jnp.concatenate(
        [from_corner(f[:, rows - w :, :w], -1, 1), mid, from_corner(f[:, rows - w :, cols - w :], -1, -1)],
        axis=2,
    )
    return jnp.concatenate([top, gap, bottom], axis=1)


def ahead(x, k, axis):
    if k == 0:
        return x
    n = x.shape[axis]
    return pltpu.roll(x, (-k) % n, axis)


def forward_tend(f, u, axis):
    fm2, fm1, f0, f1, f2, f3 = [ahead(f, k, axis) for k in (-2, -1, 0, 1, 2, 3)]
    a_sum = (fm2 + f3) - 8.0 * (fm1 + f2) + 37.0 * (f0 + f1)
    b_sum = (fm2 - f3) - 5.0 * (fm1 - f2) + 10.0 * (f0 - f1)
    flux = (u * a_sum + jnp.abs(u) * b_sum) * (1.0 / 60.0)
    return -courant * (flux - ahead(flux, -1, axis))


def adjoint_tend(f, u, axis):
    g = courant * (ahead(f, 1, axis) - f)
    pu = u * g
    qu = jnp.abs(u) * g
    total = (
        ahead(pu + qu, 2, axis)
        + ahead(-8.0 * pu - 5.0 * qu, 1, axis)
        + (37.0 * pu + 10.0 * qu)
        + ahead(37.0 * pu - 10.0 * qu, -1, axis)
        + ahead(-8.0 * pu + 5.0 * qu, -2, axis)
        + ahead(pu - qu, -3, axis)
    )
    return total * (1.0 / 60.0)


def laplace(q):
    return ahead(q, 1, 0) + ahead(q, -1, 0) + ahead(q, 1, 1) + ahead(q, -1, 1) - 4.0 * q


def extend(main, rows, cols):
    return jnp.concatenate([jnp.concatenate([main, rows], axis=0), cols], axis=1)


def pack_kernel(pbf, pbl, tbf, tbl, u0f, u0l, pcf, pcl, tcf, tcl, ucf, ucl,
                xf, xl, yf, yl, cpp, cpm, cmp_, cmm):
    lz = pbf.shape[0]
    rows = pcf.shape[1]
    lane = lax.broadcasted_iota(jnp.int32, (rows, strip), 1)

    def body(j, c):
        xf[j] = jnp.concatenate([pbf[j][0:4], tbf[j][0:4], u0f[j][0:4]], axis=0)
        xl[j] = jnp.concatenate([pbl[j][4:8], tbl[j][4:8], u0l[j][4:8]], axis=0)
        a, b, u = pcf[j], tcf[j], ucf[j]
        first = jnp.where(lane < 4, a, jnp.where(lane < 8, pltpu.roll(b, 4, 1), pltpu.roll(u, 8, 1)))
        yf[j] = first[:, :12]
        a, b, u = pcl[j], tcl[j], ucl[j]
        last = jnp.where(
            lane < 4, pltpu.roll(a, 4, 1), jnp.where(lane < 8, pltpu.roll(b, 8, 1), pltpu.roll(u, 12, 1))
        )
        yl[j] = last[:, :12]
        top_first, top_last = pcf[j][0:4], pcl[j][0:4]
        bot_first, bot_last = pcf[j][rows - 4 : rows], pcl[j][rows - 4 : rows]
        cpp[j] = top_first[:, 0:4]
        cpm[j] = top_last[:, strip - 4 : strip]
        cmp_[j] = bot_first[:, 0:4]
        cmm[j] = bot_last[:, strip - 4 : strip]
        return c

    lax.fori_loop(0, lz, body, 0)


def lane_strip(near, far, width):
    rows = near.shape[0]
    a = jnp.concatenate([near, jnp.zeros((rows, strip - width), jnp.float32)], axis=1)
    b = jnp.concatenate([far, jnp.zeros((rows, strip - width), jnp.float32)], axis=1)
    return a + pltpu.roll(b, strip - width, 1)


def kernel(
    lo_ref, mid_ref, up_ref, bp_ref, cd_ref,
    pbm, tbm, u0m, u1m, xn, xp, yn, yp, cpp, cpm, cmp_, cmm,
    thm, x8n, x8p, y8n, y8p, f4, wall, mask,
    tg_out, pg_out, fg_out, wg_out,
    dd, qa, car_a, car_b, cpc, cp1, cq2,
):
    phase = pl.program_id(0)
    blk = pl.program_id(1)
    nblk = pl.num_programs(1)
    lz = pbm.shape[0]
    rows, cols = pbm.shape[1], pbm.shape[2]
    wide = cpc.shape[1]
    lane = lax.broadcasted_iota(jnp.int32, (rows, strip), 1)

    def coef(ref, k):
        return jnp.full((1, wide), ref[k], jnp.float32)

    def ystrip(j, which):
        n = jnp.concatenate([yn[j], jnp.zeros((rows, strip - 12), jnp.float32)], axis=1)
        p = jnp.concatenate([yp[j], jnp.zeros((rows, strip - 12), jnp.float32)], axis=1)
        n = pltpu.roll(n, (strip - 4 * which) % strip, 1)
        p = pltpu.roll(p, strip - 4 - 4 * which, 1)
        return jnp.where(lane < 4, n, jnp.where(lane >= strip - 4, p, 0.0))

    def press_ext(j):
        xr = jnp.concatenate([pbm[j], xn[j][0:4], xp[j][0:4]], axis=0)
        top = lane_strip(cpp[j], cpm[j], 4)[0:4]
        bot = lane_strip(cmp_[j], cmm[j], 4)[0:4]
        ys = jnp.concatenate([ystrip(j, 0), top, bot], axis=0)
        return jnp.concatenate([xr, ys], axis=1)

    @pl.when(phase == 0)
    def _():
        @pl.when(blk == 0)
        def _():
            car_a[...] = jnp.zeros(car_a.shape, jnp.float32)
            cpc[...] = jnp.zeros(cpc.shape, jnp.float32)

        def body(j, c):
            k = blk * lz + j
            ak = coef(lo_ref, k)
            r = 1.0 / (coef(mid_ref, k) - ak * cpc[...])
            cp = coef(up_ref, k) * r
            cpc[...] = cp
            cp1[k] = cp
            d = press_ext(j)
            dn = (d - ak * car_a[...]) * r
            car_a[...] = dn
            dd[k] = dn
            return c

        lax.fori_loop(0, lz, body, 0)

    @pl.when(phase == 1)
    def _():
        @pl.when(blk == 0)
        def _():
            car_a[...] = jnp.zeros(car_a.shape, jnp.float32)
            car_b[...] = jnp.zeros(car_b.shape, jnp.float32)
            cpc[...] = jnp.zeros(cpc.shape, jnp.float32)

        def body(j, c):
            k = (nblk - 1 - blk) * lz + (lz - 1 - j)
            x = dd[k] - cp1[k] * car_a[...]
            car_a[...] = x
            qa[k] = x
            pb1 = (x + diffusion * laplace(x)) * mask[...]
            ck = coef(up_ref, k)
            s = 1.0 / (coef(mid_ref, k) - ck * cpc[...])
            cq = coef(lo_ref, k) * s
            cpc[...] = cq
            cq2[k] = cq
            e = (pb1 - ck * car_b[...]) * s
            car_b[...] = e
            dd[k] = e
            return c

        lax.fori_loop(0, lz, body, 0)

    @pl.when(phase == 2)
    def _():
        @pl.when(blk == 0)
        def _():
            car_a[...] = jnp.zeros(car_a.shape, jnp.float32)

        def field_ext(i):
            xr = jnp.concatenate(
                [f4[i], x8n[8 + i], jnp.zeros((2, cols), jnp.float32), x8p[8 + i]], axis=0
            )
            ys = jnp.concatenate(
                [lane_strip(y8n[8 + i], y8p[8 + i], 3), jnp.zeros((halo_rows, strip), jnp.float32)], axis=0
            )
            return jnp.concatenate([xr, ys], axis=1)

        def level(j, canopy, acc):
            k = blk * lz + j
            qb = dd[k] - cq2[k] * car_a[...]
            car_a[...] = qb
            pg = qb + diffusion * laplace(qb)
            pg_out[j] = pg[:rows, :cols]
            tbx = jnp.concatenate([tbm[j], xn[j][4:8], xp[j][4:8]], axis=0)
            tby = jnp.concatenate([ystrip(j, 1), jnp.zeros((halo_rows, strip), jnp.float32)], axis=0)
            th2b = jnp.concatenate([tbx, tby], axis=1) + buoyancy * (qa[k] + qb)
            if canopy:
                ud, cls, hb, lay = acc[2]
                prof = jnp.zeros(hb.shape, jnp.float32)
                for bb in range(bp_ref.shape[0] // canopy_levels):
                    prof = jnp.where(hb == float(bb), bp_ref[bb * canopy_levels + j], prof)
                act = jnp.where(lay > j.astype(jnp.float32), 1.0, 0.0)
                am = ud * prof * act
                th1b = (1.0 - am) * th2b
            else:
                th1b = th2b
            u0e = jnp.concatenate([u0m[j], xn[j][8:12], xp[j][8:12]], axis=0)
            u1e = jnp.concatenate([u1m[j], ystrip(j, 2)], axis=1)
            adv = adjoint_tend(th1b[:, :cols], u0e, 0)[:rows, :] + adjoint_tend(th1b[:rows, :], u1e, 1)[:, :cols]
            tg_out[j] = th1b[:rows, :cols] + adv
            if canopy:
                th = thm[j]
                thx = jnp.concatenate([th, x8n[j], jnp.zeros((2, cols), jnp.float32), x8p[j]], axis=0)
                thy = jnp.concatenate([th, lane_strip(y8n[j], y8p[j], 3)], axis=1)
                fx = forward_tend(thx, u0e, 0)[:rows, :]
                fy = forward_tend(thy, u1e, 1)[:, :cols]
                first = th + (fx + fy)
                sb = th2b[:rows, :cols]
                fg, wg, fields, drag = acc
                dpa = drag * prof[:rows, :cols] * act[:rows, :cols]
                fg = fg + dpa * (wall[...] - first) * sb
                wg = wg + am[:rows, :cols] * sb
                acc = (fg, wg, fields, drag)
            return acc

        @pl.when(blk == 0)
        def _():
            zero = jnp.zeros((rows, cols), jnp.float32)
            cls = field_ext(1)
            drag = jnp.zeros(cls.shape, jnp.float32)
            for c in range(cd_ref.shape[0]):
                drag = jnp.where(cls == float(c), cd_ref[c], drag)
            ud = field_ext(0) * drag
            fields = (ud, cls, field_ext(2), field_ext(3))
            fg, wg, _, _ = lax.fori_loop(
                0, canopy_levels, lambda j, a: level(j, True, a), (zero, zero, fields, drag[:rows, :cols])
            )
            fg_out[...] = fg
            wg_out[...] = wg
            lax.fori_loop(canopy_levels, lz, lambda j, a: level(j, False, a), 0)

        @pl.when(blk > 0)
        def _():
            lax.fori_loop(0, lz, lambda j, a: level(j, False, a), 0)


def per_device(
    theta, winds, theta_bar, press_bar, urban_frac, wall_temp, urban_class, canopy_layers,
    height_bin, class_drag, bin_profile, sound_coef,
):
    levels, rows, cols = theta.shape
    rext, cext = rows + halo_rows, cols + strip
    lz = block_levels
    nblk = levels // lz
    kc = canopy_levels
    rb, cb = rows // 8 - 1, cols // strip - 1

    lvl = lambda b: (b, 0, 0)
    pack = pl.pallas_call(
        pack_kernel,
        grid=(nblk,),
        in_specs=[
            pl.BlockSpec((lz, 8, cols), lvl),
            pl.BlockSpec((lz, 8, cols), lambda b: (b, rb, 0)),
            pl.BlockSpec((lz, 8, cols), lvl),
            pl.BlockSpec((lz, 8, cols), lambda b: (b, rb, 0)),
            pl.BlockSpec((None, lz, 8, cols), lambda b: (0, b, 0, 0)),
            pl.BlockSpec((None, lz, 8, cols), lambda b: (0, b, rb, 0)),
            pl.BlockSpec((lz, rows, strip), lvl),
            pl.BlockSpec((lz, rows, strip), lambda b: (b, 0, cb)),
            pl.BlockSpec((lz, rows, strip), lvl),
            pl.BlockSpec((lz, rows, strip), lambda b: (b, 0, cb)),
            pl.BlockSpec((None, lz, rows, strip), lambda b: (1, b, 0, 0)),
            pl.BlockSpec((None, lz, rows, strip), lambda b: (1, b, 0, cb)),
        ],
        out_specs=[pl.BlockSpec((lz, 12, cols), lvl)] * 2
        + [pl.BlockSpec((lz, rows, 12), lvl)] * 2
        + [pl.BlockSpec((lz, 4, 4), lvl)] * 4,
        out_shape=[jax.ShapeDtypeStruct((levels, 12, cols), jnp.float32)] * 2
        + [jax.ShapeDtypeStruct((levels, rows, 12), jnp.float32)] * 2
        + [jax.ShapeDtypeStruct((levels, 4, 4), jnp.float32)] * 4,
        compiler_params=pltpu.CompilerParams(dimension_semantics=("arbitrary",)),
    )
    xf, xl, yf, yl, cpp, cpm, cmp_, cmm = pack(
        press_bar, press_bar, theta_bar, theta_bar, winds, winds,
        press_bar, press_bar, theta_bar, theta_bar, winds, winds,
    )
    xn = from_side(xf, "gx", 1)
    xp = from_side(xl, "gx", -1)
    yn = from_side(yf, "gy", 1)
    yp = from_side(yl, "gy", -1)
    cpp = from_corner(cpp, 1, 1)
    cpm = from_corner(cpm, 1, -1)
    cmp_ = from_corner(cmp_, -1, 1)
    cmm = from_corner(cmm, -1, -1)

    f4 = jnp.stack(
        [urban_frac, urban_class.astype(jnp.float32), height_bin.astype(jnp.float32), canopy_layers.astype(jnp.float32)]
    )
    small = jnp.concatenate([theta[:kc], f4], axis=0)
    x8n = from_side(small[:, :3, :], "gx", 1)
    x8p = from_side(small[:, rows - 3 :, :], "gx", -1)
    y8n = from_side(small[:, :, :3], "gy", 1)
    y8p = from_side(small[:, :, cols - 3 :], "gy", -1)

    ix = lax.axis_index("gx")
    iy = lax.axis_index("gy")
    nx, ny = lax.axis_size("gx"), lax.axis_size("gy")
    r = jnp.arange(rext, dtype=jnp.int32)[:, None]
    cc = jnp.arange(cext, dtype=jnp.int32)[None, :]
    row_ok = (r < rows) | ((r < rows + 4) & (ix < nx - 1)) | ((r >= rext - 4) & (ix > 0))
    col_ok = (cc < cols) | ((cc < cols + 4) & (iy < ny - 1)) | ((cc >= cext - 4) & (iy > 0))
    mask = (row_ok & col_ok).astype(jnp.float32)
    bp8 = bin_profile[:, :kc].reshape(-1)

    zero1 = jnp.zeros((1,), jnp.float32)
    lower = jnp.concatenate([zero1, -sound_coef[:-1]])
    upper = jnp.concatenate([-sound_coef[1:], zero1])
    middle = 1.0 + 2.0 * sound_coef

    ph0 = lambda p, b: (jnp.where(p == 0, b, nblk - 1), 0, 0)
    ph2 = lambda p, b: (jnp.where(p == 2, b, 0), 0, 0)
    ph02 = lambda p, b: (jnp.where(p == 1, nblk - 1, b), 0, 0)
    const3 = lambda p, b: (0, 0, 0)
    const2 = lambda p, b: (0, 0)
    smem = pl.BlockSpec(memory_space=pltpu.SMEM)
    n_small = small.shape[0]
    in_specs = [
        smem, smem, smem, smem, smem,
        pl.BlockSpec((lz, rows, cols), ph0),
        pl.BlockSpec((lz, rows, cols), ph2),
        pl.BlockSpec((None, lz, rows, cols), lambda p, b: (0, jnp.where(p == 2, b, 0), 0, 0)),
        pl.BlockSpec((None, lz, rows, cols), lambda p, b: (1, jnp.where(p == 2, b, 0), 0, 0)),
        pl.BlockSpec((lz, 12, cols), ph02),
        pl.BlockSpec((lz, 12, cols), ph02),
        pl.BlockSpec((lz, rows, 12), ph02),
        pl.BlockSpec((lz, rows, 12), ph02),
        pl.BlockSpec((lz, 4, 4), ph0),
        pl.BlockSpec((lz, 4, 4), ph0),
        pl.BlockSpec((lz, 4, 4), ph0),
        pl.BlockSpec((lz, 4, 4), ph0),
        pl.BlockSpec((kc, rows, cols), const3),
        pl.BlockSpec((n_small, 3, cols), const3),
        pl.BlockSpec((n_small, 3, cols), const3),
        pl.BlockSpec((n_small, rows, 3), const3),
        pl.BlockSpec((n_small, rows, 3), const3),
        pl.BlockSpec((4, rows, cols), const3),
        pl.BlockSpec((rows, cols), const2),
        pl.BlockSpec((rext, cext), const2),
    ]
    out_specs = [
        pl.BlockSpec((lz, rows, cols), ph2),
        pl.BlockSpec((lz, rows, cols), ph2),
        pl.BlockSpec((rows, cols), const2),
        pl.BlockSpec((rows, cols), const2),
    ]
    out_shape = [
        jax.ShapeDtypeStruct((levels, rows, cols), jnp.float32),
        jax.ShapeDtypeStruct((levels, rows, cols), jnp.float32),
        jax.ShapeDtypeStruct((rows, cols), jnp.float32),
        jax.ShapeDtypeStruct((rows, cols), jnp.float32),
    ]
    scratch = [
        pltpu.VMEM((levels, rext, cext), jnp.float32),
        pltpu.VMEM((levels, rext, cext), jnp.float32),
        pltpu.VMEM((rext, cext), jnp.float32),
        pltpu.VMEM((rext, cext), jnp.float32),
        pltpu.VMEM((1, cext), jnp.float32),
        pltpu.VMEM((levels, 1, cext), jnp.float32),
        pltpu.VMEM((levels, 1, cext), jnp.float32),
    ]
    call = pl.pallas_call(
        kernel,
        grid=(3, nblk),
        in_specs=in_specs,
        out_specs=out_specs,
        out_shape=out_shape,
        scratch_shapes=scratch,
        compiler_params=pltpu.CompilerParams(
            dimension_semantics=("arbitrary", "arbitrary"),
            vmem_limit_bytes=56 * 1024 * 1024,
        ),
    )
    tg, pg, fg, wg = call(
        lower, middle, upper, bp8, class_drag,
        press_bar, theta_bar, winds, winds, xn, xp, yn, yp, cpp, cpm, cmp_, cmm,
        theta, x8n, x8p, y8n, y8p, f4, wall_temp, mask,
    )
    return tg, pg, fg, wg


def extend_xla(main, rows, cols, corner):
    levels = main.shape[0]
    if corner is None:
        corner = jnp.zeros((levels, rows.shape[1], cols.shape[2]), main.dtype)
    return jnp.concatenate(
        [jnp.concatenate([main, rows], axis=1), jnp.concatenate([cols, corner], axis=1)], axis=2
    )


def solution(mesh):
    in_specs = (
        P(None, "gx", "gy"),
        P(None, None, "gx", "gy"),
        P(None, "gx", "gy"),
        P(None, "gx", "gy"),
        P("gx", "gy"),
        P("gx", "gy"),
        P("gx", "gy"),
        P("gx", "gy"),
        P("gx", "gy"),
        P(),
        P(),
        P(),
    )
    out_specs = (P(None, "gx", "gy"), P(None, "gx", "gy"), P("gx", "gy"), P("gx", "gy"))
    return jax.shard_map(
        per_device, mesh=mesh, in_specs=in_specs, out_specs=out_specs, check_vma=False
    )
```

```python
import functools

import jax
import jax.numpy as jnp
from jax import lax
from jax.experimental import pallas as pl
from jax.experimental.pallas import tpu as pltpu
from jax.sharding import PartitionSpec as P

courant = 0.3
diffusion = 0.1
buoyancy = 0.5
canopy_levels = 8
halo_rows = 8
strip = 128
block_levels = 12


def from_side(x, axis, delta):
    n = lax.axis_size(axis)
    if delta > 0:
        pairs = [(i + delta, i) for i in range(n - delta)]
    else:
        pairs = [(i, i - delta) for i in range(n + delta)]
    return lax.ppermute(x, axis, pairs)


def from_corner(x, dx, dy):
    nx, ny = lax.axis_size("gx"), lax.axis_size("gy")
    pairs = []
    for ix in range(nx):
        for iy in range(ny):
            sx, sy = ix + dx, iy + dy
            if 0 <= sx < nx and 0 <= sy < ny:
                pairs.append((sx * ny + sy, ix * ny + iy))
    return lax.ppermute(x, ("gx", "gy"), pairs)


def row_halo(f, lo, hi):
    levels, rows, cols = f.shape
    parts = []
    if hi:
        parts.append(from_side(f[:, :hi, :], "gx", 1))
    parts.append(jnp.zeros((levels, halo_rows - hi - lo, cols), f.dtype))
    if lo:
        parts.append(from_side(f[:, rows - lo :, :], "gx", -1))
    return jnp.concatenate(parts, axis=1)


def col_halo(f, lo, hi):
    levels, rows, cols = f.shape
    parts = []
    if hi:
        parts.append(from_side(f[:, :, :hi], "gy", 1))
    parts.append(jnp.zeros((levels, rows, strip - hi - lo), f.dtype))
    if lo:
        parts.append(from_side(f[:, :, cols - lo :], "gy", -1))
    return jnp.concatenate(parts, axis=2)


def corner_rows(f, w):
    levels, rows, cols = f.shape
    mid = jnp.zeros((levels, w, strip - 2 * w), f.dtype)
    gap = jnp.zeros((levels, halo_rows - 2 * w, strip), f.dtype)
    top = jnp.concatenate(
        [from_corner(f[:, :w, :w], 1, 1), mid, from_corner(f[:, :w, cols - w :], 1, -1)], axis=2
    )
    bottom = jnp.concatenate(
        [from_corner(f[:, rows - w :, :w], -1, 1), mid, from_corner(f[:, rows - w :, cols - w :], -1, -1)],
        axis=2,
    )
    return jnp.concatenate([top, gap, bottom], axis=1)


def ahead(x, k, axis):
    if k == 0:
        return x
    n = x.shape[axis]
    return pltpu.roll(x, (-k) % n, axis)


def forward_tend(f, u, axis):
    fm2, fm1, f0, f1, f2, f3 = [ahead(f, k, axis) for k in (-2, -1, 0, 1, 2, 3)]
    a_sum = (fm2 + f3) - 8.0 * (fm1 + f2) + 37.0 * (f0 + f1)
    b_sum = (fm2 - f3) - 5.0 * (fm1 - f2) + 10.0 * (f0 - f1)
    flux = (u * a_sum + jnp.abs(u) * b_sum) * (1.0 / 60.0)
    return -courant * (flux - ahead(flux, -1, axis))


def adjoint_tend(f, u, axis):
    g = courant * (ahead(f, 1, axis) - f)
    pu = u * g
    qu = jnp.abs(u) * g
    total = (
        ahead(pu + qu, 2, axis)
        + ahead(-8.0 * pu - 5.0 * qu, 1, axis)
        + (37.0 * pu + 10.0 * qu)
        + ahead(37.0 * pu - 10.0 * qu, -1, axis)
        + ahead(-8.0 * pu + 5.0 * qu, -2, axis)
        + ahead(pu - qu, -3, axis)
    )
    return total * (1.0 / 60.0)


def laplace(q):
    return ahead(q, 1, 0) + ahead(q, -1, 0) + ahead(q, 1, 1) + ahead(q, -1, 1) - 4.0 * q


def extend(main, rows, cols):
    return jnp.concatenate([jnp.concatenate([main, rows], axis=0), cols], axis=1)


def pack_kernel(pbf, pbl, tbf, tbl, u0f, u0l, pcf, pcl, tcf, tcl, ucf, ucl,
                xfp, xft, xlp, xlt, yfp, yft, ylp, ylt, cpp, cpm, cmp_, cmm):
    lz = pbf.shape[0]
    rows = pcf.shape[1]
    lane = lax.broadcasted_iota(jnp.int32, (rows, strip), 1)

    def body(j, c):
        xfp[j] = pbf[j][0:4]
        xft[j] = jnp.concatenate([tbf[j][0:4], u0f[j][0:4]], axis=0)
        xlp[j] = pbl[j][4:8]
        xlt[j] = jnp.concatenate([tbl[j][4:8], u0l[j][4:8]], axis=0)
        a, b, u = pcf[j], tcf[j], ucf[j]
        yfp[j] = a[:, 0:4]
        yft[j] = jnp.where(lane < 4, b, pltpu.roll(u, 4, 1))[:, :8]
        a, b, u = pcl[j], tcl[j], ucl[j]
        ylp[j] = pltpu.roll(a, 4, 1)[:, :4]
        ylt[j] = jnp.where(lane < 4, pltpu.roll(b, 4, 1), pltpu.roll(u, 8, 1))[:, :8]
        top_first, top_last = pcf[j][0:4], pcl[j][0:4]
        bot_first, bot_last = pcf[j][rows - 4 : rows], pcl[j][rows - 4 : rows]
        cpp[j] = top_first[:, 0:4]
        cpm[j] = top_last[:, strip - 4 : strip]
        cmp_[j] = bot_first[:, 0:4]
        cmm[j] = bot_last[:, strip - 4 : strip]
        return c

    lax.fori_loop(0, lz, body, 0)


def lane_strip(near, far, width):
    rows = near.shape[0]
    a = jnp.concatenate([near, jnp.zeros((rows, strip - width), jnp.float32)], axis=1)
    b = jnp.concatenate([far, jnp.zeros((rows, strip - width), jnp.float32)], axis=1)
    return a + pltpu.roll(b, strip - width, 1)


def kernel_a(
    lo_ref, mid_ref, up_ref,
    pbm, xn, xp, yn, yp, cpp, cpm, cmp_, cmm, mask,
    e_out, qa_out, cq_out,
    dd, car_a, car_b, cpc, cp1,
):
    phase = pl.program_id(0)
    blk = pl.program_id(1)
    nblk = pl.num_programs(1)
    lz = pbm.shape[0]
    wide = cpc.shape[1]

    def coef(ref, k):
        return jnp.full((1, wide), ref[k], jnp.float32)

    def press_ext(j):
        xr = jnp.concatenate([pbm[j], xn[j], xp[j]], axis=0)
        top = lane_strip(cpp[j], cpm[j], 4)
        bot = lane_strip(cmp_[j], cmm[j], 4)
        ys = jnp.concatenate([lane_strip(yn[j], yp[j], 4), top, bot], axis=0)
        return jnp.concatenate([xr, ys], axis=1)

    @pl.when(phase == 0)
    def _():
        @pl.when(blk == 0)
        def _():
            car_a[...] = jnp.zeros(car_a.shape, jnp.float32)
            cpc[...] = jnp.zeros(cpc.shape, jnp.float32)

        def body(j, c):
            k = blk * lz + j
            ak = coef(lo_ref, k)
            r = 1.0 / (coef(mid_ref, k) - ak * cpc[...])
            cp = coef(up_ref, k) * r
            cpc[...] = cp
            cp1[k] = cp
            dn = (press_ext(j) - ak * car_a[...]) * r
            car_a[...] = dn
            dd[k] = dn
            return c

        lax.fori_loop(0, lz, body, 0)

    @pl.when(phase == 1)
    def _():
        @pl.when(blk == 0)
        def _():
            car_a[...] = jnp.zeros(car_a.shape, jnp.float32)
            car_b[...] = jnp.zeros(car_b.shape, jnp.float32)
            cpc[...] = jnp.zeros(cpc.shape, jnp.float32)

        def body(j, c):
            jj = lz - 1 - j
            k = (nblk - 1 - blk) * lz + jj
            x = dd[k] - cp1[k] * car_a[...]
            car_a[...] = x
            qa_out[jj] = x
            pb1 = (x + diffusion * laplace(x)) * mask[...]
            ck = coef(up_ref, k)
            s = 1.0 / (coef(mid_ref, k) - ck * cpc[...])
            cq = coef(lo_ref, k) * s
            cpc[...] = cq
            cq_out[jj] = cq
            e = (pb1 - ck * car_b[...]) * s
            car_b[...] = e
            e_out[jj] = e
            return c

        lax.fori_loop(0, lz, body, 0)


def kernel_b(
    bp_ref, cd_ref,
    ee, qa, cq2, tbm, u0m, u1m, xn, xp, yn, yp,
    thm, x8n, x8p, y8n, y8p, f4, wall,
    tg_out, pg_out, fg_out, wg_out,
    car_a,
):
    blk = pl.program_id(0)
    lz = tbm.shape[0]
    rows, cols = tbm.shape[1], tbm.shape[2]

    @pl.when(blk == 0)
    def _():
        car_a[...] = jnp.zeros(car_a.shape, jnp.float32)

    def field_ext(i):
        xr = jnp.concatenate([f4[i], x8n[8 + i], jnp.zeros((2, cols), jnp.float32), x8p[8 + i]], axis=0)
        ys = jnp.concatenate(
            [lane_strip(y8n[8 + i], y8p[8 + i], 3), jnp.zeros((halo_rows, strip), jnp.float32)], axis=0
        )
        return jnp.concatenate([xr, ys], axis=1)

    def level(j, canopy, acc):
        qb = ee[j] - cq2[j] * car_a[...]
        car_a[...] = qb
        pg = qb + diffusion * laplace(qb)
        pg_out[j] = pg[:rows, :cols]
        xnj, xpj, ynj, ypj = xn[j], xp[j], yn[j], yp[j]
        tbx = jnp.concatenate([tbm[j], xnj[0:4], xpj[0:4]], axis=0)
        tby = jnp.concatenate(
            [lane_strip(ynj[:, 0:4], ypj[:, 0:4], 4), jnp.zeros((halo_rows, strip), jnp.float32)], axis=0
        )
        th2b = jnp.concatenate([tbx, tby], axis=1) + buoyancy * (qa[j] + qb)
        if canopy:
            ud, cls, hb, lay = acc[2]
            prof = jnp.zeros(hb.shape, jnp.float32)
            for bb in range(bp_ref.shape[0] // canopy_levels):
                prof = jnp.where(hb == float(bb), bp_ref[bb * canopy_levels + j], prof)
            act = jnp.where(lay > j.astype(jnp.float32), 1.0, 0.0)
            am = ud * prof * act
            th1b = (1.0 - am) * th2b
        else:
            th1b = th2b
        u0e = jnp.concatenate([u0m[j], xnj[4:8], xpj[4:8]], axis=0)
        u1e = jnp.concatenate([u1m[j], lane_strip(ynj[:, 4:8], ypj[:, 4:8], 4)], axis=1)
        adv = adjoint_tend(th1b[:, :cols], u0e, 0)[:rows, :] + adjoint_tend(th1b[:rows, :], u1e, 1)[:, :cols]
        tg_out[j] = th1b[:rows, :cols] + adv
        if canopy:
            th = thm[j]
            thx = jnp.concatenate([th, x8n[j], jnp.zeros((2, cols), jnp.float32), x8p[j]], axis=0)
            thy = jnp.concatenate([th, lane_strip(y8n[j], y8p[j], 3)], axis=1)
            fx = forward_tend(thx, u0e, 0)[:rows, :]
            fy = forward_tend(thy, u1e, 1)[:, :cols]
            first = th + (fx + fy)
            sb = th2b[:rows, :cols]
            fg, wg, fields, drag = acc
            dpa = drag * prof[:rows, :cols] * act[:rows, :cols]
            fg = fg + dpa * (wall[...] - first) * sb
            wg = wg + am[:rows, :cols] * sb
            acc = (fg, wg, fields, drag)
        return acc

    @pl.when(blk == 0)
    def _():
        zero = jnp.zeros((rows, cols), jnp.float32)
        cls = field_ext(1)
        drag = jnp.zeros(cls.shape, jnp.float32)
        for c in range(cd_ref.shape[0]):
            drag = jnp.where(cls == float(c), cd_ref[c], drag)
        ud = field_ext(0) * drag
        fields = (ud, cls, field_ext(2), field_ext(3))
        fg, wg, _, _ = lax.fori_loop(
            0, canopy_levels, lambda j, a: level(j, True, a), (zero, zero, fields, drag[:rows, :cols])
        )
        fg_out[...] = fg
        wg_out[...] = wg
        lax.fori_loop(canopy_levels, lz, lambda j, a: level(j, False, a), 0)

    @pl.when(blk > 0)
    def _():
        lax.fori_loop(0, lz, lambda j, a: level(j, False, a), 0)


def per_device(
    theta, winds, theta_bar, press_bar, urban_frac, wall_temp, urban_class, canopy_layers,
    height_bin, class_drag, bin_profile, sound_coef,
):
    levels, rows, cols = theta.shape
    rext, cext = rows + halo_rows, cols + strip
    lz = block_levels
    nblk = levels // lz
    kc = canopy_levels
    rb, cb = rows // 8 - 1, cols // strip - 1
    f32 = jnp.float32

    lvl = lambda b: (b, 0, 0)
    pack = pl.pallas_call(
        pack_kernel,
        grid=(nblk,),
        in_specs=[
            pl.BlockSpec((lz, 8, cols), lvl),
            pl.BlockSpec((lz, 8, cols), lambda b: (b, rb, 0)),
            pl.BlockSpec((lz, 8, cols), lvl),
            pl.BlockSpec((lz, 8, cols), lambda b: (b, rb, 0)),
            pl.BlockSpec((None, lz, 8, cols), lambda b: (0, b, 0, 0)),
            pl.BlockSpec((None, lz, 8, cols), lambda b: (0, b, rb, 0)),
            pl.BlockSpec((lz, rows, strip), lvl),
            pl.BlockSpec((lz, rows, strip), lambda b: (b, 0, cb)),
            pl.BlockSpec((lz, rows, strip), lvl),
            pl.BlockSpec((lz, rows, strip), lambda b: (b, 0, cb)),
            pl.BlockSpec((None, lz, rows, strip), lambda b: (1, b, 0, 0)),
            pl.BlockSpec((None, lz, rows, strip), lambda b: (1, b, 0, cb)),
        ],
        out_specs=[pl.BlockSpec((lz, 4, cols), lvl), pl.BlockSpec((lz, 8, cols), lvl)] * 2
        + [pl.BlockSpec((lz, rows, 4), lvl), pl.BlockSpec((lz, rows, 8), lvl)] * 2
        + [pl.BlockSpec((lz, 4, 4), lvl)] * 4,
        out_shape=[jax.ShapeDtypeStruct((levels, 4, cols), f32), jax.ShapeDtypeStruct((levels, 8, cols), f32)] * 2
        + [jax.ShapeDtypeStruct((levels, rows, 4), f32), jax.ShapeDtypeStruct((levels, rows, 8), f32)] * 2
        + [jax.ShapeDtypeStruct((levels, 4, 4), f32)] * 4,
        compiler_params=pltpu.CompilerParams(dimension_semantics=("arbitrary",)),
    )
    xfp, xft, xlp, xlt, yfp, yft, ylp, ylt, cpp, cpm, cmp_, cmm = pack(
        press_bar, press_bar, theta_bar, theta_bar, winds, winds,
        press_bar, press_bar, theta_bar, theta_bar, winds, winds,
    )
    xnp, xpp = from_side(xfp, "gx", 1), from_side(xlp, "gx", -1)
    ynp, ypp = from_side(yfp, "gy", 1), from_side(ylp, "gy", -1)
    cpp = from_corner(cpp, 1, 1)
    cpm = from_corner(cpm, 1, -1)
    cmp_ = from_corner(cmp_, -1, 1)
    cmm = from_corner(cmm, -1, -1)

    ix = lax.axis_index("gx")
    iy = lax.axis_index("gy")
    nx, ny = lax.axis_size("gx"), lax.axis_size("gy")
    r = jnp.arange(rext, dtype=jnp.int32)[:, None]
    cc = jnp.arange(cext, dtype=jnp.int32)[None, :]
    row_ok = (r < rows) | ((r < rows + 4) & (ix < nx - 1)) | ((r >= rext - 4) & (ix > 0))
    col_ok = (cc < cols) | ((cc < cols + 4) & (iy < ny - 1)) | ((cc >= cext - 4) & (iy > 0))
    mask = (row_ok & col_ok).astype(f32)

    zero1 = jnp.zeros((1,), f32)
    lower = jnp.concatenate([zero1, -sound_coef[:-1]])
    upper = jnp.concatenate([-sound_coef[1:], zero1])
    middle = 1.0 + 2.0 * sound_coef

    ph0 = lambda p, b: (jnp.where(p == 0, b, nblk - 1), 0, 0)
    ph1 = lambda p, b: (jnp.where(p == 1, nblk - 1 - b, nblk - 1), 0, 0)
    smem = pl.BlockSpec(memory_space=pltpu.SMEM)
    call_a = pl.pallas_call(
        kernel_a,
        grid=(2, nblk),
        in_specs=[
            smem, smem, smem,
            pl.BlockSpec((lz, rows, cols), ph0),
            pl.BlockSpec((lz, 4, cols), ph0),
            pl.BlockSpec((lz, 4, cols), ph0),
            pl.BlockSpec((lz, rows, 4), ph0),
            pl.BlockSpec((lz, rows, 4), ph0),
        ]
        + [pl.BlockSpec((lz, 4, 4), ph0)] * 4
        + [pl.BlockSpec((rext, cext), lambda p, b: (0, 0))],
        out_specs=[
            pl.BlockSpec((lz, rext, cext), ph1),
            pl.BlockSpec((lz, rext, cext), ph1),
            pl.BlockSpec((lz, 1, cext), ph1),
        ],
        out_shape=[
            jax.ShapeDtypeStruct((levels, rext, cext), f32),
            jax.ShapeDtypeStruct((levels, rext, cext), f32),
            jax.ShapeDtypeStruct((levels, 1, cext), f32),
        ],
        scratch_shapes=[
            pltpu.VMEM((levels, rext, cext), f32),
            pltpu.VMEM((rext, cext), f32),
            pltpu.VMEM((rext, cext), f32),
            pltpu.VMEM((1, cext), f32),
            pltpu.VMEM((levels, 1, cext), f32),
        ],
        compiler_params=pltpu.CompilerParams(
            dimension_semantics=("arbitrary", "arbitrary"),
            vmem_limit_bytes=48 * 1024 * 1024,
        ),
    )
    ee, qa, cq2 = call_a(lower, middle, upper, press_bar, xnp, xpp, ynp, ypp, cpp, cpm, cmp_, cmm, mask)

    xnt, xpt = from_side(xft, "gx", 1), from_side(xlt, "gx", -1)
    ynt, ypt = from_side(yft, "gy", 1), from_side(ylt, "gy", -1)
    f4 = jnp.stack(
        [urban_frac, urban_class.astype(f32), height_bin.astype(f32), canopy_layers.astype(f32)]
    )
    small = jnp.concatenate([theta[:kc], f4], axis=0)
    x8n = from_side(small[:, :3, :], "gx", 1)
    x8p = from_side(small[:, rows - 3 :, :], "gx", -1)
    y8n = from_side(small[:, :, :3], "gy", 1)
    y8p = from_side(small[:, :, cols - 3 :], "gy", -1)
    bp8 = bin_profile[:, :kc].reshape(-1)

    blk3 = lambda b: (b, 0, 0)
    const3 = lambda b: (0, 0, 0)
    const2 = lambda b: (0, 0)
    n_small = small.shape[0]
    call_b = pl.pallas_call(
        kernel_b,
        grid=(nblk,),
        in_specs=[
            smem, smem,
            pl.BlockSpec((lz, rext, cext), blk3),
            pl.BlockSpec((lz, rext, cext), blk3),
            pl.BlockSpec((lz, 1, cext), blk3),
            pl.BlockSpec((lz, rows, cols), blk3),
            pl.BlockSpec((None, lz, rows, cols), lambda b: (0, b, 0, 0)),
            pl.BlockSpec((None, lz, rows, cols), lambda b: (1, b, 0, 0)),
            pl.BlockSpec((lz, 8, cols), blk3),
            pl.BlockSpec((lz, 8, cols), blk3),
            pl.BlockSpec((lz, rows, 8), blk3),
            pl.BlockSpec((lz, rows, 8), blk3),
            pl.BlockSpec((kc, rows, cols), const3),
            pl.BlockSpec((n_small, 3, cols), const3),
            pl.BlockSpec((n_small, 3, cols), const3),
            pl.BlockSpec((n_small, rows, 3), const3),
            pl.BlockSpec((n_small, rows, 3), const3),
            pl.BlockSpec((4, rows, cols), const3),
            pl.BlockSpec((rows, cols), const2),
        ],
        out_specs=[
            pl.BlockSpec((lz, rows, cols), blk3),
            pl.BlockSpec((lz, rows, cols), blk3),
            pl.BlockSpec((rows, cols), const2),
            pl.BlockSpec((rows, cols), const2),
        ],
        out_shape=[
            jax.ShapeDtypeStruct((levels, rows, cols), f32),
            jax.ShapeDtypeStruct((levels, rows, cols), f32),
            jax.ShapeDtypeStruct((rows, cols), f32),
            jax.ShapeDtypeStruct((rows, cols), f32),
        ],
        scratch_shapes=[pltpu.VMEM((rext, cext), f32)],
        compiler_params=pltpu.CompilerParams(
            dimension_semantics=("arbitrary",),
            vmem_limit_bytes=48 * 1024 * 1024,
        ),
    )
    tg, pg, fg, wg = call_b(
        bp8, class_drag, ee, qa, cq2, theta_bar, winds, winds, xnt, xpt, ynt, ypt,
        theta, x8n, x8p, y8n, y8p, f4, wall_temp,
    )
    return tg, pg, fg, wg


def extend_xla(main, rows, cols, corner):
    levels = main.shape[0]
    if corner is None:
        corner = jnp.zeros((levels, rows.shape[1], cols.shape[2]), main.dtype)
    return jnp.concatenate(
        [jnp.concatenate([main, rows], axis=1), jnp.concatenate([cols, corner], axis=1)], axis=2
    )


def solution(mesh):
    in_specs = (
        P(None, "gx", "gy"),
        P(None, None, "gx", "gy"),
        P(None, "gx", "gy"),
        P(None, "gx", "gy"),
        P("gx", "gy"),
        P("gx", "gy"),
        P("gx", "gy"),
        P("gx", "gy"),
        P("gx", "gy"),
        P(),
        P(),
        P(),
    )
    out_specs = (P(None, "gx", "gy"), P(None, "gx", "gy"), P("gx", "gy"), P("gx", "gy"))
    return jax.shard_map(
        per_device, mesh=mesh, in_specs=in_specs, out_specs=out_specs, check_vma=False
    )
```

```python
import functools

import jax
import jax.numpy as jnp
from jax import lax
from jax.experimental import pallas as pl
from jax.experimental.pallas import tpu as pltpu
from jax.sharding import PartitionSpec as P

courant = 0.3
diffusion = 0.1
buoyancy = 0.5
canopy_levels = 8
halo_rows = 8
strip = 128
block_levels = 12


def from_side(x, axis, delta):
    n = lax.axis_size(axis)
    if delta > 0:
        pairs = [(i + delta, i) for i in range(n - delta)]
    else:
        pairs = [(i, i - delta) for i in range(n + delta)]
    return lax.ppermute(x, axis, pairs)


def from_corner(x, dx, dy):
    nx, ny = lax.axis_size("gx"), lax.axis_size("gy")
    pairs = []
    for ix in range(nx):
        for iy in range(ny):
            sx, sy = ix + dx, iy + dy
            if 0 <= sx < nx and 0 <= sy < ny:
                pairs.append((sx * ny + sy, ix * ny + iy))
    return lax.ppermute(x, ("gx", "gy"), pairs)


def row_halo(f, lo, hi):
    levels, rows, cols = f.shape
    parts = []
    if hi:
        parts.append(from_side(f[:, :hi, :], "gx", 1))
    parts.append(jnp.zeros((levels, halo_rows - hi - lo, cols), f.dtype))
    if lo:
        parts.append(from_side(f[:, rows - lo :, :], "gx", -1))
    return jnp.concatenate(parts, axis=1)


def col_halo(f, lo, hi):
    levels, rows, cols = f.shape
    parts = []
    if hi:
        parts.append(from_side(f[:, :, :hi], "gy", 1))
    parts.append(jnp.zeros((levels, rows, strip - hi - lo), f.dtype))
    if lo:
        parts.append(from_side(f[:, :, cols - lo :], "gy", -1))
    return jnp.concatenate(parts, axis=2)


def corner_rows(f, w):
    levels, rows, cols = f.shape
    mid = jnp.zeros((levels, w, strip - 2 * w), f.dtype)
    gap = jnp.zeros((levels, halo_rows - 2 * w, strip), f.dtype)
    top = jnp.concatenate(
        [from_corner(f[:, :w, :w], 1, 1), mid, from_corner(f[:, :w, cols - w :], 1, -1)], axis=2
    )
    bottom = jnp.concatenate(
        [from_corner(f[:, rows - w :, :w], -1, 1), mid, from_corner(f[:, rows - w :, cols - w :], -1, -1)],
        axis=2,
    )
    return jnp.concatenate([top, gap, bottom], axis=1)


def ahead(x, k, axis):
    if k == 0:
        return x
    n = x.shape[axis]
    return pltpu.roll(x, (-k) % n, axis)


def forward_tend(f, u, axis):
    fm2, fm1, f0, f1, f2, f3 = [ahead(f, k, axis) for k in (-2, -1, 0, 1, 2, 3)]
    a_sum = (fm2 + f3) - 8.0 * (fm1 + f2) + 37.0 * (f0 + f1)
    b_sum = (fm2 - f3) - 5.0 * (fm1 - f2) + 10.0 * (f0 - f1)
    flux = (u * a_sum + jnp.abs(u) * b_sum) * (1.0 / 60.0)
    return -courant * (flux - ahead(flux, -1, axis))


def adjoint_tend(f, u, axis):
    g = courant * (ahead(f, 1, axis) - f)
    pu = u * g
    qu = jnp.abs(u) * g
    total = (
        ahead(pu + qu, 2, axis)
        + ahead(-8.0 * pu - 5.0 * qu, 1, axis)
        + (37.0 * pu + 10.0 * qu)
        + ahead(37.0 * pu - 10.0 * qu, -1, axis)
        + ahead(-8.0 * pu + 5.0 * qu, -2, axis)
        + ahead(pu - qu, -3, axis)
    )
    return total * (1.0 / 60.0)


def laplace(q):
    return ahead(q, 1, 0) + ahead(q, -1, 0) + ahead(q, 1, 1) + ahead(q, -1, 1) - 4.0 * q


def extend(main, rows, cols):
    return jnp.concatenate([jnp.concatenate([main, rows], axis=0), cols], axis=1)


def pack_kernel(pbf, pbl, tbf, tbl, u0f, u0l, pcf, pcl, tcf, tcl, ucf, ucl,
                xf, xl, yf, yl, cpp, cpm, cmp_, cmm):
    lz = pbf.shape[0]
    rows = pcf.shape[1]
    lane = lax.broadcasted_iota(jnp.int32, (rows, strip), 1)

    def body(j, c):
        xf[j] = jnp.concatenate([pbf[j][0:4], tbf[j][0:3], u0f[j][0:2]], axis=0)
        xl[j] = jnp.concatenate([pbl[j][4:8], tbl[j][5:8], u0l[j][5:8]], axis=0)
        a, b, u = pcf[j], tcf[j], ucf[j]
        first = jnp.where(lane < 4, a, jnp.where(lane < 7, pltpu.roll(b, 4, 1), pltpu.roll(u, 7, 1)))
        yf[j] = first[:, :9]
        a, b, u = pcl[j], tcl[j], ucl[j]
        last = jnp.where(
            lane < 4, pltpu.roll(a, 4, 1), jnp.where(lane < 7, pltpu.roll(b, 7, 1), pltpu.roll(u, 10, 1))
        )
        yl[j] = last[:, :10]
        top_first, top_last = pcf[j][0:4], pcl[j][0:4]
        bot_first, bot_last = pcf[j][rows - 4 : rows], pcl[j][rows - 4 : rows]
        cpp[j] = top_first[:, 0:4]
        cpm[j] = top_last[:, strip - 4 : strip]
        cmp_[j] = bot_first[:, 0:4]
        cmm[j] = bot_last[:, strip - 4 : strip]
        return c

    lax.fori_loop(0, lz, body, 0)


def lane_strip(near, far, width):
    rows = near.shape[0]
    a = jnp.concatenate([near, jnp.zeros((rows, strip - width), jnp.float32)], axis=1)
    b = jnp.concatenate([far, jnp.zeros((rows, strip - width), jnp.float32)], axis=1)
    return a + pltpu.roll(b, strip - width, 1)


def kernel(
    lo_ref, mid_ref, up_ref, bp_ref, cd_ref,
    pbm, tbm, u0m, u1m, xn, xp, yn, yp, cpp, cpm, cmp_, cmm,
    thm, x8n, x8p, y8n, y8p, f4, wall, mask,
    tg_out, pg_out, fg_out, wg_out,
    dd, qa, car_a, car_b, cpc, cp1, cq2,
):
    phase = pl.program_id(0)
    blk = pl.program_id(1)
    nblk = pl.num_programs(1)
    lz = pbm.shape[0]
    rows, cols = pbm.shape[1], pbm.shape[2]
    wide = cpc.shape[1]
    lane = lax.broadcasted_iota(jnp.int32, (rows, strip), 1)

    def coef(ref, k):
        return jnp.full((1, wide), ref[k], jnp.float32)

    def ystrip(j, off, wn, wp):
        n = jnp.concatenate([yn[j], jnp.zeros((rows, strip - yn.shape[2]), jnp.float32)], axis=1)
        p = jnp.concatenate([yp[j], jnp.zeros((rows, strip - yp.shape[2]), jnp.float32)], axis=1)
        n = pltpu.roll(n, (strip - off) % strip, 1)
        p = pltpu.roll(p, strip - wp - off, 1)
        return jnp.where(lane < wn, n, jnp.where(lane >= strip - wp, p, 0.0))

    def press_ext(j):
        xr = jnp.concatenate([pbm[j], xn[j][0:4], xp[j][0:4]], axis=0)
        top = lane_strip(cpp[j], cpm[j], 4)[0:4]
        bot = lane_strip(cmp_[j], cmm[j], 4)[0:4]
        ys = jnp.concatenate([ystrip(j, 0, 4, 4), top, bot], axis=0)
        return jnp.concatenate([xr, ys], axis=1)

    @pl.when(phase == 0)
    def _():
        @pl.when(blk == 0)
        def _():
            car_a[...] = jnp.zeros(car_a.shape, jnp.float32)
            cpc[...] = jnp.zeros(cpc.shape, jnp.float32)

        def body(j, c):
            k = blk * lz + j
            ak = coef(lo_ref, k)
            r = 1.0 / (coef(mid_ref, k) - ak * cpc[...])
            cp = coef(up_ref, k) * r
            cpc[...] = cp
            cp1[k] = cp
            d = press_ext(j)
            dn = (d - ak * car_a[...]) * r
            car_a[...] = dn
            dd[k] = dn
            return c

        lax.fori_loop(0, lz, body, 0)

    @pl.when(phase == 1)
    def _():
        @pl.when(blk == 0)
        def _():
            car_a[...] = jnp.zeros(car_a.shape, jnp.float32)
            car_b[...] = jnp.zeros(car_b.shape, jnp.float32)
            cpc[...] = jnp.zeros(cpc.shape, jnp.float32)

        def body(j, c):
            k = (nblk - 1 - blk) * lz + (lz - 1 - j)
            x = dd[k] - cp1[k] * car_a[...]
            car_a[...] = x
            qa[k] = x
            pb1 = (x + diffusion * laplace(x)) * mask[...]
            ck = coef(up_ref, k)
            s = 1.0 / (coef(mid_ref, k) - ck * cpc[...])
            cq = coef(lo_ref, k) * s
            cpc[...] = cq
            cq2[k] = cq
            e = (pb1 - ck * car_b[...]) * s
            car_b[...] = e
            dd[k] = e
            return c

        lax.fori_loop(0, lz, body, 0)

    @pl.when(phase == 2)
    def _():
        @pl.when(blk == 0)
        def _():
            car_a[...] = jnp.zeros(car_a.shape, jnp.float32)

        def field_ext(i):
            xr = jnp.concatenate(
                [f4[i], x8n[8 + i], jnp.zeros((2, cols), jnp.float32), x8p[8 + i]], axis=0
            )
            ys = jnp.concatenate(
                [lane_strip(y8n[8 + i], y8p[8 + i], 3), jnp.zeros((halo_rows, strip), jnp.float32)], axis=0
            )
            return jnp.concatenate([xr, ys], axis=1)

        def level(j, canopy, acc):
            k = blk * lz + j
            qb = dd[k] - cq2[k] * car_a[...]
            car_a[...] = qb
            pg = qb + diffusion * laplace(qb)
            pg_out[j] = pg[:rows, :cols]
            xnj, xpj = xn[j], xp[j]
            tbx = jnp.concatenate([tbm[j], xnj[4:7], jnp.zeros((2, cols), jnp.float32), xpj[4:7]], axis=0)
            tby = jnp.concatenate([ystrip(j, 4, 3, 3), jnp.zeros((halo_rows, strip), jnp.float32)], axis=0)
            th2b = jnp.concatenate([tbx, tby], axis=1) + buoyancy * (qa[k] + qb)
            if canopy:
                ud, cls, hb, lay = acc[2]
                prof = jnp.zeros(hb.shape, jnp.float32)
                for bb in range(bp_ref.shape[0] // canopy_levels):
                    prof = jnp.where(hb == float(bb), bp_ref[bb * canopy_levels + j], prof)
                act = jnp.where(lay > j.astype(jnp.float32), 1.0, 0.0)
                am = ud * prof * act
                th1b = (1.0 - am) * th2b
            else:
                th1b = th2b
            u0e = jnp.concatenate([u0m[j], xnj[7:9], jnp.zeros((3, cols), jnp.float32), xpj[7:10]], axis=0)
            u1e = jnp.concatenate([u1m[j], ystrip(j, 7, 2, 3)], axis=1)
            adv = adjoint_tend(th1b[:, :cols], u0e, 0)[:rows, :] + adjoint_tend(th1b[:rows, :], u1e, 1)[:, :cols]
            tg_out[j] = th1b[:rows, :cols] + adv
            if canopy:
                th = thm[j]
                thx = jnp.concatenate([th, x8n[j], jnp.zeros((2, cols), jnp.float32), x8p[j]], axis=0)
                thy = jnp.concatenate([th, lane_strip(y8n[j], y8p[j], 3)], axis=1)
                fx = forward_tend(thx, u0e, 0)[:rows, :]
                fy = forward_tend(thy, u1e, 1)[:, :cols]
                first = th + (fx + fy)
                sb = th2b[:rows, :cols]
                fg, wg, fields, drag = acc
                dpa = drag * prof[:rows, :cols] * act[:rows, :cols]
                fg = fg + dpa * (wall[...] - first) * sb
                wg = wg + am[:rows, :cols] * sb
                acc = (fg, wg, fields, drag)
            return acc

        @pl.when(blk == 0)
        def _():
            zero = jnp.zeros((rows, cols), jnp.float32)
            cls = field_ext(1)
            drag = jnp.zeros(cls.shape, jnp.float32)
            for c in range(cd_ref.shape[0]):
                drag = jnp.where(cls == float(c), cd_ref[c], drag)
            ud = field_ext(0) * drag
            fields = (ud, cls, field_ext(2), field_ext(3))
            fg, wg, _, _ = lax.fori_loop(
                0, canopy_levels, lambda j, a: level(j, True, a), (zero, zero, fields, drag[:rows, :cols])
            )
            fg_out[...] = fg
            wg_out[...] = wg
            lax.fori_loop(canopy_levels, lz, lambda j, a: level(j, False, a), 0)

        @pl.when(blk > 0)
        def _():
            lax.fori_loop(0, lz, lambda j, a: level(j, False, a), 0)


def per_device(
    theta, winds, theta_bar, press_bar, urban_frac, wall_temp, urban_class, canopy_layers,
    height_bin, class_drag, bin_profile, sound_coef,
):
    levels, rows, cols = theta.shape
    rext, cext = rows + halo_rows, cols + strip
    lz = block_levels
    nblk = levels // lz
    kc = canopy_levels
    rb, cb = rows // 8 - 1, cols // strip - 1

    lvl = lambda b: (b, 0, 0)
    pack = pl.pallas_call(
        pack_kernel,
        grid=(nblk,),
        in_specs=[
            pl.BlockSpec((lz, 8, cols), lvl),
            pl.BlockSpec((lz, 8, cols), lambda b: (b, rb, 0)),
            pl.BlockSpec((lz, 8, cols), lvl),
            pl.BlockSpec((lz, 8, cols), lambda b: (b, rb, 0)),
            pl.BlockSpec((None, lz, 8, cols), lambda b: (0, b, 0, 0)),
            pl.BlockSpec((None, lz, 8, cols), lambda b: (0, b, rb, 0)),
            pl.BlockSpec((lz, rows, strip), lvl),
            pl.BlockSpec((lz, rows, strip), lambda b: (b, 0, cb)),
            pl.BlockSpec((lz, rows, strip), lvl),
            pl.BlockSpec((lz, rows, strip), lambda b: (b, 0, cb)),
            pl.BlockSpec((None, lz, rows, strip), lambda b: (1, b, 0, 0)),
            pl.BlockSpec((None, lz, rows, strip), lambda b: (1, b, 0, cb)),
        ],
        out_specs=[pl.BlockSpec((lz, 9, cols), lvl), pl.BlockSpec((lz, 10, cols), lvl)]
        + [pl.BlockSpec((lz, rows, 9), lvl), pl.BlockSpec((lz, rows, 10), lvl)]
        + [pl.BlockSpec((lz, 4, 4), lvl)] * 4,
        out_shape=[jax.ShapeDtypeStruct((levels, 9, cols), jnp.float32), jax.ShapeDtypeStruct((levels, 10, cols), jnp.float32)]
        + [jax.ShapeDtypeStruct((levels, rows, 9), jnp.float32), jax.ShapeDtypeStruct((levels, rows, 10), jnp.float32)]
        + [jax.ShapeDtypeStruct((levels, 4, 4), jnp.float32)] * 4,
        compiler_params=pltpu.CompilerParams(dimension_semantics=("arbitrary",)),
    )
    xf, xl, yf, yl, cpp, cpm, cmp_, cmm = pack(
        press_bar, press_bar, theta_bar, theta_bar, winds, winds,
        press_bar, press_bar, theta_bar, theta_bar, winds, winds,
    )
    xn = from_side(xf, "gx", 1)
    xp = from_side(xl, "gx", -1)
    yn = from_side(yf, "gy", 1)
    yp = from_side(yl, "gy", -1)
    cpp = from_corner(cpp, 1, 1)
    cpm = from_corner(cpm, 1, -1)
    cmp_ = from_corner(cmp_, -1, 1)
    cmm = from_corner(cmm, -1, -1)

    f4 = jnp.stack(
        [urban_frac, urban_class.astype(jnp.float32), height_bin.astype(jnp.float32), canopy_layers.astype(jnp.float32)]
    )
    small = jnp.concatenate([theta[:kc], f4], axis=0)
    x8n = from_side(small[:, :3, :], "gx", 1)
    x8p = from_side(small[:, rows - 3 :, :], "gx", -1)
    y8n = from_side(small[:, :, :3], "gy", 1)
    y8p = from_side(small[:, :, cols - 3 :], "gy", -1)

    ix = lax.axis_index("gx")
    iy = lax.axis_index("gy")
    nx, ny = lax.axis_size("gx"), lax.axis_size("gy")
    r = jnp.arange(rext, dtype=jnp.int32)[:, None]
    cc = jnp.arange(cext, dtype=jnp.int32)[None, :]
    row_ok = (r < rows) | ((r < rows + 4) & (ix < nx - 1)) | ((r >= rext - 4) & (ix > 0))
    col_ok = (cc < cols) | ((cc < cols + 4) & (iy < ny - 1)) | ((cc >= cext - 4) & (iy > 0))
    mask = (row_ok & col_ok).astype(jnp.float32)
    bp8 = bin_profile[:, :kc].reshape(-1)

    zero1 = jnp.zeros((1,), jnp.float32)
    lower = jnp.concatenate([zero1, -sound_coef[:-1]])
    upper = jnp.concatenate([-sound_coef[1:], zero1])
    middle = 1.0 + 2.0 * sound_coef

    ph0 = lambda p, b: (jnp.where(p == 0, b, nblk - 1), 0, 0)
    ph2 = lambda p, b: (jnp.where(p == 2, b, 0), 0, 0)
    ph02 = lambda p, b: (jnp.where(p == 1, nblk - 1, b), 0, 0)
    const3 = lambda p, b: (0, 0, 0)
    const2 = lambda p, b: (0, 0)
    smem = pl.BlockSpec(memory_space=pltpu.SMEM)
    n_small = small.shape[0]
    in_specs = [
        smem, smem, smem, smem, smem,
        pl.BlockSpec((lz, rows, cols), ph0),
        pl.BlockSpec((lz, rows, cols), ph2),
        pl.BlockSpec((None, lz, rows, cols), lambda p, b: (0, jnp.where(p == 2, b, 0), 0, 0)),
        pl.BlockSpec((None, lz, rows, cols), lambda p, b: (1, jnp.where(p == 2, b, 0), 0, 0)),
        pl.BlockSpec((lz, 9, cols), ph02),
        pl.BlockSpec((lz, 10, cols), ph02),
        pl.BlockSpec((lz, rows, 9), ph02),
        pl.BlockSpec((lz, rows, 10), ph02),
        pl.BlockSpec((lz, 4, 4), ph0),
        pl.BlockSpec((lz, 4, 4), ph0),
        pl.BlockSpec((lz, 4, 4), ph0),
        pl.BlockSpec((lz, 4, 4), ph0),
        pl.BlockSpec((kc, rows, cols), const3),
        pl.BlockSpec((n_small, 3, cols), const3),
        pl.BlockSpec((n_small, 3, cols), const3),
        pl.BlockSpec((n_small, rows, 3), const3),
        pl.BlockSpec((n_small, rows, 3), const3),
        pl.BlockSpec((4, rows, cols), const3),
        pl.BlockSpec((rows, cols), const2),
        pl.BlockSpec((rext, cext), const2),
    ]
    out_specs = [
        pl.BlockSpec((lz, rows, cols), ph2),
        pl.BlockSpec((lz, rows, cols), ph2),
        pl.BlockSpec((rows, cols), const2),
        pl.BlockSpec((rows, cols), const2),
    ]
    out_shape = [
        jax.ShapeDtypeStruct((levels, rows, cols), jnp.float32),
        jax.ShapeDtypeStruct((levels, rows, cols), jnp.float32),
        jax.ShapeDtypeStruct((rows, cols), jnp.float32),
        jax.ShapeDtypeStruct((rows, cols), jnp.float32),
    ]
    scratch = [
        pltpu.VMEM((levels, rext, cext), jnp.float32),
        pltpu.VMEM((levels, rext, cext), jnp.float32),
        pltpu.VMEM((rext, cext), jnp.float32),
        pltpu.VMEM((rext, cext), jnp.float32),
        pltpu.VMEM((1, cext), jnp.float32),
        pltpu.VMEM((levels, 1, cext), jnp.float32),
        pltpu.VMEM((levels, 1, cext), jnp.float32),
    ]
    call = pl.pallas_call(
        kernel,
        grid=(3, nblk),
        in_specs=in_specs,
        out_specs=out_specs,
        out_shape=out_shape,
        scratch_shapes=scratch,
        compiler_params=pltpu.CompilerParams(
            dimension_semantics=("arbitrary", "arbitrary"),
            vmem_limit_bytes=56 * 1024 * 1024,
        ),
    )
    tg, pg, fg, wg = call(
        lower, middle, upper, bp8, class_drag,
        press_bar, theta_bar, winds, winds, xn, xp, yn, yp, cpp, cpm, cmp_, cmm,
        theta, x8n, x8p, y8n, y8p, f4, wall_temp, mask,
    )
    return tg, pg, fg, wg


def extend_xla(main, rows, cols, corner):
    levels = main.shape[0]
    if corner is None:
        corner = jnp.zeros((levels, rows.shape[1], cols.shape[2]), main.dtype)
    return jnp.concatenate(
        [jnp.concatenate([main, rows], axis=1), jnp.concatenate([cols, corner], axis=1)], axis=2
    )


def solution(mesh):
    in_specs = (
        P(None, "gx", "gy"),
        P(None, None, "gx", "gy"),
        P(None, "gx", "gy"),
        P(None, "gx", "gy"),
        P("gx", "gy"),
        P("gx", "gy"),
        P("gx", "gy"),
        P("gx", "gy"),
        P("gx", "gy"),
        P(),
        P(),
        P(),
    )
    out_specs = (P(None, "gx", "gy"), P(None, "gx", "gy"), P("gx", "gy"), P("gx", "gy"))
    return jax.shard_map(
        per_device, mesh=mesh, in_specs=in_specs, out_specs=out_specs, check_vma=False
    )
```

```python
import functools

import jax
import jax.numpy as jnp
from jax import lax
from jax.experimental import pallas as pl
from jax.experimental.pallas import tpu as pltpu
from jax.sharding import PartitionSpec as P

courant = 0.3
diffusion = 0.1
buoyancy = 0.5
canopy_levels = 8
halo_rows = 8
strip = 128
block_levels = 12


def from_side(x, axis, delta):
    n = lax.axis_size(axis)
    if delta > 0:
        pairs = [(i + delta, i) for i in range(n - delta)]
    else:
        pairs = [(i, i - delta) for i in range(n + delta)]
    return lax.ppermute(x, axis, pairs)


def from_corner(x, dx, dy):
    nx, ny = lax.axis_size("gx"), lax.axis_size("gy")
    pairs = []
    for ix in range(nx):
        for iy in range(ny):
            sx, sy = ix + dx, iy + dy
            if 0 <= sx < nx and 0 <= sy < ny:
                pairs.append((sx * ny + sy, ix * ny + iy))
    return lax.ppermute(x, ("gx", "gy"), pairs)


def row_halo(f, lo, hi):
    levels, rows, cols = f.shape
    parts = []
    if hi:
        parts.append(from_side(f[:, :hi, :], "gx", 1))
    parts.append(jnp.zeros((levels, halo_rows - hi - lo, cols), f.dtype))
    if lo:
        parts.append(from_side(f[:, rows - lo :, :], "gx", -1))
    return jnp.concatenate(parts, axis=1)


def col_halo(f, lo, hi):
    levels, rows, cols = f.shape
    parts = []
    if hi:
        parts.append(from_side(f[:, :, :hi], "gy", 1))
    parts.append(jnp.zeros((levels, rows, strip - hi - lo), f.dtype))
    if lo:
        parts.append(from_side(f[:, :, cols - lo :], "gy", -1))
    return jnp.concatenate(parts, axis=2)


def corner_rows(f, w):
    levels, rows, cols = f.shape
    mid = jnp.zeros((levels, w, strip - 2 * w), f.dtype)
    gap = jnp.zeros((levels, halo_rows - 2 * w, strip), f.dtype)
    top = jnp.concatenate(
        [from_corner(f[:, :w, :w], 1, 1), mid, from_corner(f[:, :w, cols - w :], 1, -1)], axis=2
    )
    bottom = jnp.concatenate(
        [from_corner(f[:, rows - w :, :w], -1, 1), mid, from_corner(f[:, rows - w :, cols - w :], -1, -1)],
        axis=2,
    )
    return jnp.concatenate([top, gap, bottom], axis=1)


def ahead(x, k, axis):
    if k == 0:
        return x
    n = x.shape[axis]
    return pltpu.roll(x, (-k) % n, axis)


def forward_tend(f, u, axis):
    fm2, fm1, f0, f1, f2, f3 = [ahead(f, k, axis) for k in (-2, -1, 0, 1, 2, 3)]
    a_sum = (fm2 + f3) - 8.0 * (fm1 + f2) + 37.0 * (f0 + f1)
    b_sum = (fm2 - f3) - 5.0 * (fm1 - f2) + 10.0 * (f0 - f1)
    flux = (u * a_sum + jnp.abs(u) * b_sum) * (1.0 / 60.0)
    return -courant * (flux - ahead(flux, -1, axis))


def adjoint_tend(f, u, axis):
    g = courant * (ahead(f, 1, axis) - f)
    pu = u * g
    qu = jnp.abs(u) * g
    total = (
        ahead(pu + qu, 2, axis)
        + ahead(-8.0 * pu - 5.0 * qu, 1, axis)
        + (37.0 * pu + 10.0 * qu)
        + ahead(37.0 * pu - 10.0 * qu, -1, axis)
        + ahead(-8.0 * pu + 5.0 * qu, -2, axis)
        + ahead(pu - qu, -3, axis)
    )
    return total * (1.0 / 60.0)


def laplace(q):
    return ahead(q, 1, 0) + ahead(q, -1, 0) + ahead(q, 1, 1) + ahead(q, -1, 1) - 4.0 * q


def extend(main, rows, cols):
    return jnp.concatenate([jnp.concatenate([main, rows], axis=0), cols], axis=1)


def pack_kernel(pbf, pbl, tbf, tbl, u0f, u0l, pcf, pcl, tcf, tcl, ucf, ucl,
                xf, xl, yf, yl, cpp, cpm, cmp_, cmm):
    lz = pbf.shape[0]
    rows = pcf.shape[1]
    lane = lax.broadcasted_iota(jnp.int32, (rows, strip), 1)

    def body(j, c):
        k = pl.program_id(0) * lz + j
        xf[:, k, :] = jnp.concatenate([pbf[j][0:4], tbf[j][0:3], u0f[j][0:2]], axis=0)
        xl[:, k, :] = jnp.concatenate([pbl[j][4:8], tbl[j][5:8], u0l[j][5:8]], axis=0)
        a, b, u = pcf[j], tcf[j], ucf[j]
        first = jnp.where(lane < 4, a, jnp.where(lane < 7, pltpu.roll(b, 4, 1), pltpu.roll(u, 7, 1)))
        yf[j] = first[:, :9]
        a, b, u = pcl[j], tcl[j], ucl[j]
        last = jnp.where(
            lane < 4, pltpu.roll(a, 4, 1), jnp.where(lane < 7, pltpu.roll(b, 7, 1), pltpu.roll(u, 10, 1))
        )
        yl[j] = last[:, :10]
        top_first, top_last = pcf[j][0:4], pcl[j][0:4]
        bot_first, bot_last = pcf[j][rows - 4 : rows], pcl[j][rows - 4 : rows]
        cpp[j] = top_first[:, 0:4]
        cpm[j] = top_last[:, strip - 4 : strip]
        cmp_[j] = bot_first[:, 0:4]
        cmm[j] = bot_last[:, strip - 4 : strip]
        return c

    lax.fori_loop(0, lz, body, 0)


def lane_strip(near, far, width):
    rows = near.shape[0]
    a = jnp.concatenate([near, jnp.zeros((rows, strip - width), jnp.float32)], axis=1)
    b = jnp.concatenate([far, jnp.zeros((rows, strip - width), jnp.float32)], axis=1)
    return a + pltpu.roll(b, strip - width, 1)


def kernel(
    lo_ref, mid_ref, up_ref, bp_ref, cd_ref,
    pbm, tbm, u0m, u1m, xn, xp, yn, yp, cpp, cpm, cmp_, cmm,
    thm, x8n, x8p, y8n, y8p, f4, wall, mask,
    tg_out, pg_out, fg_out, wg_out,
    dd, qa, car_a, car_b, cpc, cp1, cq2,
):
    phase = pl.program_id(0)
    blk = pl.program_id(1)
    nblk = pl.num_programs(1)
    lz = pbm.shape[0]
    rows, cols = pbm.shape[1], pbm.shape[2]
    wide = cpc.shape[1]
    lane = lax.broadcasted_iota(jnp.int32, (rows, strip), 1)

    def coef(ref, k):
        return jnp.full((1, wide), ref[k], jnp.float32)

    def ystrip(j, off, wn, wp):
        n = jnp.concatenate([yn[j], jnp.zeros((rows, strip - yn.shape[2]), jnp.float32)], axis=1)
        p = jnp.concatenate([yp[j], jnp.zeros((rows, strip - yp.shape[2]), jnp.float32)], axis=1)
        n = pltpu.roll(n, (strip - off) % strip, 1)
        p = pltpu.roll(p, strip - wp - off, 1)
        return jnp.where(lane < wn, n, jnp.where(lane >= strip - wp, p, 0.0))

    def press_ext(j, k):
        xr = jnp.concatenate([pbm[j], xn[:, k, :][0:4], xp[:, k, :][0:4]], axis=0)
        top = lane_strip(cpp[j], cpm[j], 4)[0:4]
        bot = lane_strip(cmp_[j], cmm[j], 4)[0:4]
        ys = jnp.concatenate([ystrip(j, 0, 4, 4), top, bot], axis=0)
        return jnp.concatenate([xr, ys], axis=1)

    @pl.when(phase == 0)
    def _():
        @pl.when(blk == 0)
        def _():
            car_a[...] = jnp.zeros(car_a.shape, jnp.float32)
            cpc[...] = jnp.zeros(cpc.shape, jnp.float32)

        def body(j, c):
            k = blk * lz + j
            ak = coef(lo_ref, k)
            r = 1.0 / (coef(mid_ref, k) - ak * cpc[...])
            cp = coef(up_ref, k) * r
            cpc[...] = cp
            cp1[k] = cp
            d = press_ext(j, k)
            dn = (d - ak * car_a[...]) * r
            car_a[...] = dn
            dd[k] = dn
            return c

        lax.fori_loop(0, lz, body, 0)

    @pl.when(phase == 1)
    def _():
        @pl.when(blk == 0)
        def _():
            car_a[...] = jnp.zeros(car_a.shape, jnp.float32)
            car_b[...] = jnp.zeros(car_b.shape, jnp.float32)
            cpc[...] = jnp.zeros(cpc.shape, jnp.float32)

        def body(j, c):
            k = (nblk - 1 - blk) * lz + (lz - 1 - j)
            x = dd[k] - cp1[k] * car_a[...]
            car_a[...] = x
            qa[k] = x
            pb1 = (x + diffusion * laplace(x)) * mask[...]
            ck = coef(up_ref, k)
            s = 1.0 / (coef(mid_ref, k) - ck * cpc[...])
            cq = coef(lo_ref, k) * s
            cpc[...] = cq
            cq2[k] = cq
            e = (pb1 - ck * car_b[...]) * s
            car_b[...] = e
            dd[k] = e
            return c

        lax.fori_loop(0, lz, body, 0)

    @pl.when(phase == 2)
    def _():
        @pl.when(blk == 0)
        def _():
            car_a[...] = jnp.zeros(car_a.shape, jnp.float32)

        def field_ext(i):
            xr = jnp.concatenate(
                [f4[i], x8n[8 + i], jnp.zeros((2, cols), jnp.float32), x8p[8 + i]], axis=0
            )
            ys = jnp.concatenate(
                [lane_strip(y8n[8 + i], y8p[8 + i], 3), jnp.zeros((halo_rows, strip), jnp.float32)], axis=0
            )
            return jnp.concatenate([xr, ys], axis=1)

        def level(j, canopy, acc):
            k = blk * lz + j
            qb = dd[k] - cq2[k] * car_a[...]
            car_a[...] = qb
            pg = qb + diffusion * laplace(qb)
            pg_out[j] = pg[:rows, :cols]
            xnj, xpj = xn[:, k, :], xp[:, k, :]
            tbx = jnp.concatenate([tbm[j], xnj[4:7], jnp.zeros((2, cols), jnp.float32), xpj[4:7]], axis=0)
            tby = jnp.concatenate([ystrip(j, 4, 3, 3), jnp.zeros((halo_rows, strip), jnp.float32)], axis=0)
            th2b = jnp.concatenate([tbx, tby], axis=1) + buoyancy * (qa[k] + qb)
            if canopy:
                ud, cls, hb, lay = acc[2]
                prof = jnp.zeros(hb.shape, jnp.float32)
                for bb in range(bp_ref.shape[0] // canopy_levels):
                    prof = jnp.where(hb == float(bb), bp_ref[bb * canopy_levels + j], prof)
                act = jnp.where(lay > j.astype(jnp.float32), 1.0, 0.0)
                am = ud * prof * act
                th1b = (1.0 - am) * th2b
            else:
                th1b = th2b
            u0e = jnp.concatenate([u0m[j], xnj[7:9], jnp.zeros((3, cols), jnp.float32), xpj[7:10]], axis=0)
            u1e = jnp.concatenate([u1m[j], ystrip(j, 7, 2, 3)], axis=1)
            adv = adjoint_tend(th1b[:, :cols], u0e, 0)[:rows, :] + adjoint_tend(th1b[:rows, :], u1e, 1)[:, :cols]
            tg_out[j] = th1b[:rows, :cols] + adv
            if canopy:
                th = thm[j]
                thx = jnp.concatenate([th, x8n[j], jnp.zeros((2, cols), jnp.float32), x8p[j]], axis=0)
                thy = jnp.concatenate([th, lane_strip(y8n[j], y8p[j], 3)], axis=1)
                fx = forward_tend(thx, u0e, 0)[:rows, :]
                fy = forward_tend(thy, u1e, 1)[:, :cols]
                first = th + (fx + fy)
                sb = th2b[:rows, :cols]
                fg, wg, fields, drag = acc
                dpa = drag * prof[:rows, :cols] * act[:rows, :cols]
                fg = fg + dpa * (wall[...] - first) * sb
                wg = wg + am[:rows, :cols] * sb
                acc = (fg, wg, fields, drag)
            return acc

        @pl.when(blk == 0)
        def _():
            zero = jnp.zeros((rows, cols), jnp.float32)
            cls = field_ext(1)
            drag = jnp.zeros(cls.shape, jnp.float32)
            for c in range(cd_ref.shape[0]):
                drag = jnp.where(cls == float(c), cd_ref[c], drag)
            ud = field_ext(0) * drag
            fields = (ud, cls, field_ext(2), field_ext(3))
            fg, wg, _, _ = lax.fori_loop(
                0, canopy_levels, lambda j, a: level(j, True, a), (zero, zero, fields, drag[:rows, :cols])
            )
            fg_out[...] = fg
            wg_out[...] = wg
            lax.fori_loop(canopy_levels, lz, lambda j, a: level(j, False, a), 0)

        @pl.when(blk > 0)
        def _():
            lax.fori_loop(0, lz, lambda j, a: level(j, False, a), 0)


def per_device(
    theta, winds, theta_bar, press_bar, urban_frac, wall_temp, urban_class, canopy_layers,
    height_bin, class_drag, bin_profile, sound_coef,
):
    levels, rows, cols = theta.shape
    rext, cext = rows + halo_rows, cols + strip
    lz = block_levels
    nblk = levels // lz
    kc = canopy_levels
    rb, cb = rows // 8 - 1, cols // strip - 1

    lvl = lambda b: (b, 0, 0)
    pack = pl.pallas_call(
        pack_kernel,
        grid=(nblk,),
        in_specs=[
            pl.BlockSpec((lz, 8, cols), lvl),
            pl.BlockSpec((lz, 8, cols), lambda b: (b, rb, 0)),
            pl.BlockSpec((lz, 8, cols), lvl),
            pl.BlockSpec((lz, 8, cols), lambda b: (b, rb, 0)),
            pl.BlockSpec((None, lz, 8, cols), lambda b: (0, b, 0, 0)),
            pl.BlockSpec((None, lz, 8, cols), lambda b: (0, b, rb, 0)),
            pl.BlockSpec((lz, rows, strip), lvl),
            pl.BlockSpec((lz, rows, strip), lambda b: (b, 0, cb)),
            pl.BlockSpec((lz, rows, strip), lvl),
            pl.BlockSpec((lz, rows, strip), lambda b: (b, 0, cb)),
            pl.BlockSpec((None, lz, rows, strip), lambda b: (1, b, 0, 0)),
            pl.BlockSpec((None, lz, rows, strip), lambda b: (1, b, 0, cb)),
        ],
        out_specs=[pl.BlockSpec((9, levels, cols), lambda b: (0, 0, 0)), pl.BlockSpec((10, levels, cols), lambda b: (0, 0, 0))]
        + [pl.BlockSpec((lz, rows, 9), lvl), pl.BlockSpec((lz, rows, 10), lvl)]
        + [pl.BlockSpec((lz, 4, 4), lvl)] * 4,
        out_shape=[jax.ShapeDtypeStruct((9, levels, cols), jnp.float32), jax.ShapeDtypeStruct((10, levels, cols), jnp.float32)]
        + [jax.ShapeDtypeStruct((levels, rows, 9), jnp.float32), jax.ShapeDtypeStruct((levels, rows, 10), jnp.float32)]
        + [jax.ShapeDtypeStruct((levels, 4, 4), jnp.float32)] * 4,
        compiler_params=pltpu.CompilerParams(dimension_semantics=("arbitrary",)),
    )
    xf, xl, yf, yl, cpp, cpm, cmp_, cmm = pack(
        press_bar, press_bar, theta_bar, theta_bar, winds, winds,
        press_bar, press_bar, theta_bar, theta_bar, winds, winds,
    )
    xn = from_side(xf, "gx", 1)
    xp = from_side(xl, "gx", -1)
    yn = from_side(yf, "gy", 1)
    yp = from_side(yl, "gy", -1)
    cpp = from_corner(cpp, 1, 1)
    cpm = from_corner(cpm, 1, -1)
    cmp_ = from_corner(cmp_, -1, 1)
    cmm = from_corner(cmm, -1, -1)

    f4 = jnp.stack(
        [urban_frac, urban_class.astype(jnp.float32), height_bin.astype(jnp.float32), canopy_layers.astype(jnp.float32)]
    )
    small = jnp.concatenate([theta[:kc], f4], axis=0)
    x8n = from_side(small[:, :3, :], "gx", 1)
    x8p = from_side(small[:, rows - 3 :, :], "gx", -1)
    y8n = from_side(small[:, :, :3], "gy", 1)
    y8p = from_side(small[:, :, cols - 3 :], "gy", -1)

    ix = lax.axis_index("gx")
    iy = lax.axis_index("gy")
    nx, ny = lax.axis_size("gx"), lax.axis_size("gy")
    r = jnp.arange(rext, dtype=jnp.int32)[:, None]
    cc = jnp.arange(cext, dtype=jnp.int32)[None, :]
    row_ok = (r < rows) | ((r < rows + 4) & (ix < nx - 1)) | ((r >= rext - 4) & (ix > 0))
    col_ok = (cc < cols) | ((cc < cols + 4) & (iy < ny - 1)) | ((cc >= cext - 4) & (iy > 0))
    mask = (row_ok & col_ok).astype(jnp.float32)
    bp8 = bin_profile[:, :kc].reshape(-1)

    zero1 = jnp.zeros((1,), jnp.float32)
    lower = jnp.concatenate([zero1, -sound_coef[:-1]])
    upper = jnp.concatenate([-sound_coef[1:], zero1])
    middle = 1.0 + 2.0 * sound_coef

    ph0 = lambda p, b: (jnp.where(p == 0, b, nblk - 1), 0, 0)
    ph2 = lambda p, b: (jnp.where(p == 2, b, 0), 0, 0)
    ph02 = lambda p, b: (jnp.where(p == 1, nblk - 1, b), 0, 0)
    const3 = lambda p, b: (0, 0, 0)
    const2 = lambda p, b: (0, 0)
    smem = pl.BlockSpec(memory_space=pltpu.SMEM)
    n_small = small.shape[0]
    in_specs = [
        smem, smem, smem, smem, smem,
        pl.BlockSpec((lz, rows, cols), ph0),
        pl.BlockSpec((lz, rows, cols), ph2),
        pl.BlockSpec((None, lz, rows, cols), lambda p, b: (0, jnp.where(p == 2, b, 0), 0, 0)),
        pl.BlockSpec((None, lz, rows, cols), lambda p, b: (1, jnp.where(p == 2, b, 0), 0, 0)),
        pl.BlockSpec((9, levels, cols), const3),
        pl.BlockSpec((10, levels, cols), const3),
        pl.BlockSpec((lz, rows, 9), ph02),
        pl.BlockSpec((lz, rows, 10), ph02),
        pl.BlockSpec((lz, 4, 4), ph0),
        pl.BlockSpec((lz, 4, 4), ph0),
        pl.BlockSpec((lz, 4, 4), ph0),
        pl.BlockSpec((lz, 4, 4), ph0),
        pl.BlockSpec((kc, rows, cols), const3),
        pl.BlockSpec((n_small, 3, cols), const3),
        pl.BlockSpec((n_small, 3, cols), const3),
        pl.BlockSpec((n_small, rows, 3), const3),
        pl.BlockSpec((n_small, rows, 3), const3),
        pl.BlockSpec((4, rows, cols), const3),
        pl.BlockSpec((rows, cols), const2),
        pl.BlockSpec((rext, cext), const2),
    ]
    out_specs = [
        pl.BlockSpec((lz, rows, cols), ph2),
        pl.BlockSpec((lz, rows, cols), ph2),
        pl.BlockSpec((rows, cols), const2),
        pl.BlockSpec((rows, cols), const2),
    ]
    out_shape = [
        jax.ShapeDtypeStruct((levels, rows, cols), jnp.float32),
        jax.ShapeDtypeStruct((levels, rows, cols), jnp.float32),
        jax.ShapeDtypeStruct((rows, cols), jnp.float32),
        jax.ShapeDtypeStruct((rows, cols), jnp.float32),
    ]
    scratch = [
        pltpu.VMEM((levels, rext, cext), jnp.float32),
        pltpu.VMEM((levels, rext, cext), jnp.float32),
        pltpu.VMEM((rext, cext), jnp.float32),
        pltpu.VMEM((rext, cext), jnp.float32),
        pltpu.VMEM((1, cext), jnp.float32),
        pltpu.VMEM((levels, 1, cext), jnp.float32),
        pltpu.VMEM((levels, 1, cext), jnp.float32),
    ]
    call = pl.pallas_call(
        kernel,
        grid=(3, nblk),
        in_specs=in_specs,
        out_specs=out_specs,
        out_shape=out_shape,
        scratch_shapes=scratch,
        compiler_params=pltpu.CompilerParams(
            dimension_semantics=("arbitrary", "arbitrary"),
            vmem_limit_bytes=56 * 1024 * 1024,
        ),
    )
    tg, pg, fg, wg = call(
        lower, middle, upper, bp8, class_drag,
        press_bar, theta_bar, winds, winds, xn, xp, yn, yp, cpp, cpm, cmp_, cmm,
        theta, x8n, x8p, y8n, y8p, f4, wall_temp, mask,
    )
    return tg, pg, fg, wg


def extend_xla(main, rows, cols, corner):
    levels = main.shape[0]
    if corner is None:
        corner = jnp.zeros((levels, rows.shape[1], cols.shape[2]), main.dtype)
    return jnp.concatenate(
        [jnp.concatenate([main, rows], axis=1), jnp.concatenate([cols, corner], axis=1)], axis=2
    )


def solution(mesh):
    in_specs = (
        P(None, "gx", "gy"),
        P(None, None, "gx", "gy"),
        P(None, "gx", "gy"),
        P(None, "gx", "gy"),
        P("gx", "gy"),
        P("gx", "gy"),
        P("gx", "gy"),
        P("gx", "gy"),
        P("gx", "gy"),
        P(),
        P(),
        P(),
    )
    out_specs = (P(None, "gx", "gy"), P(None, "gx", "gy"), P("gx", "gy"), P("gx", "gy"))
    return jax.shard_map(
        per_device, mesh=mesh, in_specs=in_specs, out_specs=out_specs, check_vma=False
    )
```

```python
import functools

import jax
import jax.numpy as jnp
from jax import lax
from jax.experimental import pallas as pl
from jax.experimental.pallas import tpu as pltpu
from jax.sharding import PartitionSpec as P

courant = 0.3
diffusion = 0.1
buoyancy = 0.5
canopy_levels = 8
halo_rows = 8
strip = 128
block_levels = 20


def from_side(x, axis, delta):
    n = lax.axis_size(axis)
    if delta > 0:
        pairs = [(i + delta, i) for i in range(n - delta)]
    else:
        pairs = [(i, i - delta) for i in range(n + delta)]
    return lax.ppermute(x, axis, pairs)


def from_corner(x, dx, dy):
    nx, ny = lax.axis_size("gx"), lax.axis_size("gy")
    pairs = []
    for ix in range(nx):
        for iy in range(ny):
            sx, sy = ix + dx, iy + dy
            if 0 <= sx < nx and 0 <= sy < ny:
                pairs.append((sx * ny + sy, ix * ny + iy))
    return lax.ppermute(x, ("gx", "gy"), pairs)


def row_halo(f, lo, hi):
    levels, rows, cols = f.shape
    parts = []
    if hi:
        parts.append(from_side(f[:, :hi, :], "gx", 1))
    parts.append(jnp.zeros((levels, halo_rows - hi - lo, cols), f.dtype))
    if lo:
        parts.append(from_side(f[:, rows - lo :, :], "gx", -1))
    return jnp.concatenate(parts, axis=1)


def col_halo(f, lo, hi):
    levels, rows, cols = f.shape
    parts = []
    if hi:
        parts.append(from_side(f[:, :, :hi], "gy", 1))
    parts.append(jnp.zeros((levels, rows, strip - hi - lo), f.dtype))
    if lo:
        parts.append(from_side(f[:, :, cols - lo :], "gy", -1))
    return jnp.concatenate(parts, axis=2)


def corner_rows(f, w):
    levels, rows, cols = f.shape
    mid = jnp.zeros((levels, w, strip - 2 * w), f.dtype)
    gap = jnp.zeros((levels, halo_rows - 2 * w, strip), f.dtype)
    top = jnp.concatenate(
        [from_corner(f[:, :w, :w], 1, 1), mid, from_corner(f[:, :w, cols - w :], 1, -1)], axis=2
    )
    bottom = jnp.concatenate(
        [from_corner(f[:, rows - w :, :w], -1, 1), mid, from_corner(f[:, rows - w :, cols - w :], -1, -1)],
        axis=2,
    )
    return jnp.concatenate([top, gap, bottom], axis=1)


def ahead(x, k, axis):
    if k == 0:
        return x
    n = x.shape[axis]
    return pltpu.roll(x, (-k) % n, axis)


def forward_tend(f, u, axis):
    fm2, fm1, f0, f1, f2, f3 = [ahead(f, k, axis) for k in (-2, -1, 0, 1, 2, 3)]
    a_sum = (fm2 + f3) - 8.0 * (fm1 + f2) + 37.0 * (f0 + f1)
    b_sum = (fm2 - f3) - 5.0 * (fm1 - f2) + 10.0 * (f0 - f1)
    flux = (u * a_sum + jnp.abs(u) * b_sum) * (1.0 / 60.0)
    return -courant * (flux - ahead(flux, -1, axis))


def adjoint_tend(f, u, axis):
    g = courant * (ahead(f, 1, axis) - f)
    pu = u * g
    qu = jnp.abs(u) * g
    total = (
        ahead(pu + qu, 2, axis)
        + ahead(-8.0 * pu - 5.0 * qu, 1, axis)
        + (37.0 * pu + 10.0 * qu)
        + ahead(37.0 * pu - 10.0 * qu, -1, axis)
        + ahead(-8.0 * pu + 5.0 * qu, -2, axis)
        + ahead(pu - qu, -3, axis)
    )
    return total * (1.0 / 60.0)


def laplace(q):
    return ahead(q, 1, 0) + ahead(q, -1, 0) + ahead(q, 1, 1) + ahead(q, -1, 1) - 4.0 * q


def extend(main, rows, cols):
    return jnp.concatenate([jnp.concatenate([main, rows], axis=0), cols], axis=1)


def pack_kernel(pbf, pbl, tbf, tbl, u0f, u0l, pcf, pcl, tcf, tcl, ucf, ucl,
                xf, xl, yf, yl, cpp, cpm, cmp_, cmm):
    lz = pbf.shape[0]
    rows = pcf.shape[1]
    lane = lax.broadcasted_iota(jnp.int32, (rows, strip), 1)

    def body(j, c):
        k = pl.program_id(0) * lz + j
        xf[:, k, :] = jnp.concatenate([pbf[j][0:4], tbf[j][0:3], u0f[j][0:2]], axis=0)
        xl[:, k, :] = jnp.concatenate([pbl[j][4:8], tbl[j][5:8], u0l[j][5:8]], axis=0)
        a, b, u = pcf[j], tcf[j], ucf[j]
        first = jnp.where(lane < 4, a, jnp.where(lane < 7, pltpu.roll(b, 4, 1), pltpu.roll(u, 7, 1)))
        yf[j] = first[:, :9]
        a, b, u = pcl[j], tcl[j], ucl[j]
        last = jnp.where(
            lane < 4, pltpu.roll(a, 4, 1), jnp.where(lane < 7, pltpu.roll(b, 7, 1), pltpu.roll(u, 10, 1))
        )
        yl[j] = last[:, :10]
        top_first, top_last = pcf[j][0:4], pcl[j][0:4]
        bot_first, bot_last = pcf[j][rows - 4 : rows], pcl[j][rows - 4 : rows]
        cpp[j] = top_first[:, 0:4]
        cpm[j] = top_last[:, strip - 4 : strip]
        cmp_[j] = bot_first[:, 0:4]
        cmm[j] = bot_last[:, strip - 4 : strip]
        return c

    lax.fori_loop(0, lz, body, 0)


def lane_strip(near, far, width):
    rows = near.shape[0]
    a = jnp.concatenate([near, jnp.zeros((rows, strip - width), jnp.float32)], axis=1)
    b = jnp.concatenate([far, jnp.zeros((rows, strip - width), jnp.float32)], axis=1)
    return a + pltpu.roll(b, strip - width, 1)


def kernel(
    lo_ref, mid_ref, up_ref, bp_ref, cd_ref,
    pbm, tbm, u0m, u1m, xn, xp, yn, yp, cpp, cpm, cmp_, cmm,
    thm, x8n, x8p, y8n, y8p, f4, wall, mask,
    tg_out, pg_out, fg_out, wg_out,
    dd, qa, car_a, car_b, cpc, cp1, cq2,
):
    phase = pl.program_id(0)
    blk = pl.program_id(1)
    nblk = pl.num_programs(1)
    lz = pbm.shape[0]
    rows, cols = pbm.shape[1], pbm.shape[2]
    wide = cpc.shape[1]
    lane = lax.broadcasted_iota(jnp.int32, (rows, strip), 1)

    def coef(ref, k):
        return jnp.full((1, wide), ref[k], jnp.float32)

    def ystrip(j, off, wn, wp):
        n = jnp.concatenate([yn[j], jnp.zeros((rows, strip - yn.shape[2]), jnp.float32)], axis=1)
        p = jnp.concatenate([yp[j], jnp.zeros((rows, strip - yp.shape[2]), jnp.float32)], axis=1)
        n = pltpu.roll(n, (strip - off) % strip, 1)
        p = pltpu.roll(p, strip - wp - off, 1)
        return jnp.where(lane < wn, n, jnp.where(lane >= strip - wp, p, 0.0))

    def press_ext(j, k):
        xr = jnp.concatenate([pbm[j], xn[:, k, :][0:4], xp[:, k, :][0:4]], axis=0)
        top = lane_strip(cpp[j], cpm[j], 4)[0:4]
        bot = lane_strip(cmp_[j], cmm[j], 4)[0:4]
        ys = jnp.concatenate([ystrip(j, 0, 4, 4), top, bot], axis=0)
        return jnp.concatenate([xr, ys], axis=1)

    @pl.when(phase == 0)
    def _():
        @pl.when(blk == 0)
        def _():
            car_a[...] = jnp.zeros(car_a.shape, jnp.float32)
            cpc[...] = jnp.zeros(cpc.shape, jnp.float32)

        def body(j, c):
            k = blk * lz + j
            ak = coef(lo_ref, k)
            r = 1.0 / (coef(mid_ref, k) - ak * cpc[...])
            cp = coef(up_ref, k) * r
            cpc[...] = cp
            cp1[k] = cp
            d = press_ext(j, k)
            dn = (d - ak * car_a[...]) * r
            car_a[...] = dn
            dd[k] = dn
            return c

        lax.fori_loop(0, lz, body, 0)

    @pl.when(phase == 1)
    def _():
        @pl.when(blk == 0)
        def _():
            car_a[...] = jnp.zeros(car_a.shape, jnp.float32)
            car_b[...] = jnp.zeros(car_b.shape, jnp.float32)
            cpc[...] = jnp.zeros(cpc.shape, jnp.float32)

        def body(j, c):
            k = (nblk - 1 - blk) * lz + (lz - 1 - j)
            x = dd[k] - cp1[k] * car_a[...]
            car_a[...] = x
            qa[k] = x
            pb1 = (x + diffusion * laplace(x)) * mask[...]
            ck = coef(up_ref, k)
            s = 1.0 / (coef(mid_ref, k) - ck * cpc[...])
            cq = coef(lo_ref, k) * s
            cpc[...] = cq
            cq2[k] = cq
            e = (pb1 - ck * car_b[...]) * s
            car_b[...] = e
            dd[k] = e
            return c

        lax.fori_loop(0, lz, body, 0)

    @pl.when(phase == 2)
    def _():
        @pl.when(blk == 0)
        def _():
            car_a[...] = jnp.zeros(car_a.shape, jnp.float32)

        def field_ext(i):
            xr = jnp.concatenate(
                [f4[i], x8n[8 + i], jnp.zeros((2, cols), jnp.float32), x8p[8 + i]], axis=0
            )
            ys = jnp.concatenate(
                [lane_strip(y8n[8 + i], y8p[8 + i], 3), jnp.zeros((halo_rows, strip), jnp.float32)], axis=0
            )
            return jnp.concatenate([xr, ys], axis=1)

        def level(j, canopy, acc):
            k = blk * lz + j
            qb = dd[k] - cq2[k] * car_a[...]
            car_a[...] = qb
            pg = qb + diffusion * laplace(qb)
            pg_out[j] = pg[:rows, :cols]
            xnj, xpj = xn[:, k, :], xp[:, k, :]
            tbx = jnp.concatenate([tbm[j], xnj[4:7], jnp.zeros((2, cols), jnp.float32), xpj[4:7]], axis=0)
            tby = jnp.concatenate([ystrip(j, 4, 3, 3), jnp.zeros((halo_rows, strip), jnp.float32)], axis=0)
            th2b = jnp.concatenate([tbx, tby], axis=1) + buoyancy * (qa[k] + qb)
            if canopy:
                ud, cls, hb, lay = acc[2]
                prof = jnp.zeros(hb.shape, jnp.float32)
                for bb in range(bp_ref.shape[0] // canopy_levels):
                    prof = jnp.where(hb == float(bb), bp_ref[bb * canopy_levels + j], prof)
                act = jnp.where(lay > j.astype(jnp.float32), 1.0, 0.0)
                am = ud * prof * act
                th1b = (1.0 - am) * th2b
            else:
                th1b = th2b
            u0e = jnp.concatenate([u0m[j], xnj[7:9], jnp.zeros((3, cols), jnp.float32), xpj[7:10]], axis=0)
            u1e = jnp.concatenate([u1m[j], ystrip(j, 7, 2, 3)], axis=1)
            adv = adjoint_tend(th1b[:, :cols], u0e, 0)[:rows, :] + adjoint_tend(th1b[:rows, :], u1e, 1)[:, :cols]
            tg_out[j] = th1b[:rows, :cols] + adv
            if canopy:
                th = thm[j]
                thx = jnp.concatenate([th, x8n[j], jnp.zeros((2, cols), jnp.float32), x8p[j]], axis=0)
                thy = jnp.concatenate([th, lane_strip(y8n[j], y8p[j], 3)], axis=1)
                fx = forward_tend(thx, u0e, 0)[:rows, :]
                fy = forward_tend(thy, u1e, 1)[:, :cols]
                first = th + (fx + fy)
                sb = th2b[:rows, :cols]
                fg, wg, fields, drag = acc
                dpa = drag * prof[:rows, :cols] * act[:rows, :cols]
                fg = fg + dpa * (wall[...] - first) * sb
                wg = wg + am[:rows, :cols] * sb
                acc = (fg, wg, fields, drag)
            return acc

        @pl.when(blk == 0)
        def _():
            zero = jnp.zeros((rows, cols), jnp.float32)
            cls = field_ext(1)
            drag = jnp.zeros(cls.shape, jnp.float32)
            for c in range(cd_ref.shape[0]):
                drag = jnp.where(cls == float(c), cd_ref[c], drag)
            ud = field_ext(0) * drag
            fields = (ud, cls, field_ext(2), field_ext(3))
            fg, wg, _, _ = lax.fori_loop(
                0, canopy_levels, lambda j, a: level(j, True, a), (zero, zero, fields, drag[:rows, :cols])
            )
            fg_out[...] = fg
            wg_out[...] = wg
            lax.fori_loop(canopy_levels, lz, lambda j, a: level(j, False, a), 0)

        @pl.when(blk > 0)
        def _():
            lax.fori_loop(0, lz, lambda j, a: level(j, False, a), 0)


def per_device(
    theta, winds, theta_bar, press_bar, urban_frac, wall_temp, urban_class, canopy_layers,
    height_bin, class_drag, bin_profile, sound_coef,
):
    levels, rows, cols = theta.shape
    rext, cext = rows + halo_rows, cols + strip
    lz = block_levels
    nblk = levels // lz
    kc = canopy_levels
    rb, cb = rows // 8 - 1, cols // strip - 1

    lvl = lambda b: (b, 0, 0)
    pack = pl.pallas_call(
        pack_kernel,
        grid=(nblk,),
        in_specs=[
            pl.BlockSpec((lz, 8, cols), lvl),
            pl.BlockSpec((lz, 8, cols), lambda b: (b, rb, 0)),
            pl.BlockSpec((lz, 8, cols), lvl),
            pl.BlockSpec((lz, 8, cols), lambda b: (b, rb, 0)),
            pl.BlockSpec((None, lz, 8, cols), lambda b: (0, b, 0, 0)),
            pl.BlockSpec((None, lz, 8, cols), lambda b: (0, b, rb, 0)),
            pl.BlockSpec((lz, rows, strip), lvl),
            pl.BlockSpec((lz, rows, strip), lambda b: (b, 0, cb)),
            pl.BlockSpec((lz, rows, strip), lvl),
            pl.BlockSpec((lz, rows, strip), lambda b: (b, 0, cb)),
            pl.BlockSpec((None, lz, rows, strip), lambda b: (1, b, 0, 0)),
            pl.BlockSpec((None, lz, rows, strip), lambda b: (1, b, 0, cb)),
        ],
        out_specs=[pl.BlockSpec((9, levels, cols), lambda b: (0, 0, 0)), pl.BlockSpec((10, levels, cols), lambda b: (0, 0, 0))]
        + [pl.BlockSpec((lz, rows, 9), lvl), pl.BlockSpec((lz, rows, 10), lvl)]
        + [pl.BlockSpec((lz, 4, 4), lvl)] * 4,
        out_shape=[jax.ShapeDtypeStruct((9, levels, cols), jnp.float32), jax.ShapeDtypeStruct((10, levels, cols), jnp.float32)]
        + [jax.ShapeDtypeStruct((levels, rows, 9), jnp.float32), jax.ShapeDtypeStruct((levels, rows, 10), jnp.float32)]
        + [jax.ShapeDtypeStruct((levels, 4, 4), jnp.float32)] * 4,
        compiler_params=pltpu.CompilerParams(dimension_semantics=("arbitrary",)),
    )
    xf, xl, yf, yl, cpp, cpm, cmp_, cmm = pack(
        press_bar, press_bar, theta_bar, theta_bar, winds, winds,
        press_bar, press_bar, theta_bar, theta_bar, winds, winds,
    )
    xn = from_side(xf, "gx", 1)
    xp = from_side(xl, "gx", -1)
    yn = from_side(yf, "gy", 1)
    yp = from_side(yl, "gy", -1)
    cpp = from_corner(cpp, 1, 1)
    cpm = from_corner(cpm, 1, -1)
    cmp_ = from_corner(cmp_, -1, 1)
    cmm = from_corner(cmm, -1, -1)

    f4 = jnp.stack(
        [urban_frac, urban_class.astype(jnp.float32), height_bin.astype(jnp.float32), canopy_layers.astype(jnp.float32)]
    )
    small = jnp.concatenate([theta[:kc], f4], axis=0)
    x8n = from_side(small[:, :3, :], "gx", 1)
    x8p = from_side(small[:, rows - 3 :, :], "gx", -1)
    y8n = from_side(small[:, :, :3], "gy", 1)
    y8p = from_side(small[:, :, cols - 3 :], "gy", -1)

    ix = lax.axis_index("gx")
    iy = lax.axis_index("gy")
    nx, ny = lax.axis_size("gx"), lax.axis_size("gy")
    r = jnp.arange(rext, dtype=jnp.int32)[:, None]
    cc = jnp.arange(cext, dtype=jnp.int32)[None, :]
    row_ok = (r < rows) | ((r < rows + 4) & (ix < nx - 1)) | ((r >= rext - 4) & (ix > 0))
    col_ok = (cc < cols) | ((cc < cols + 4) & (iy < ny - 1)) | ((cc >= cext - 4) & (iy > 0))
    mask = (row_ok & col_ok).astype(jnp.float32)
    bp8 = bin_profile[:, :kc].reshape(-1)

    zero1 = jnp.zeros((1,), jnp.float32)
    lower = jnp.concatenate([zero1, -sound_coef[:-1]])
    upper = jnp.concatenate([-sound_coef[1:], zero1])
    middle = 1.0 + 2.0 * sound_coef

    ph0 = lambda p, b: (jnp.where(p == 0, b, nblk - 1), 0, 0)
    ph2 = lambda p, b: (jnp.where(p == 2, b, 0), 0, 0)
    ph02 = lambda p, b: (jnp.where(p == 1, nblk - 1, b), 0, 0)
    const3 = lambda p, b: (0, 0, 0)
    const2 = lambda p, b: (0, 0)
    smem = pl.BlockSpec(memory_space=pltpu.SMEM)
    n_small = small.shape[0]
    in_specs = [
        smem, smem, smem, smem, smem,
        pl.BlockSpec((lz, rows, cols), ph0),
        pl.BlockSpec((lz, rows, cols), ph2),
        pl.BlockSpec((None, lz, rows, cols), lambda p, b: (0, jnp.where(p == 2, b, 0), 0, 0)),
        pl.BlockSpec((None, lz, rows, cols), lambda p, b: (1, jnp.where(p == 2, b, 0), 0, 0)),
        pl.BlockSpec((9, levels, cols), const3),
        pl.BlockSpec((10, levels, cols), const3),
        pl.BlockSpec((lz, rows, 9), ph02),
        pl.BlockSpec((lz, rows, 10), ph02),
        pl.BlockSpec((lz, 4, 4), ph0),
        pl.BlockSpec((lz, 4, 4), ph0),
        pl.BlockSpec((lz, 4, 4), ph0),
        pl.BlockSpec((lz, 4, 4), ph0),
        pl.BlockSpec((kc, rows, cols), const3),
        pl.BlockSpec((n_small, 3, cols), const3),
        pl.BlockSpec((n_small, 3, cols), const3),
        pl.BlockSpec((n_small, rows, 3), const3),
        pl.BlockSpec((n_small, rows, 3), const3),
        pl.BlockSpec((4, rows, cols), const3),
        pl.BlockSpec((rows, cols), const2),
        pl.BlockSpec((rext, cext), const2),
    ]
    out_specs = [
        pl.BlockSpec((lz, rows, cols), ph2),
        pl.BlockSpec((lz, rows, cols), ph2),
        pl.BlockSpec((rows, cols), const2),
        pl.BlockSpec((rows, cols), const2),
    ]
    out_shape = [
        jax.ShapeDtypeStruct((levels, rows, cols), jnp.float32),
        jax.ShapeDtypeStruct((levels, rows, cols), jnp.float32),
        jax.ShapeDtypeStruct((rows, cols), jnp.float32),
        jax.ShapeDtypeStruct((rows, cols), jnp.float32),
    ]
    scratch = [
        pltpu.VMEM((levels, rext, cext), jnp.float32),
        pltpu.VMEM((levels, rext, cext), jnp.float32),
        pltpu.VMEM((rext, cext), jnp.float32),
        pltpu.VMEM((rext, cext), jnp.float32),
        pltpu.VMEM((1, cext), jnp.float32),
        pltpu.VMEM((levels, 1, cext), jnp.float32),
        pltpu.VMEM((levels, 1, cext), jnp.float32),
    ]
    call = pl.pallas_call(
        kernel,
        grid=(3, nblk),
        in_specs=in_specs,
        out_specs=out_specs,
        out_shape=out_shape,
        scratch_shapes=scratch,
        compiler_params=pltpu.CompilerParams(
            dimension_semantics=("arbitrary", "arbitrary"),
            vmem_limit_bytes=56 * 1024 * 1024,
        ),
    )
    tg, pg, fg, wg = call(
        lower, middle, upper, bp8, class_drag,
        press_bar, theta_bar, winds, winds, xn, xp, yn, yp, cpp, cpm, cmp_, cmm,
        theta, x8n, x8p, y8n, y8p, f4, wall_temp, mask,
    )
    return tg, pg, fg, wg


def extend_xla(main, rows, cols, corner):
    levels = main.shape[0]
    if corner is None:
        corner = jnp.zeros((levels, rows.shape[1], cols.shape[2]), main.dtype)
    return jnp.concatenate(
        [jnp.concatenate([main, rows], axis=1), jnp.concatenate([cols, corner], axis=1)], axis=2
    )


def solution(mesh):
    in_specs = (
        P(None, "gx", "gy"),
        P(None, None, "gx", "gy"),
        P(None, "gx", "gy"),
        P(None, "gx", "gy"),
        P("gx", "gy"),
        P("gx", "gy"),
        P("gx", "gy"),
        P("gx", "gy"),
        P("gx", "gy"),
        P(),
        P(),
        P(),
    )
    out_specs = (P(None, "gx", "gy"), P(None, "gx", "gy"), P("gx", "gy"), P("gx", "gy"))
    return jax.shard_map(
        per_device, mesh=mesh, in_specs=in_specs, out_specs=out_specs, check_vma=False
    )
```

```python
import functools

import jax
import jax.numpy as jnp
from jax import lax
from jax.experimental import pallas as pl
from jax.experimental.pallas import tpu as pltpu
from jax.sharding import PartitionSpec as P

courant = 0.3
diffusion = 0.1
buoyancy = 0.5
canopy_levels = 8
halo_rows = 8
strip = 128
block_levels = 20


def from_side(x, axis, delta):
    n = lax.axis_size(axis)
    if delta > 0:
        pairs = [(i + delta, i) for i in range(n - delta)]
    else:
        pairs = [(i, i - delta) for i in range(n + delta)]
    return lax.ppermute(x, axis, pairs)


def from_corner(x, dx, dy):
    nx, ny = lax.axis_size("gx"), lax.axis_size("gy")
    pairs = []
    for ix in range(nx):
        for iy in range(ny):
            sx, sy = ix + dx, iy + dy
            if 0 <= sx < nx and 0 <= sy < ny:
                pairs.append((sx * ny + sy, ix * ny + iy))
    return lax.ppermute(x, ("gx", "gy"), pairs)


def row_halo(f, lo, hi):
    levels, rows, cols = f.shape
    parts = []
    if hi:
        parts.append(from_side(f[:, :hi, :], "gx", 1))
    parts.append(jnp.zeros((levels, halo_rows - hi - lo, cols), f.dtype))
    if lo:
        parts.append(from_side(f[:, rows - lo :, :], "gx", -1))
    return jnp.concatenate(parts, axis=1)


def col_halo(f, lo, hi):
    levels, rows, cols = f.shape
    parts = []
    if hi:
        parts.append(from_side(f[:, :, :hi], "gy", 1))
    parts.append(jnp.zeros((levels, rows, strip - hi - lo), f.dtype))
    if lo:
        parts.append(from_side(f[:, :, cols - lo :], "gy", -1))
    return jnp.concatenate(parts, axis=2)


def corner_rows(f, w):
    levels, rows, cols = f.shape
    mid = jnp.zeros((levels, w, strip - 2 * w), f.dtype)
    gap = jnp.zeros((levels, halo_rows - 2 * w, strip), f.dtype)
    top = jnp.concatenate(
        [from_corner(f[:, :w, :w], 1, 1), mid, from_corner(f[:, :w, cols - w :], 1, -1)], axis=2
    )
    bottom = jnp.concatenate(
        [from_corner(f[:, rows - w :, :w], -1, 1), mid, from_corner(f[:, rows - w :, cols - w :], -1, -1)],
        axis=2,
    )
    return jnp.concatenate([top, gap, bottom], axis=1)


def ahead(x, k, axis):
    if k == 0:
        return x
    n = x.shape[axis]
    return pltpu.roll(x, (-k) % n, axis)


def forward_tend(f, u, axis):
    fm2, fm1, f0, f1, f2, f3 = [ahead(f, k, axis) for k in (-2, -1, 0, 1, 2, 3)]
    a_sum = (fm2 + f3) - 8.0 * (fm1 + f2) + 37.0 * (f0 + f1)
    b_sum = (fm2 - f3) - 5.0 * (fm1 - f2) + 10.0 * (f0 - f1)
    flux = (u * a_sum + jnp.abs(u) * b_sum) * (1.0 / 60.0)
    return -courant * (flux - ahead(flux, -1, axis))


def adjoint_tend(f, u, axis):
    g = courant * (ahead(f, 1, axis) - f)
    pu = u * g
    qu = jnp.abs(u) * g
    total = (
        ahead(pu + qu, 2, axis)
        + ahead(-8.0 * pu - 5.0 * qu, 1, axis)
        + (37.0 * pu + 10.0 * qu)
        + ahead(37.0 * pu - 10.0 * qu, -1, axis)
        + ahead(-8.0 * pu + 5.0 * qu, -2, axis)
        + ahead(pu - qu, -3, axis)
    )
    return total * (1.0 / 60.0)


def laplace(q):
    return ahead(q, 1, 0) + ahead(q, -1, 0) + ahead(q, 1, 1) + ahead(q, -1, 1) - 4.0 * q


def extend(main, rows, cols):
    return jnp.concatenate([jnp.concatenate([main, rows], axis=0), cols], axis=1)


def pack_kernel(pbf, pbl, tbf, tbl, u0f, u0l, pcf, pcl, tcf, tcl, ucf, ucl,
                xf, xl, yf, yl, cpp, cpm, cmp_, cmm):
    lz = pbf.shape[0]
    rows = pcf.shape[1]
    lane = lax.broadcasted_iota(jnp.int32, (rows, strip), 1)

    def body(j, c):
        k = pl.program_id(0) * lz + j
        xf[:, k, :] = jnp.concatenate([pbf[j][0:4], tbf[j][0:3], u0f[j][0:2]], axis=0)
        xl[:, k, :] = jnp.concatenate([pbl[j][4:8], tbl[j][5:8], u0l[j][5:8]], axis=0)
        a, b, u = pcf[j], tcf[j], ucf[j]
        first = jnp.where(lane < 4, a, jnp.where(lane < 7, pltpu.roll(b, 4, 1), pltpu.roll(u, 7, 1)))
        yf[j] = first[:, :9]
        a, b, u = pcl[j], tcl[j], ucl[j]
        last = jnp.where(
            lane < 4, pltpu.roll(a, 4, 1), jnp.where(lane < 7, pltpu.roll(b, 7, 1), pltpu.roll(u, 10, 1))
        )
        yl[j] = last[:, :10]
        top_first, top_last = pcf[j][0:4], pcl[j][0:4]
        bot_first, bot_last = pcf[j][rows - 4 : rows], pcl[j][rows - 4 : rows]
        cpp[j] = top_first[:, 0:4]
        cpm[j] = top_last[:, strip - 4 : strip]
        cmp_[j] = bot_first[:, 0:4]
        cmm[j] = bot_last[:, strip - 4 : strip]
        return c

    lax.fori_loop(0, lz, body, 0)


def lane_strip(near, far, width):
    rows = near.shape[0]
    a = jnp.concatenate([near, jnp.zeros((rows, strip - width), jnp.float32)], axis=1)
    b = jnp.concatenate([far, jnp.zeros((rows, strip - width), jnp.float32)], axis=1)
    return a + pltpu.roll(b, strip - width, 1)


def kernel(
    lo_ref, mid_ref, up_ref, bp_ref, cd_ref,
    pbm, tbm, u0m, u1m, xn, xp, yn, yp,
    thm, x8n, x8p, y8n, y8p, f4, wall, mask,
    tg_out, pg_out, fg_out, wg_out,
    dd, qa, car_a, car_b, cpc, cp1, cq2,
):
    phase = pl.program_id(0)
    blk = pl.program_id(1)
    nblk = pl.num_programs(1)
    lz = pbm.shape[0]
    rows, cols = pbm.shape[1], pbm.shape[2]
    wide = cpc.shape[1]
    rext = yn.shape[1]
    lane = lax.broadcasted_iota(jnp.int32, (rext, strip), 1)

    def coef(ref, k):
        return jnp.full((1, wide), ref[k], jnp.float32)

    def ystrip(j, off, wn, wp):
        n = jnp.concatenate([yn[j], jnp.zeros((rext, strip - yn.shape[2]), jnp.float32)], axis=1)
        p = jnp.concatenate([yp[j], jnp.zeros((rext, strip - yp.shape[2]), jnp.float32)], axis=1)
        n = pltpu.roll(n, (strip - off) % strip, 1)
        p = pltpu.roll(p, strip - wp - off, 1)
        return jnp.where(lane < wn, n, jnp.where(lane >= strip - wp, p, 0.0))

    def press_ext(j, k):
        xr = jnp.concatenate([pbm[j], xn[:, k, :][0:4], xp[:, k, :][0:4]], axis=0)
        return jnp.concatenate([xr, ystrip(j, 0, 4, 4)], axis=1)

    @pl.when(phase == 0)
    def _():
        @pl.when(blk == 0)
        def _():
            car_a[...] = jnp.zeros(car_a.shape, jnp.float32)
            cpc[...] = jnp.zeros(cpc.shape, jnp.float32)

        def body(j, c):
            k = blk * lz + j
            ak = coef(lo_ref, k)
            r = 1.0 / (coef(mid_ref, k) - ak * cpc[...])
            cp = coef(up_ref, k) * r
            cpc[...] = cp
            cp1[k] = cp
            d = press_ext(j, k)
            dn = (d - ak * car_a[...]) * r
            car_a[...] = dn
            dd[k] = dn
            return c

        lax.fori_loop(0, lz, body, 0)

    @pl.when(phase == 1)
    def _():
        @pl.when(blk == 0)
        def _():
            car_a[...] = jnp.zeros(car_a.shape, jnp.float32)
            car_b[...] = jnp.zeros(car_b.shape, jnp.float32)
            cpc[...] = jnp.zeros(cpc.shape, jnp.float32)

        def body(j, c):
            k = (nblk - 1 - blk) * lz + (lz - 1 - j)
            x = dd[k] - cp1[k] * car_a[...]
            car_a[...] = x
            qa[k] = x
            pb1 = (x + diffusion * laplace(x)) * mask[...]
            ck = coef(up_ref, k)
            s = 1.0 / (coef(mid_ref, k) - ck * cpc[...])
            cq = coef(lo_ref, k) * s
            cpc[...] = cq
            cq2[k] = cq
            e = (pb1 - ck * car_b[...]) * s
            car_b[...] = e
            dd[k] = e
            return c

        lax.fori_loop(0, lz, body, 0)

    @pl.when(phase == 2)
    def _():
        @pl.when(blk == 0)
        def _():
            car_a[...] = jnp.zeros(car_a.shape, jnp.float32)

        def field_ext(i):
            xr = jnp.concatenate(
                [f4[i], x8n[8 + i], jnp.zeros((2, cols), jnp.float32), x8p[8 + i]], axis=0
            )
            ys = jnp.concatenate(
                [lane_strip(y8n[8 + i], y8p[8 + i], 3), jnp.zeros((halo_rows, strip), jnp.float32)], axis=0
            )
            return jnp.concatenate([xr, ys], axis=1)

        def level(j, canopy, acc):
            k = blk * lz + j
            qb = dd[k] - cq2[k] * car_a[...]
            car_a[...] = qb
            pg = qb + diffusion * laplace(qb)
            pg_out[j] = pg[:rows, :cols]
            xnj, xpj = xn[:, k, :], xp[:, k, :]
            tbx = jnp.concatenate([tbm[j], xnj[4:7], jnp.zeros((2, cols), jnp.float32), xpj[4:7]], axis=0)
            tby = ystrip(j, 4, 3, 3)
            th2b = jnp.concatenate([tbx, tby], axis=1) + buoyancy * (qa[k] + qb)
            if canopy:
                ud, cls, hb, lay = acc[2]
                prof = jnp.zeros(hb.shape, jnp.float32)
                for bb in range(bp_ref.shape[0] // canopy_levels):
                    prof = jnp.where(hb == float(bb), bp_ref[bb * canopy_levels + j], prof)
                act = jnp.where(lay > j.astype(jnp.float32), 1.0, 0.0)
                am = ud * prof * act
                th1b = (1.0 - am) * th2b
            else:
                th1b = th2b
            u0e = jnp.concatenate([u0m[j], xnj[7:9], jnp.zeros((3, cols), jnp.float32), xpj[7:10]], axis=0)
            u1e = jnp.concatenate([u1m[j], ystrip(j, 7, 2, 3)[:rows]], axis=1)
            adv = adjoint_tend(th1b[:, :cols], u0e, 0)[:rows, :] + adjoint_tend(th1b[:rows, :], u1e, 1)[:, :cols]
            tg_out[j] = th1b[:rows, :cols] + adv
            if canopy:
                th = thm[j]
                thx = jnp.concatenate([th, x8n[j], jnp.zeros((2, cols), jnp.float32), x8p[j]], axis=0)
                thy = jnp.concatenate([th, lane_strip(y8n[j], y8p[j], 3)], axis=1)
                fx = forward_tend(thx, u0e, 0)[:rows, :]
                fy = forward_tend(thy, u1e, 1)[:, :cols]
                first = th + (fx + fy)
                sb = th2b[:rows, :cols]
                fg, wg, fields, drag = acc
                dpa = drag * prof[:rows, :cols] * act[:rows, :cols]
                fg = fg + dpa * (wall[...] - first) * sb
                wg = wg + am[:rows, :cols] * sb
                acc = (fg, wg, fields, drag)
            return acc

        @pl.when(blk == 0)
        def _():
            zero = jnp.zeros((rows, cols), jnp.float32)
            cls = field_ext(1)
            drag = jnp.zeros(cls.shape, jnp.float32)
            for c in range(cd_ref.shape[0]):
                drag = jnp.where(cls == float(c), cd_ref[c], drag)
            ud = field_ext(0) * drag
            fields = (ud, cls, field_ext(2), field_ext(3))
            fg, wg, _, _ = lax.fori_loop(
                0, canopy_levels, lambda j, a: level(j, True, a), (zero, zero, fields, drag[:rows, :cols])
            )
            fg_out[...] = fg
            wg_out[...] = wg
            lax.fori_loop(canopy_levels, lz, lambda j, a: level(j, False, a), 0)

        @pl.when(blk > 0)
        def _():
            lax.fori_loop(0, lz, lambda j, a: level(j, False, a), 0)


def per_device(
    theta, winds, theta_bar, press_bar, urban_frac, wall_temp, urban_class, canopy_layers,
    height_bin, class_drag, bin_profile, sound_coef,
):
    levels, rows, cols = theta.shape
    rext, cext = rows + halo_rows, cols + strip
    lz = block_levels
    nblk = levels // lz
    kc = canopy_levels
    rb, cb = rows // 8 - 1, cols // strip - 1

    lvl = lambda b: (b, 0, 0)
    pack = pl.pallas_call(
        pack_kernel,
        grid=(nblk,),
        in_specs=[
            pl.BlockSpec((lz, 8, cols), lvl),
            pl.BlockSpec((lz, 8, cols), lambda b: (b, rb, 0)),
            pl.BlockSpec((lz, 8, cols), lvl),
            pl.BlockSpec((lz, 8, cols), lambda b: (b, rb, 0)),
            pl.BlockSpec((None, lz, 8, cols), lambda b: (0, b, 0, 0)),
            pl.BlockSpec((None, lz, 8, cols), lambda b: (0, b, rb, 0)),
            pl.BlockSpec((lz, rows, strip), lvl),
            pl.BlockSpec((lz, rows, strip), lambda b: (b, 0, cb)),
            pl.BlockSpec((lz, rows, strip), lvl),
            pl.BlockSpec((lz, rows, strip), lambda b: (b, 0, cb)),
            pl.BlockSpec((None, lz, rows, strip), lambda b: (1, b, 0, 0)),
            pl.BlockSpec((None, lz, rows, strip), lambda b: (1, b, 0, cb)),
        ],
        out_specs=[pl.BlockSpec((9, levels, cols), lambda b: (0, 0, 0)), pl.BlockSpec((10, levels, cols), lambda b: (0, 0, 0))]
        + [pl.BlockSpec((lz, rows, 9), lvl), pl.BlockSpec((lz, rows, 10), lvl)]
        + [pl.BlockSpec((lz, 4, 4), lvl)] * 4,
        out_shape=[jax.ShapeDtypeStruct((9, levels, cols), jnp.float32), jax.ShapeDtypeStruct((10, levels, cols), jnp.float32)]
        + [jax.ShapeDtypeStruct((levels, rows, 9), jnp.float32), jax.ShapeDtypeStruct((levels, rows, 10), jnp.float32)]
        + [jax.ShapeDtypeStruct((levels, 4, 4), jnp.float32)] * 4,
        compiler_params=pltpu.CompilerParams(dimension_semantics=("arbitrary",)),
    )
    xf, xl, yf, yl, cpp, cpm, cmp_, cmm = pack(
        press_bar, press_bar, theta_bar, theta_bar, winds, winds,
        press_bar, press_bar, theta_bar, theta_bar, winds, winds,
    )
    f4 = jnp.stack(
        [urban_frac, urban_class.astype(jnp.float32), height_bin.astype(jnp.float32), canopy_layers.astype(jnp.float32)]
    )
    small = jnp.concatenate([theta[:kc], f4], axis=0)
    n_small = small.shape[0]
    n_items = n_small * 3

    def item_rows(sel):
        e = small[:, sel, :].reshape(n_items, cols)
        return jnp.pad(e, ((0, levels - n_items), (0, 0)))[None]

    def item_cols(sel):
        e = jnp.swapaxes(small[:, :, sel], 1, 2).reshape(n_items, rows)
        return jnp.pad(e, ((0, levels - n_items), (0, 0)))[:, :, None]

    xn = from_side(jnp.concatenate([xf, item_rows(slice(0, 3))], axis=0), "gx", 1)
    xp = from_side(jnp.concatenate([xl, item_rows(slice(rows - 3, rows))], axis=0), "gx", -1)

    def corner_block(sel, width):
        c = jnp.concatenate([xn[0:4, :, sel], xp[0:4, :, sel]], axis=0)
        c = jnp.swapaxes(c, 0, 1)
        return jnp.pad(c, ((0, 0), (0, 0), (0, width - 4)))

    yfe = jnp.concatenate([yf, item_cols(slice(0, 3))], axis=2)
    yle = jnp.concatenate([yl, item_cols(slice(cols - 3, cols))], axis=2)
    yfe = jnp.concatenate([yfe, corner_block(slice(0, 4), yfe.shape[2])], axis=1)
    yle = jnp.concatenate([yle, corner_block(slice(cols - 4, cols), yle.shape[2])], axis=1)
    yn = from_side(yfe, "gy", 1)
    yp = from_side(yle, "gy", -1)
    x8n = xn[9, :n_items].reshape(n_small, 3, cols)
    x8p = xp[10, :n_items].reshape(n_small, 3, cols)
    y8n = jnp.swapaxes(yn[:n_items, :rows, 9].reshape(n_small, 3, rows), 1, 2)
    y8p = jnp.swapaxes(yp[:n_items, :rows, 10].reshape(n_small, 3, rows), 1, 2)

    ix = lax.axis_index("gx")
    iy = lax.axis_index("gy")
    nx, ny = lax.axis_size("gx"), lax.axis_size("gy")
    r = jnp.arange(rext, dtype=jnp.int32)[:, None]
    cc = jnp.arange(cext, dtype=jnp.int32)[None, :]
    row_ok = (r < rows) | ((r < rows + 4) & (ix < nx - 1)) | ((r >= rext - 4) & (ix > 0))
    col_ok = (cc < cols) | ((cc < cols + 4) & (iy < ny - 1)) | ((cc >= cext - 4) & (iy > 0))
    mask = (row_ok & col_ok).astype(jnp.float32)
    bp8 = bin_profile[:, :kc].reshape(-1)

    zero1 = jnp.zeros((1,), jnp.float32)
    lower = jnp.concatenate([zero1, -sound_coef[:-1]])
    upper = jnp.concatenate([-sound_coef[1:], zero1])
    middle = 1.0 + 2.0 * sound_coef

    ph0 = lambda p, b: (jnp.where(p == 0, b, nblk - 1), 0, 0)
    ph2 = lambda p, b: (jnp.where(p == 2, b, 0), 0, 0)
    ph02 = lambda p, b: (jnp.where(p == 1, nblk - 1, b), 0, 0)
    const3 = lambda p, b: (0, 0, 0)
    const2 = lambda p, b: (0, 0)
    smem = pl.BlockSpec(memory_space=pltpu.SMEM)
    in_specs = [
        smem, smem, smem, smem, smem,
        pl.BlockSpec((lz, rows, cols), ph0),
        pl.BlockSpec((lz, rows, cols), ph2),
        pl.BlockSpec((None, lz, rows, cols), lambda p, b: (0, jnp.where(p == 2, b, 0), 0, 0)),
        pl.BlockSpec((None, lz, rows, cols), lambda p, b: (1, jnp.where(p == 2, b, 0), 0, 0)),
        pl.BlockSpec((10, levels, cols), const3),
        pl.BlockSpec((11, levels, cols), const3),
        pl.BlockSpec((lz, rext, 10), ph02),
        pl.BlockSpec((lz, rext, 11), ph02),
        pl.BlockSpec((kc, rows, cols), const3),
        pl.BlockSpec((n_small, 3, cols), const3),
        pl.BlockSpec((n_small, 3, cols), const3),
        pl.BlockSpec((n_small, rows, 3), const3),
        pl.BlockSpec((n_small, rows, 3), const3),
        pl.BlockSpec((4, rows, cols), const3),
        pl.BlockSpec((rows, cols), const2),
        pl.BlockSpec((rext, cext), const2),
    ]
    out_specs = [
        pl.BlockSpec((lz, rows, cols), ph2),
        pl.BlockSpec((lz, rows, cols), ph2),
        pl.BlockSpec((rows, cols), const2),
        pl.BlockSpec((rows, cols), const2),
    ]
    out_shape = [
        jax.ShapeDtypeStruct((levels, rows, cols), jnp.float32),
        jax.ShapeDtypeStruct((levels, rows, cols), jnp.float32),
        jax.ShapeDtypeStruct((rows, cols), jnp.float32),
        jax.ShapeDtypeStruct((rows, cols), jnp.float32),
    ]
    scratch = [
        pltpu.VMEM((levels, rext, cext), jnp.float32),
        pltpu.VMEM((levels, rext, cext), jnp.float32),
        pltpu.VMEM((rext, cext), jnp.float32),
        pltpu.VMEM((rext, cext), jnp.float32),
        pltpu.VMEM((1, cext), jnp.float32),
        pltpu.VMEM((levels, 1, cext), jnp.float32),
        pltpu.VMEM((levels, 1, cext), jnp.float32),
    ]
    call = pl.pallas_call(
        kernel,
        grid=(3, nblk),
        in_specs=in_specs,
        out_specs=out_specs,
        out_shape=out_shape,
        scratch_shapes=scratch,
        compiler_params=pltpu.CompilerParams(
            dimension_semantics=("arbitrary", "arbitrary"),
            vmem_limit_bytes=56 * 1024 * 1024,
        ),
    )
    tg, pg, fg, wg = call(
        lower, middle, upper, bp8, class_drag,
        press_bar, theta_bar, winds, winds, xn, xp, yn, yp,
        theta, x8n, x8p, y8n, y8p, f4, wall_temp, mask,
    )
    return tg, pg, fg, wg


def extend_xla(main, rows, cols, corner):
    levels = main.shape[0]
    if corner is None:
        corner = jnp.zeros((levels, rows.shape[1], cols.shape[2]), main.dtype)
    return jnp.concatenate(
        [jnp.concatenate([main, rows], axis=1), jnp.concatenate([cols, corner], axis=1)], axis=2
    )


def solution(mesh):
    in_specs = (
        P(None, "gx", "gy"),
        P(None, None, "gx", "gy"),
        P(None, "gx", "gy"),
        P(None, "gx", "gy"),
        P("gx", "gy"),
        P("gx", "gy"),
        P("gx", "gy"),
        P("gx", "gy"),
        P("gx", "gy"),
        P(),
        P(),
        P(),
    )
    out_specs = (P(None, "gx", "gy"), P(None, "gx", "gy"), P("gx", "gy"), P("gx", "gy"))
    return jax.shard_map(
        per_device, mesh=mesh, in_specs=in_specs, out_specs=out_specs, check_vma=False
    )
```

```python
import functools

import jax
import jax.numpy as jnp
from jax import lax
from jax.experimental import pallas as pl
from jax.experimental.pallas import tpu as pltpu
from jax.sharding import PartitionSpec as P

courant = 0.3
diffusion = 0.1
buoyancy = 0.5
canopy_levels = 8
halo_rows = 8
strip = 128
block_levels = 20


def from_side(x, axis, delta):
    n = lax.axis_size(axis)
    if delta > 0:
        pairs = [(i + delta, i) for i in range(n - delta)]
    else:
        pairs = [(i, i - delta) for i in range(n + delta)]
    return lax.ppermute(x, axis, pairs)


def from_corner(x, dx, dy):
    nx, ny = lax.axis_size("gx"), lax.axis_size("gy")
    pairs = []
    for ix in range(nx):
        for iy in range(ny):
            sx, sy = ix + dx, iy + dy
            if 0 <= sx < nx and 0 <= sy < ny:
                pairs.append((sx * ny + sy, ix * ny + iy))
    return lax.ppermute(x, ("gx", "gy"), pairs)


def row_halo(f, lo, hi):
    levels, rows, cols = f.shape
    parts = []
    if hi:
        parts.append(from_side(f[:, :hi, :], "gx", 1))
    parts.append(jnp.zeros((levels, halo_rows - hi - lo, cols), f.dtype))
    if lo:
        parts.append(from_side(f[:, rows - lo :, :], "gx", -1))
    return jnp.concatenate(parts, axis=1)


def col_halo(f, lo, hi):
    levels, rows, cols = f.shape
    parts = []
    if hi:
        parts.append(from_side(f[:, :, :hi], "gy", 1))
    parts.append(jnp.zeros((levels, rows, strip - hi - lo), f.dtype))
    if lo:
        parts.append(from_side(f[:, :, cols - lo :], "gy", -1))
    return jnp.concatenate(parts, axis=2)


def corner_rows(f, w):
    levels, rows, cols = f.shape
    mid = jnp.zeros((levels, w, strip - 2 * w), f.dtype)
    gap = jnp.zeros((levels, halo_rows - 2 * w, strip), f.dtype)
    top = jnp.concatenate(
        [from_corner(f[:, :w, :w], 1, 1), mid, from_corner(f[:, :w, cols - w :], 1, -1)], axis=2
    )
    bottom = jnp.concatenate(
        [from_corner(f[:, rows - w :, :w], -1, 1), mid, from_corner(f[:, rows - w :, cols - w :], -1, -1)],
        axis=2,
    )
    return jnp.concatenate([top, gap, bottom], axis=1)


def ahead(x, k, axis):
    if k == 0:
        return x
    n = x.shape[axis]
    return pltpu.roll(x, (-k) % n, axis)


def forward_tend(f, u, axis):
    fm2, fm1, f0, f1, f2, f3 = [ahead(f, k, axis) for k in (-2, -1, 0, 1, 2, 3)]
    a_sum = (fm2 + f3) - 8.0 * (fm1 + f2) + 37.0 * (f0 + f1)
    b_sum = (fm2 - f3) - 5.0 * (fm1 - f2) + 10.0 * (f0 - f1)
    flux = (u * a_sum + jnp.abs(u) * b_sum) * (1.0 / 60.0)
    return -courant * (flux - ahead(flux, -1, axis))


def adjoint_tend(f, u, axis):
    g = courant * (ahead(f, 1, axis) - f)
    pu = u * g
    qu = jnp.abs(u) * g
    total = (
        ahead(pu + qu, 2, axis)
        + ahead(-8.0 * pu - 5.0 * qu, 1, axis)
        + (37.0 * pu + 10.0 * qu)
        + ahead(37.0 * pu - 10.0 * qu, -1, axis)
        + ahead(-8.0 * pu + 5.0 * qu, -2, axis)
        + ahead(pu - qu, -3, axis)
    )
    return total * (1.0 / 60.0)


def laplace(q):
    return ahead(q, 1, 0) + ahead(q, -1, 0) + ahead(q, 1, 1) + ahead(q, -1, 1) - 4.0 * q


def extend(main, rows, cols):
    return jnp.concatenate([jnp.concatenate([main, rows], axis=0), cols], axis=1)


def pack_rows_kernel(pbf, pbl, tbf, tbl, u0f, u0l, xf, xl):
    lz = pbf.shape[0]

    def body(j, c):
        k = pl.program_id(0) * lz + j
        xf[:, k, :] = jnp.concatenate([pbf[j][0:4], tbf[j][0:3], u0f[j][0:2]], axis=0)
        xl[:, k, :] = jnp.concatenate([pbl[j][4:8], tbl[j][5:8], u0l[j][5:8]], axis=0)
        return c

    lax.fori_loop(0, lz, body, 0)


def pack_cols_kernel(pcf, pcl, tcf, tcl, ucf, ucl, yf, yl):
    lz = pcf.shape[0]
    rows = pcf.shape[1]
    lane = lax.broadcasted_iota(jnp.int32, (rows, strip), 1)

    def body(j, c):
        a, b, u = pcf[j], tcf[j], ucf[j]
        first = jnp.where(lane < 4, a, jnp.where(lane < 7, pltpu.roll(b, 4, 1), pltpu.roll(u, 7, 1)))
        yf[j] = first[:, :9]
        a, b, u = pcl[j], tcl[j], ucl[j]
        last = jnp.where(
            lane < 4, pltpu.roll(a, 4, 1), jnp.where(lane < 7, pltpu.roll(b, 7, 1), pltpu.roll(u, 10, 1))
        )
        yl[j] = last[:, :10]
        return c

    lax.fori_loop(0, lz, body, 0)


def lane_strip(near, far, width):
    rows = near.shape[0]
    a = jnp.concatenate([near, jnp.zeros((rows, strip - width), jnp.float32)], axis=1)
    b = jnp.concatenate([far, jnp.zeros((rows, strip - width), jnp.float32)], axis=1)
    return a + pltpu.roll(b, strip - width, 1)


def kernel(
    lo_ref, mid_ref, up_ref, bp_ref, cd_ref,
    pbm, tbm, u0m, u1m, xn, xp, yn, yp,
    thm, x8n, x8p, y8n, y8p, f4, wall, mask,
    tg_out, pg_out, fg_out, wg_out,
    dd, qa, car_a, car_b, cpc, cp1, cq2,
):
    phase = pl.program_id(0)
    blk = pl.program_id(1)
    nblk = pl.num_programs(1)
    lz = pbm.shape[0]
    rows, cols = pbm.shape[1], pbm.shape[2]
    wide = cpc.shape[1]
    rext = yn.shape[1]
    lane = lax.broadcasted_iota(jnp.int32, (rext, strip), 1)

    def coef(ref, k):
        return jnp.full((1, wide), ref[k], jnp.float32)

    def ystrip(j, off, wn, wp):
        n = jnp.concatenate([yn[j], jnp.zeros((rext, strip - yn.shape[2]), jnp.float32)], axis=1)
        p = jnp.concatenate([yp[j], jnp.zeros((rext, strip - yp.shape[2]), jnp.float32)], axis=1)
        n = pltpu.roll(n, (strip - off) % strip, 1)
        p = pltpu.roll(p, strip - wp - off, 1)
        return jnp.where(lane < wn, n, jnp.where(lane >= strip - wp, p, 0.0))

    def press_ext(j, k):
        xr = jnp.concatenate([pbm[j], xn[:, k, :][0:4], xp[:, k, :][0:4]], axis=0)
        return jnp.concatenate([xr, ystrip(j, 0, 4, 4)], axis=1)

    @pl.when(phase == 0)
    def _():
        @pl.when(blk == 0)
        def _():
            car_a[...] = jnp.zeros(car_a.shape, jnp.float32)
            cpc[...] = jnp.zeros(cpc.shape, jnp.float32)

        def body(j, c):
            k = blk * lz + j
            ak = coef(lo_ref, k)
            r = 1.0 / (coef(mid_ref, k) - ak * cpc[...])
            cp = coef(up_ref, k) * r
            cpc[...] = cp
            cp1[k] = cp
            d = press_ext(j, k)
            dn = (d - ak * car_a[...]) * r
            car_a[...] = dn
            dd[k] = dn
            return c

        lax.fori_loop(0, lz, body, 0)

    @pl.when(phase == 1)
    def _():
        @pl.when(blk == 0)
        def _():
            car_a[...] = jnp.zeros(car_a.shape, jnp.float32)
            car_b[...] = jnp.zeros(car_b.shape, jnp.float32)
            cpc[...] = jnp.zeros(cpc.shape, jnp.float32)

        def body(j, c):
            k = (nblk - 1 - blk) * lz + (lz - 1 - j)
            x = dd[k] - cp1[k] * car_a[...]
            car_a[...] = x
            qa[k] = x
            pb1 = (x + diffusion * laplace(x)) * mask[...]
            ck = coef(up_ref, k)
            s = 1.0 / (coef(mid_ref, k) - ck * cpc[...])
            cq = coef(lo_ref, k) * s
            cpc[...] = cq
            cq2[k] = cq
            e = (pb1 - ck * car_b[...]) * s
            car_b[...] = e
            dd[k] = e
            return c

        lax.fori_loop(0, lz, body, 0)

    @pl.when(phase == 2)
    def _():
        @pl.when(blk == 0)
        def _():
            car_a[...] = jnp.zeros(car_a.shape, jnp.float32)

        def field_ext(i):
            xr = jnp.concatenate(
                [f4[i], x8n[8 + i], jnp.zeros((2, cols), jnp.float32), x8p[8 + i]], axis=0
            )
            ys = jnp.concatenate(
                [lane_strip(y8n[8 + i], y8p[8 + i], 3), jnp.zeros((halo_rows, strip), jnp.float32)], axis=0
            )
            return jnp.concatenate([xr, ys], axis=1)

        def level(j, canopy, acc):
            k = blk * lz + j
            qb = dd[k] - cq2[k] * car_a[...]
            car_a[...] = qb
            pg = qb + diffusion * laplace(qb)
            pg_out[j] = pg[:rows, :cols]
            xnj, xpj = xn[:, k, :], xp[:, k, :]
            tbx = jnp.concatenate([tbm[j], xnj[4:7], jnp.zeros((2, cols), jnp.float32), xpj[4:7]], axis=0)
            tby = ystrip(j, 4, 3, 3)
            th2b = jnp.concatenate([tbx, tby], axis=1) + buoyancy * (qa[k] + qb)
            if canopy:
                ud, cls, hb, lay = acc[2]
                prof = jnp.zeros(hb.shape, jnp.float32)
                for bb in range(bp_ref.shape[0] // canopy_levels):
                    prof = jnp.where(hb == float(bb), bp_ref[bb * canopy_levels + j], prof)
                act = jnp.where(lay > j.astype(jnp.float32), 1.0, 0.0)
                am = ud * prof * act
                th1b = (1.0 - am) * th2b
            else:
                th1b = th2b
            u0e = jnp.concatenate([u0m[j], xnj[7:9], jnp.zeros((3, cols), jnp.float32), xpj[7:10]], axis=0)
            u1e = jnp.concatenate([u1m[j], ystrip(j, 7, 2, 3)[:rows]], axis=1)
            adv = adjoint_tend(th1b[:, :cols], u0e, 0)[:rows, :] + adjoint_tend(th1b[:rows, :], u1e, 1)[:, :cols]
            tg_out[j] = th1b[:rows, :cols] + adv
            if canopy:
                th = thm[j]
                thx = jnp.concatenate([th, x8n[j], jnp.zeros((2, cols), jnp.float32), x8p[j]], axis=0)
                thy = jnp.concatenate([th, lane_strip(y8n[j], y8p[j], 3)], axis=1)
                fx = forward_tend(thx, u0e, 0)[:rows, :]
                fy = forward_tend(thy, u1e, 1)[:, :cols]
                first = th + (fx + fy)
                sb = th2b[:rows, :cols]
                fg, wg, fields, drag = acc
                dpa = drag * prof[:rows, :cols] * act[:rows, :cols]
                fg = fg + dpa * (wall[...] - first) * sb
                wg = wg + am[:rows, :cols] * sb
                acc = (fg, wg, fields, drag)
            return acc

        @pl.when(blk == 0)
        def _():
            zero = jnp.zeros((rows, cols), jnp.float32)
            cls = field_ext(1)
            drag = jnp.zeros(cls.shape, jnp.float32)
            for c in range(cd_ref.shape[0]):
                drag = jnp.where(cls == float(c), cd_ref[c], drag)
            ud = field_ext(0) * drag
            fields = (ud, cls, field_ext(2), field_ext(3))
            fg, wg, _, _ = lax.fori_loop(
                0, canopy_levels, lambda j, a: level(j, True, a), (zero, zero, fields, drag[:rows, :cols])
            )
            fg_out[...] = fg
            wg_out[...] = wg
            lax.fori_loop(canopy_levels, lz, lambda j, a: level(j, False, a), 0)

        @pl.when(blk > 0)
        def _():
            lax.fori_loop(0, lz, lambda j, a: level(j, False, a), 0)


def per_device(
    theta, winds, theta_bar, press_bar, urban_frac, wall_temp, urban_class, canopy_layers,
    height_bin, class_drag, bin_profile, sound_coef,
):
    levels, rows, cols = theta.shape
    rext, cext = rows + halo_rows, cols + strip
    lz = block_levels
    nblk = levels // lz
    kc = canopy_levels
    rb, cb = rows // 8 - 1, cols // strip - 1

    lvl = lambda b: (b, 0, 0)
    pack_rows = pl.pallas_call(
        pack_rows_kernel,
        grid=(nblk,),
        in_specs=[
            pl.BlockSpec((lz, 8, cols), lvl),
            pl.BlockSpec((lz, 8, cols), lambda b: (b, rb, 0)),
            pl.BlockSpec((lz, 8, cols), lvl),
            pl.BlockSpec((lz, 8, cols), lambda b: (b, rb, 0)),
            pl.BlockSpec((None, lz, 8, cols), lambda b: (0, b, 0, 0)),
            pl.BlockSpec((None, lz, 8, cols), lambda b: (0, b, rb, 0)),
        ],
        out_specs=[pl.BlockSpec((9, levels, cols), lambda b: (0, 0, 0)), pl.BlockSpec((10, levels, cols), lambda b: (0, 0, 0))],
        out_shape=[jax.ShapeDtypeStruct((9, levels, cols), jnp.float32), jax.ShapeDtypeStruct((10, levels, cols), jnp.float32)],
        compiler_params=pltpu.CompilerParams(dimension_semantics=("arbitrary",)),
    )
    pack_cols = pl.pallas_call(
        pack_cols_kernel,
        grid=(nblk,),
        in_specs=[
            pl.BlockSpec((lz, rows, strip), lvl),
            pl.BlockSpec((lz, rows, strip), lambda b: (b, 0, cb)),
            pl.BlockSpec((lz, rows, strip), lvl),
            pl.BlockSpec((lz, rows, strip), lambda b: (b, 0, cb)),
            pl.BlockSpec((None, lz, rows, strip), lambda b: (1, b, 0, 0)),
            pl.BlockSpec((None, lz, rows, strip), lambda b: (1, b, 0, cb)),
        ],
        out_specs=[pl.BlockSpec((lz, rows, 9), lvl), pl.BlockSpec((lz, rows, 10), lvl)],
        out_shape=[jax.ShapeDtypeStruct((levels, rows, 9), jnp.float32), jax.ShapeDtypeStruct((levels, rows, 10), jnp.float32)],
        compiler_params=pltpu.CompilerParams(dimension_semantics=("arbitrary",)),
    )
    xf, xl = pack_rows(press_bar, press_bar, theta_bar, theta_bar, winds, winds)
    yf, yl = pack_cols(press_bar, press_bar, theta_bar, theta_bar, winds, winds)

    f4 = jnp.stack(
        [urban_frac, urban_class.astype(jnp.float32), height_bin.astype(jnp.float32), canopy_layers.astype(jnp.float32)]
    )
    small = jnp.concatenate([theta[:kc], f4], axis=0)
    n_small = small.shape[0]
    n_items = n_small * 3

    def item_rows(sel):
        e = small[:, sel, :].reshape(n_items, cols)
        return jnp.pad(e, ((0, levels - n_items), (0, 0)))[None]

    def item_cols(sel):
        e = jnp.swapaxes(small[:, :, sel], 1, 2).reshape(n_items, rows)
        return jnp.pad(e, ((0, levels - n_items), (0, 0)))[:, :, None]

    xn = from_side(jnp.concatenate([xf, item_rows(slice(0, 3))], axis=0), "gx", 1)
    xp = from_side(jnp.concatenate([xl, item_rows(slice(rows - 3, rows))], axis=0), "gx", -1)

    def corner_block(sel, width):
        c = jnp.concatenate([xn[0:4, :, sel], xp[0:4, :, sel]], axis=0)
        c = jnp.swapaxes(c, 0, 1)
        return jnp.pad(c, ((0, 0), (0, 0), (0, width - 4)))

    yfe = jnp.concatenate([yf, item_cols(slice(0, 3))], axis=2)
    yle = jnp.concatenate([yl, item_cols(slice(cols - 3, cols))], axis=2)
    yfe = jnp.concatenate([yfe, corner_block(slice(0, 4), yfe.shape[2])], axis=1)
    yle = jnp.concatenate([yle, corner_block(slice(cols - 4, cols), yle.shape[2])], axis=1)
    yn = from_side(yfe, "gy", 1)
    yp = from_side(yle, "gy", -1)
    x8n = xn[9, :n_items].reshape(n_small, 3, cols)
    x8p = xp[10, :n_items].reshape(n_small, 3, cols)
    y8n = jnp.swapaxes(yn[:n_items, :rows, 9].reshape(n_small, 3, rows), 1, 2)
    y8p = jnp.swapaxes(yp[:n_items, :rows, 10].reshape(n_small, 3, rows), 1, 2)

    ix = lax.axis_index("gx")
    iy = lax.axis_index("gy")
    nx, ny = lax.axis_size("gx"), lax.axis_size("gy")
    r = jnp.arange(rext, dtype=jnp.int32)[:, None]
    cc = jnp.arange(cext, dtype=jnp.int32)[None, :]
    row_ok = (r < rows) | ((r < rows + 4) & (ix < nx - 1)) | ((r >= rext - 4) & (ix > 0))
    col_ok = (cc < cols) | ((cc < cols + 4) & (iy < ny - 1)) | ((cc >= cext - 4) & (iy > 0))
    mask = (row_ok & col_ok).astype(jnp.float32)
    bp8 = bin_profile[:, :kc].reshape(-1)

    zero1 = jnp.zeros((1,), jnp.float32)
    lower = jnp.concatenate([zero1, -sound_coef[:-1]])
    upper = jnp.concatenate([-sound_coef[1:], zero1])
    middle = 1.0 + 2.0 * sound_coef

    ph0 = lambda p, b: (jnp.where(p == 0, b, nblk - 1), 0, 0)
    ph2 = lambda p, b: (jnp.where(p == 2, b, 0), 0, 0)
    ph02 = lambda p, b: (jnp.where(p == 1, nblk - 1, b), 0, 0)
    const3 = lambda p, b: (0, 0, 0)
    const2 = lambda p, b: (0, 0)
    smem = pl.BlockSpec(memory_space=pltpu.SMEM)
    in_specs = [
        smem, smem, smem, smem, smem,
        pl.BlockSpec((lz, rows, cols), ph0),
        pl.BlockSpec((lz, rows, cols), ph2),
        pl.BlockSpec((None, lz, rows, cols), lambda p, b: (0, jnp.where(p == 2, b, 0), 0, 0)),
        pl.BlockSpec((None, lz, rows, cols), lambda p, b: (1, jnp.where(p == 2, b, 0), 0, 0)),
        pl.BlockSpec((10, levels, cols), const3),
        pl.BlockSpec((11, levels, cols), const3),
        pl.BlockSpec((lz, rext, 10), ph02),
        pl.BlockSpec((lz, rext, 11), ph02),
        pl.BlockSpec((kc, rows, cols), const3),
        pl.BlockSpec((n_small, 3, cols), const3),
        pl.BlockSpec((n_small, 3, cols), const3),
        pl.BlockSpec((n_small, rows, 3), const3),
        pl.BlockSpec((n_small, rows, 3), const3),
        pl.BlockSpec((4, rows, cols), const3),
        pl.BlockSpec((rows, cols), const2),
        pl.BlockSpec((rext, cext), const2),
    ]
    out_specs = [
        pl.BlockSpec((lz, rows, cols), ph2),
        pl.BlockSpec((lz, rows, cols), ph2),
        pl.BlockSpec((rows, cols), const2),
        pl.BlockSpec((rows, cols), const2),
    ]
    out_shape = [
        jax.ShapeDtypeStruct((levels, rows, cols), jnp.float32),
        jax.ShapeDtypeStruct((levels, rows, cols), jnp.float32),
        jax.ShapeDtypeStruct((rows, cols), jnp.float32),
        jax.ShapeDtypeStruct((rows, cols), jnp.float32),
    ]
    scratch = [
        pltpu.VMEM((levels, rext, cext), jnp.float32),
        pltpu.VMEM((levels, rext, cext), jnp.float32),
        pltpu.VMEM((rext, cext), jnp.float32),
        pltpu.VMEM((rext, cext), jnp.float32),
        pltpu.VMEM((1, cext), jnp.float32),
        pltpu.VMEM((levels, 1, cext), jnp.float32),
        pltpu.VMEM((levels, 1, cext), jnp.float32),
    ]
    call = pl.pallas_call(
        kernel,
        grid=(3, nblk),
        in_specs=in_specs,
        out_specs=out_specs,
        out_shape=out_shape,
        scratch_shapes=scratch,
        compiler_params=pltpu.CompilerParams(
            dimension_semantics=("arbitrary", "arbitrary"),
            vmem_limit_bytes=56 * 1024 * 1024,
        ),
    )
    tg, pg, fg, wg = call(
        lower, middle, upper, bp8, class_drag,
        press_bar, theta_bar, winds, winds, xn, xp, yn, yp,
        theta, x8n, x8p, y8n, y8p, f4, wall_temp, mask,
    )
    return tg, pg, fg, wg


def extend_xla(main, rows, cols, corner):
    levels = main.shape[0]
    if corner is None:
        corner = jnp.zeros((levels, rows.shape[1], cols.shape[2]), main.dtype)
    return jnp.concatenate(
        [jnp.concatenate([main, rows], axis=1), jnp.concatenate([cols, corner], axis=1)], axis=2
    )


def solution(mesh):
    in_specs = (
        P(None, "gx", "gy"),
        P(None, None, "gx", "gy"),
        P(None, "gx", "gy"),
        P(None, "gx", "gy"),
        P("gx", "gy"),
        P("gx", "gy"),
        P("gx", "gy"),
        P("gx", "gy"),
        P("gx", "gy"),
        P(),
        P(),
        P(),
    )
    out_specs = (P(None, "gx", "gy"), P(None, "gx", "gy"), P("gx", "gy"), P("gx", "gy"))
    return jax.shard_map(
        per_device, mesh=mesh, in_specs=in_specs, out_specs=out_specs, check_vma=False
    )
```

```python
import functools

import jax
import jax.numpy as jnp
from jax import lax
from jax.experimental import pallas as pl
from jax.experimental.pallas import tpu as pltpu
from jax.sharding import PartitionSpec as P

courant = 0.3
diffusion = 0.1
buoyancy = 0.5
canopy_levels = 8
halo_rows = 8
strip = 128
block_levels = 20
pack_levels = 6


def from_side(x, axis, delta):
    n = lax.axis_size(axis)
    if delta > 0:
        pairs = [(i + delta, i) for i in range(n - delta)]
    else:
        pairs = [(i, i - delta) for i in range(n + delta)]
    return lax.ppermute(x, axis, pairs)


def from_corner(x, dx, dy):
    nx, ny = lax.axis_size("gx"), lax.axis_size("gy")
    pairs = []
    for ix in range(nx):
        for iy in range(ny):
            sx, sy = ix + dx, iy + dy
            if 0 <= sx < nx and 0 <= sy < ny:
                pairs.append((sx * ny + sy, ix * ny + iy))
    return lax.ppermute(x, ("gx", "gy"), pairs)


def row_halo(f, lo, hi):
    levels, rows, cols = f.shape
    parts = []
    if hi:
        parts.append(from_side(f[:, :hi, :], "gx", 1))
    parts.append(jnp.zeros((levels, halo_rows - hi - lo, cols), f.dtype))
    if lo:
        parts.append(from_side(f[:, rows - lo :, :], "gx", -1))
    return jnp.concatenate(parts, axis=1)


def col_halo(f, lo, hi):
    levels, rows, cols = f.shape
    parts = []
    if hi:
        parts.append(from_side(f[:, :, :hi], "gy", 1))
    parts.append(jnp.zeros((levels, rows, strip - hi - lo), f.dtype))
    if lo:
        parts.append(from_side(f[:, :, cols - lo :], "gy", -1))
    return jnp.concatenate(parts, axis=2)


def corner_rows(f, w):
    levels, rows, cols = f.shape
    mid = jnp.zeros((levels, w, strip - 2 * w), f.dtype)
    gap = jnp.zeros((levels, halo_rows - 2 * w, strip), f.dtype)
    top = jnp.concatenate(
        [from_corner(f[:, :w, :w], 1, 1), mid, from_corner(f[:, :w, cols - w :], 1, -1)], axis=2
    )
    bottom = jnp.concatenate(
        [from_corner(f[:, rows - w :, :w], -1, 1), mid, from_corner(f[:, rows - w :, cols - w :], -1, -1)],
        axis=2,
    )
    return jnp.concatenate([top, gap, bottom], axis=1)


def ahead(x, k, axis):
    if k == 0:
        return x
    n = x.shape[axis]
    return pltpu.roll(x, (-k) % n, axis)


def forward_tend(f, u, axis):
    fm2, fm1, f0, f1, f2, f3 = [ahead(f, k, axis) for k in (-2, -1, 0, 1, 2, 3)]
    a_sum = (fm2 + f3) - 8.0 * (fm1 + f2) + 37.0 * (f0 + f1)
    b_sum = (fm2 - f3) - 5.0 * (fm1 - f2) + 10.0 * (f0 - f1)
    flux = (u * a_sum + jnp.abs(u) * b_sum) * (1.0 / 60.0)
    return -courant * (flux - ahead(flux, -1, axis))


def adjoint_tend(f, u, axis):
    g = courant * (ahead(f, 1, axis) - f)
    pu = u * g
    qu = jnp.abs(u) * g
    total = (
        ahead(pu + qu, 2, axis)
        + ahead(-8.0 * pu - 5.0 * qu, 1, axis)
        + (37.0 * pu + 10.0 * qu)
        + ahead(37.0 * pu - 10.0 * qu, -1, axis)
        + ahead(-8.0 * pu + 5.0 * qu, -2, axis)
        + ahead(pu - qu, -3, axis)
    )
    return total * (1.0 / 60.0)


def laplace(q):
    return ahead(q, 1, 0) + ahead(q, -1, 0) + ahead(q, 1, 1) + ahead(q, -1, 1) - 4.0 * q


def extend(main, rows, cols):
    return jnp.concatenate([jnp.concatenate([main, rows], axis=0), cols], axis=1)


def pack_rows_kernel(pbf, pbl, tbf, tbl, u0f, u0l, xf, xl):
    lz = pbf.shape[0]

    def body(j, c):
        k = pl.program_id(0) * lz + j
        xf[:, k, :] = jnp.concatenate([pbf[j][0:4], tbf[j][0:3], u0f[j][0:2]], axis=0)
        xl[:, k, :] = jnp.concatenate([pbl[j][4:8], tbl[j][5:8], u0l[j][5:8]], axis=0)
        return c

    lax.fori_loop(0, lz, body, 0)


def pack_cols_kernel(pcf, pcl, tcf, tcl, ucf, ucl, yf, yl):
    lz = pcf.shape[0]
    rows = pcf.shape[1]
    lane = lax.broadcasted_iota(jnp.int32, (rows, strip), 1)

    def body(j, c):
        a, b, u = pcf[j], tcf[j], ucf[j]
        first = jnp.where(lane < 4, a, jnp.where(lane < 7, pltpu.roll(b, 4, 1), pltpu.roll(u, 7, 1)))
        yf[j] = first[:, :9]
        a, b, u = pcl[j], tcl[j], ucl[j]
        last = jnp.where(
            lane < 4, pltpu.roll(a, 4, 1), jnp.where(lane < 7, pltpu.roll(b, 7, 1), pltpu.roll(u, 10, 1))
        )
        yl[j] = last[:, :10]
        return c

    lax.fori_loop(0, lz, body, 0)


def lane_strip(near, far, width):
    rows = near.shape[0]
    a = jnp.concatenate([near, jnp.zeros((rows, strip - width), jnp.float32)], axis=1)
    b = jnp.concatenate([far, jnp.zeros((rows, strip - width), jnp.float32)], axis=1)
    return a + pltpu.roll(b, strip - width, 1)


def kernel(
    lo_ref, mid_ref, up_ref, bp_ref, cd_ref,
    pbm, tbm, u0m, u1m, xn, xp, yn, yp,
    thm, x8n, x8p, y8n, y8p, f4, wall, mask,
    tg_out, pg_out, fg_out, wg_out,
    dd, qa, car_a, car_b, cpc, cp1, cq2,
):
    phase = pl.program_id(0)
    blk = pl.program_id(1)
    nblk = pl.num_programs(1)
    lz = pbm.shape[0]
    rows, cols = pbm.shape[1], pbm.shape[2]
    wide = cpc.shape[1]
    rext = yn.shape[1]
    lane = lax.broadcasted_iota(jnp.int32, (rext, strip), 1)

    def coef(ref, k):
        return jnp.full((1, wide), ref[k], jnp.float32)

    def ystrip(j, off, wn, wp):
        n = jnp.concatenate([yn[j], jnp.zeros((rext, strip - yn.shape[2]), jnp.float32)], axis=1)
        p = jnp.concatenate([yp[j], jnp.zeros((rext, strip - yp.shape[2]), jnp.float32)], axis=1)
        n = pltpu.roll(n, (strip - off) % strip, 1)
        p = pltpu.roll(p, strip - wp - off, 1)
        return jnp.where(lane < wn, n, jnp.where(lane >= strip - wp, p, 0.0))

    def press_ext(j, k):
        xr = jnp.concatenate([pbm[j], xn[:, k, :][0:4], xp[:, k, :][0:4]], axis=0)
        return jnp.concatenate([xr, ystrip(j, 0, 4, 4)], axis=1)

    @pl.when(phase == 0)
    def _():
        @pl.when(blk == 0)
        def _():
            car_a[...] = jnp.zeros(car_a.shape, jnp.float32)
            cpc[...] = jnp.zeros(cpc.shape, jnp.float32)

        def body(j, c):
            k = blk * lz + j
            ak = coef(lo_ref, k)
            r = 1.0 / (coef(mid_ref, k) - ak * cpc[...])
            cp = coef(up_ref, k) * r
            cpc[...] = cp
            cp1[k] = cp
            d = press_ext(j, k)
            dn = (d - ak * car_a[...]) * r
            car_a[...] = dn
            dd[k] = dn
            return c

        lax.fori_loop(0, lz, body, 0)

    @pl.when(phase == 1)
    def _():
        @pl.when(blk == 0)
        def _():
            car_a[...] = jnp.zeros(car_a.shape, jnp.float32)
            car_b[...] = jnp.zeros(car_b.shape, jnp.float32)
            cpc[...] = jnp.zeros(cpc.shape, jnp.float32)

        def body(j, c):
            k = (nblk - 1 - blk) * lz + (lz - 1 - j)
            x = dd[k] - cp1[k] * car_a[...]
            car_a[...] = x
            qa[k] = x
            pb1 = (x + diffusion * laplace(x)) * mask[...]
            ck = coef(up_ref, k)
            s = 1.0 / (coef(mid_ref, k) - ck * cpc[...])
            cq = coef(lo_ref, k) * s
            cpc[...] = cq
            cq2[k] = cq
            e = (pb1 - ck * car_b[...]) * s
            car_b[...] = e
            dd[k] = e
            return c

        lax.fori_loop(0, lz, body, 0)

    @pl.when(phase == 2)
    def _():
        @pl.when(blk == 0)
        def _():
            car_a[...] = jnp.zeros(car_a.shape, jnp.float32)

        def field_ext(i):
            xr = jnp.concatenate(
                [f4[i], x8n[8 + i], jnp.zeros((2, cols), jnp.float32), x8p[8 + i]], axis=0
            )
            ys = jnp.concatenate(
                [lane_strip(y8n[8 + i], y8p[8 + i], 3), jnp.zeros((halo_rows, strip), jnp.float32)], axis=0
            )
            return jnp.concatenate([xr, ys], axis=1)

        def level(j, canopy, acc):
            k = blk * lz + j
            qb = dd[k] - cq2[k] * car_a[...]
            car_a[...] = qb
            pg = qb + diffusion * laplace(qb)
            pg_out[j] = pg[:rows, :cols]
            xnj, xpj = xn[:, k, :], xp[:, k, :]
            tbx = jnp.concatenate([tbm[j], xnj[4:7], jnp.zeros((2, cols), jnp.float32), xpj[4:7]], axis=0)
            tby = ystrip(j, 4, 3, 3)
            th2b = jnp.concatenate([tbx, tby], axis=1) + buoyancy * (qa[k] + qb)
            if canopy:
                ud, cls, hb, lay = acc[2]
                prof = jnp.zeros(hb.shape, jnp.float32)
                for bb in range(bp_ref.shape[0] // canopy_levels):
                    prof = jnp.where(hb == float(bb), bp_ref[bb * canopy_levels + j], prof)
                act = jnp.where(lay > j.astype(jnp.float32), 1.0, 0.0)
                am = ud * prof * act
                th1b = (1.0 - am) * th2b
            else:
                th1b = th2b
            u0e = jnp.concatenate([u0m[j], xnj[7:9], jnp.zeros((3, cols), jnp.float32), xpj[7:10]], axis=0)
            u1e = jnp.concatenate([u1m[j], ystrip(j, 7, 2, 3)[:rows]], axis=1)
            adv = adjoint_tend(th1b[:, :cols], u0e, 0)[:rows, :] + adjoint_tend(th1b[:rows, :], u1e, 1)[:, :cols]
            tg_out[j] = th1b[:rows, :cols] + adv
            if canopy:
                th = thm[j]
                thx = jnp.concatenate([th, x8n[j], jnp.zeros((2, cols), jnp.float32), x8p[j]], axis=0)
                thy = jnp.concatenate([th, lane_strip(y8n[j], y8p[j], 3)], axis=1)
                fx = forward_tend(thx, u0e, 0)[:rows, :]
                fy = forward_tend(thy, u1e, 1)[:, :cols]
                first = th + (fx + fy)
                sb = th2b[:rows, :cols]
                fg, wg, fields, drag = acc
                dpa = drag * prof[:rows, :cols] * act[:rows, :cols]
                fg = fg + dpa * (wall[...] - first) * sb
                wg = wg + am[:rows, :cols] * sb
                acc = (fg, wg, fields, drag)
            return acc

        @pl.when(blk == 0)
        def _():
            zero = jnp.zeros((rows, cols), jnp.float32)
            cls = field_ext(1)
            drag = jnp.zeros(cls.shape, jnp.float32)
            for c in range(cd_ref.shape[0]):
                drag = jnp.where(cls == float(c), cd_ref[c], drag)
            ud = field_ext(0) * drag
            fields = (ud, cls, field_ext(2), field_ext(3))
            fg, wg, _, _ = lax.fori_loop(
                0, canopy_levels, lambda j, a: level(j, True, a), (zero, zero, fields, drag[:rows, :cols])
            )
            fg_out[...] = fg
            wg_out[...] = wg
            lax.fori_loop(canopy_levels, lz, lambda j, a: level(j, False, a), 0)

        @pl.when(blk > 0)
        def _():
            lax.fori_loop(0, lz, lambda j, a: level(j, False, a), 0)


def per_device(
    theta, winds, theta_bar, press_bar, urban_frac, wall_temp, urban_class, canopy_layers,
    height_bin, class_drag, bin_profile, sound_coef,
):
    levels, rows, cols = theta.shape
    rext, cext = rows + halo_rows, cols + strip
    lz = block_levels
    nblk = levels // lz
    kc = canopy_levels
    rb, cb = rows // 8 - 1, cols // strip - 1

    lvl = lambda b: (b, 0, 0)
    lz, nblk_main = pack_levels, nblk
    nblk = levels // lz
    pack_rows = pl.pallas_call(
        pack_rows_kernel,
        grid=(nblk,),
        in_specs=[
            pl.BlockSpec((lz, 8, cols), lvl),
            pl.BlockSpec((lz, 8, cols), lambda b: (b, rb, 0)),
            pl.BlockSpec((lz, 8, cols), lvl),
            pl.BlockSpec((lz, 8, cols), lambda b: (b, rb, 0)),
            pl.BlockSpec((None, lz, 8, cols), lambda b: (0, b, 0, 0)),
            pl.BlockSpec((None, lz, 8, cols), lambda b: (0, b, rb, 0)),
        ],
        out_specs=[pl.BlockSpec((9, levels, cols), lambda b: (0, 0, 0)), pl.BlockSpec((10, levels, cols), lambda b: (0, 0, 0))],
        out_shape=[jax.ShapeDtypeStruct((9, levels, cols), jnp.float32), jax.ShapeDtypeStruct((10, levels, cols), jnp.float32)],
        compiler_params=pltpu.CompilerParams(dimension_semantics=("arbitrary",)),
    )
    pack_cols = pl.pallas_call(
        pack_cols_kernel,
        grid=(nblk,),
        in_specs=[
            pl.BlockSpec((lz, rows, strip), lvl),
            pl.BlockSpec((lz, rows, strip), lambda b: (b, 0, cb)),
            pl.BlockSpec((lz, rows, strip), lvl),
            pl.BlockSpec((lz, rows, strip), lambda b: (b, 0, cb)),
            pl.BlockSpec((None, lz, rows, strip), lambda b: (1, b, 0, 0)),
            pl.BlockSpec((None, lz, rows, strip), lambda b: (1, b, 0, cb)),
        ],
        out_specs=[pl.BlockSpec((lz, rows, 9), lvl), pl.BlockSpec((lz, rows, 10), lvl)],
        out_shape=[jax.ShapeDtypeStruct((levels, rows, 9), jnp.float32), jax.ShapeDtypeStruct((levels, rows, 10), jnp.float32)],
        compiler_params=pltpu.CompilerParams(dimension_semantics=("arbitrary",)),
    )
    xf, xl = pack_rows(press_bar, press_bar, theta_bar, theta_bar, winds, winds)
    yf, yl = pack_cols(press_bar, press_bar, theta_bar, theta_bar, winds, winds)
    lz, nblk = block_levels, nblk_main

    f4 = jnp.stack(
        [urban_frac, urban_class.astype(jnp.float32), height_bin.astype(jnp.float32), canopy_layers.astype(jnp.float32)]
    )
    small = jnp.concatenate([theta[:kc], f4], axis=0)
    n_small = small.shape[0]
    n_items = n_small * 3

    def item_rows(sel):
        e = small[:, sel, :].reshape(n_items, cols)
        return jnp.pad(e, ((0, levels - n_items), (0, 0)))[None]

    def item_cols(sel):
        e = jnp.swapaxes(small[:, :, sel], 1, 2).reshape(n_items, rows)
        return jnp.pad(e, ((0, levels - n_items), (0, 0)))[:, :, None]

    xn = from_side(jnp.concatenate([xf, item_rows(slice(0, 3))], axis=0), "gx", 1)
    xp = from_side(jnp.concatenate([xl, item_rows(slice(rows - 3, rows))], axis=0), "gx", -1)

    def corner_block(sel, width):
        c = jnp.concatenate([xn[0:4, :, sel], xp[0:4, :, sel]], axis=0)
        c = jnp.swapaxes(c, 0, 1)
        return jnp.pad(c, ((0, 0), (0, 0), (0, width - 4)))

    yfe = jnp.concatenate([yf, item_cols(slice(0, 3))], axis=2)
    yle = jnp.concatenate([yl, item_cols(slice(cols - 3, cols))], axis=2)
    yfe = jnp.concatenate([yfe, corner_block(slice(0, 4), yfe.shape[2])], axis=1)
    yle = jnp.concatenate([yle, corner_block(slice(cols - 4, cols), yle.shape[2])], axis=1)
    yn = from_side(yfe, "gy", 1)
    yp = from_side(yle, "gy", -1)
    x8n = xn[9, :n_items].reshape(n_small, 3, cols)
    x8p = xp[10, :n_items].reshape(n_small, 3, cols)
    y8n = jnp.swapaxes(yn[:n_items, :rows, 9].reshape(n_small, 3, rows), 1, 2)
    y8p = jnp.swapaxes(yp[:n_items, :rows, 10].reshape(n_small, 3, rows), 1, 2)

    ix = lax.axis_index("gx")
    iy = lax.axis_index("gy")
    nx, ny = lax.axis_size("gx"), lax.axis_size("gy")
    r = jnp.arange(rext, dtype=jnp.int32)[:, None]
    cc = jnp.arange(cext, dtype=jnp.int32)[None, :]
    row_ok = (r < rows) | ((r < rows + 4) & (ix < nx - 1)) | ((r >= rext - 4) & (ix > 0))
    col_ok = (cc < cols) | ((cc < cols + 4) & (iy < ny - 1)) | ((cc >= cext - 4) & (iy > 0))
    mask = (row_ok & col_ok).astype(jnp.float32)
    bp8 = bin_profile[:, :kc].reshape(-1)

    zero1 = jnp.zeros((1,), jnp.float32)
    lower = jnp.concatenate([zero1, -sound_coef[:-1]])
    upper = jnp.concatenate([-sound_coef[1:], zero1])
    middle = 1.0 + 2.0 * sound_coef

    ph0 = lambda p, b: (jnp.where(p == 0, b, nblk - 1), 0, 0)
    ph2 = lambda p, b: (jnp.where(p == 2, b, 0), 0, 0)
    ph02 = lambda p, b: (jnp.where(p == 1, nblk - 1, b), 0, 0)
    const3 = lambda p, b: (0, 0, 0)
    const2 = lambda p, b: (0, 0)
    smem = pl.BlockSpec(memory_space=pltpu.SMEM)
    in_specs = [
        smem, smem, smem, smem, smem,
        pl.BlockSpec((lz, rows, cols), ph0),
        pl.BlockSpec((lz, rows, cols), ph2),
        pl.BlockSpec((None, lz, rows, cols), lambda p, b: (0, jnp.where(p == 2, b, 0), 0, 0)),
        pl.BlockSpec((None, lz, rows, cols), lambda p, b: (1, jnp.where(p == 2, b, 0), 0, 0)),
        pl.BlockSpec((10, levels, cols), const3),
        pl.BlockSpec((11, levels, cols), const3),
        pl.BlockSpec((lz, rext, 10), ph02),
        pl.BlockSpec((lz, rext, 11), ph02),
        pl.BlockSpec((kc, rows, cols), const3),
        pl.BlockSpec((n_small, 3, cols), const3),
        pl.BlockSpec((n_small, 3, cols), const3),
        pl.BlockSpec((n_small, rows, 3), const3),
        pl.BlockSpec((n_small, rows, 3), const3),
        pl.BlockSpec((4, rows, cols), const3),
        pl.BlockSpec((rows, cols), const2),
        pl.BlockSpec((rext, cext), const2),
    ]
    out_specs = [
        pl.BlockSpec((lz, rows, cols), ph2),
        pl.BlockSpec((lz, rows, cols), ph2),
        pl.BlockSpec((rows, cols), const2),
        pl.BlockSpec((rows, cols), const2),
    ]
    out_shape = [
        jax.ShapeDtypeStruct((levels, rows, cols), jnp.float32),
        jax.ShapeDtypeStruct((levels, rows, cols), jnp.float32),
        jax.ShapeDtypeStruct((rows, cols), jnp.float32),
        jax.ShapeDtypeStruct((rows, cols), jnp.float32),
    ]
    scratch = [
        pltpu.VMEM((levels, rext, cext), jnp.float32),
        pltpu.VMEM((levels, rext, cext), jnp.float32),
        pltpu.VMEM((rext, cext), jnp.float32),
        pltpu.VMEM((rext, cext), jnp.float32),
        pltpu.VMEM((1, cext), jnp.float32),
        pltpu.VMEM((levels, 1, cext), jnp.float32),
        pltpu.VMEM((levels, 1, cext), jnp.float32),
    ]
    call = pl.pallas_call(
        kernel,
        grid=(3, nblk),
        in_specs=in_specs,
        out_specs=out_specs,
        out_shape=out_shape,
        scratch_shapes=scratch,
        compiler_params=pltpu.CompilerParams(
            dimension_semantics=("arbitrary", "arbitrary"),
            vmem_limit_bytes=56 * 1024 * 1024,
        ),
    )
    tg, pg, fg, wg = call(
        lower, middle, upper, bp8, class_drag,
        press_bar, theta_bar, winds, winds, xn, xp, yn, yp,
        theta, x8n, x8p, y8n, y8p, f4, wall_temp, mask,
    )
    return tg, pg, fg, wg


def extend_xla(main, rows, cols, corner):
    levels = main.shape[0]
    if corner is None:
        corner = jnp.zeros((levels, rows.shape[1], cols.shape[2]), main.dtype)
    return jnp.concatenate(
        [jnp.concatenate([main, rows], axis=1), jnp.concatenate([cols, corner], axis=1)], axis=2
    )


def solution(mesh):
    in_specs = (
        P(None, "gx", "gy"),
        P(None, None, "gx", "gy"),
        P(None, "gx", "gy"),
        P(None, "gx", "gy"),
        P("gx", "gy"),
        P("gx", "gy"),
        P("gx", "gy"),
        P("gx", "gy"),
        P("gx", "gy"),
        P(),
        P(),
        P(),
    )
    out_specs = (P(None, "gx", "gy"), P(None, "gx", "gy"), P("gx", "gy"), P("gx", "gy"))
    return jax.shard_map(
        per_device, mesh=mesh, in_specs=in_specs, out_specs=out_specs, check_vma=False
    )
```

```python
import functools

import jax
import jax.numpy as jnp
from jax import lax
from jax.experimental import pallas as pl
from jax.experimental.pallas import tpu as pltpu
from jax.sharding import PartitionSpec as P

courant = 0.3
diffusion = 0.1
buoyancy = 0.5
canopy_levels = 8
halo_rows = 8
strip = 128
block_levels = 20
pack_levels = 60


def from_side(x, axis, delta):
    n = lax.axis_size(axis)
    if delta > 0:
        pairs = [(i + delta, i) for i in range(n - delta)]
    else:
        pairs = [(i, i - delta) for i in range(n + delta)]
    return lax.ppermute(x, axis, pairs)


def from_corner(x, dx, dy):
    nx, ny = lax.axis_size("gx"), lax.axis_size("gy")
    pairs = []
    for ix in range(nx):
        for iy in range(ny):
            sx, sy = ix + dx, iy + dy
            if 0 <= sx < nx and 0 <= sy < ny:
                pairs.append((sx * ny + sy, ix * ny + iy))
    return lax.ppermute(x, ("gx", "gy"), pairs)


def row_halo(f, lo, hi):
    levels, rows, cols = f.shape
    parts = []
    if hi:
        parts.append(from_side(f[:, :hi, :], "gx", 1))
    parts.append(jnp.zeros((levels, halo_rows - hi - lo, cols), f.dtype))
    if lo:
        parts.append(from_side(f[:, rows - lo :, :], "gx", -1))
    return jnp.concatenate(parts, axis=1)


def col_halo(f, lo, hi):
    levels, rows, cols = f.shape
    parts = []
    if hi:
        parts.append(from_side(f[:, :, :hi], "gy", 1))
    parts.append(jnp.zeros((levels, rows, strip - hi - lo), f.dtype))
    if lo:
        parts.append(from_side(f[:, :, cols - lo :], "gy", -1))
    return jnp.concatenate(parts, axis=2)


def corner_rows(f, w):
    levels, rows, cols = f.shape
    mid = jnp.zeros((levels, w, strip - 2 * w), f.dtype)
    gap = jnp.zeros((levels, halo_rows - 2 * w, strip), f.dtype)
    top = jnp.concatenate(
        [from_corner(f[:, :w, :w], 1, 1), mid, from_corner(f[:, :w, cols - w :], 1, -1)], axis=2
    )
    bottom = jnp.concatenate(
        [from_corner(f[:, rows - w :, :w], -1, 1), mid, from_corner(f[:, rows - w :, cols - w :], -1, -1)],
        axis=2,
    )
    return jnp.concatenate([top, gap, bottom], axis=1)


def ahead(x, k, axis):
    if k == 0:
        return x
    n = x.shape[axis]
    return pltpu.roll(x, (-k) % n, axis)


def forward_tend(f, u, axis):
    fm2, fm1, f0, f1, f2, f3 = [ahead(f, k, axis) for k in (-2, -1, 0, 1, 2, 3)]
    a_sum = (fm2 + f3) - 8.0 * (fm1 + f2) + 37.0 * (f0 + f1)
    b_sum = (fm2 - f3) - 5.0 * (fm1 - f2) + 10.0 * (f0 - f1)
    flux = (u * a_sum + jnp.abs(u) * b_sum) * (1.0 / 60.0)
    return -courant * (flux - ahead(flux, -1, axis))


def adjoint_tend(f, u, axis):
    g = courant * (ahead(f, 1, axis) - f)
    pu = u * g
    qu = jnp.abs(u) * g
    total = (
        ahead(pu + qu, 2, axis)
        + ahead(-8.0 * pu - 5.0 * qu, 1, axis)
        + (37.0 * pu + 10.0 * qu)
        + ahead(37.0 * pu - 10.0 * qu, -1, axis)
        + ahead(-8.0 * pu + 5.0 * qu, -2, axis)
        + ahead(pu - qu, -3, axis)
    )
    return total * (1.0 / 60.0)


def laplace(q):
    return ahead(q, 1, 0) + ahead(q, -1, 0) + ahead(q, 1, 1) + ahead(q, -1, 1) - 4.0 * q


def extend(main, rows, cols):
    return jnp.concatenate([jnp.concatenate([main, rows], axis=0), cols], axis=1)


def pack_rows_kernel(pbf, pbl, tbf, tbl, u0f, u0l, xf, xl):
    lz = pbf.shape[0]

    def body(j, c):
        k = pl.program_id(0) * lz + j
        xf[:, k, :] = jnp.concatenate([pbf[j][0:4], tbf[j][0:3], u0f[j][0:2]], axis=0)
        xl[:, k, :] = jnp.concatenate([pbl[j][4:8], tbl[j][5:8], u0l[j][5:8]], axis=0)
        return c

    lax.fori_loop(0, lz, body, 0)


def pack_cols_kernel(pcf, pcl, tcf, tcl, ucf, ucl, yf, yl):
    lz = pcf.shape[0]
    rows = pcf.shape[1]
    lane = lax.broadcasted_iota(jnp.int32, (rows, strip), 1)

    def body(j, c):
        a, b, u = pcf[j], tcf[j], ucf[j]
        first = jnp.where(lane < 4, a, jnp.where(lane < 7, pltpu.roll(b, 4, 1), pltpu.roll(u, 7, 1)))
        yf[j] = first[:, :9]
        a, b, u = pcl[j], tcl[j], ucl[j]
        last = jnp.where(
            lane < 4, pltpu.roll(a, 4, 1), jnp.where(lane < 7, pltpu.roll(b, 7, 1), pltpu.roll(u, 10, 1))
        )
        yl[j] = last[:, :10]
        return c

    lax.fori_loop(0, lz, body, 0)


def lane_strip(near, far, width):
    rows = near.shape[0]
    a = jnp.concatenate([near, jnp.zeros((rows, strip - width), jnp.float32)], axis=1)
    b = jnp.concatenate([far, jnp.zeros((rows, strip - width), jnp.float32)], axis=1)
    return a + pltpu.roll(b, strip - width, 1)


def kernel(
    lo_ref, mid_ref, up_ref, bp_ref, cd_ref,
    pbm, tbm, u0m, u1m, xn, xp, yn, yp,
    thm, x8n, x8p, y8n, y8p, f4, wall, mask,
    tg_out, pg_out, fg_out, wg_out,
    dd, qa, car_a, car_b, cpc, cp1, cq2,
):
    phase = pl.program_id(0)
    blk = pl.program_id(1)
    nblk = pl.num_programs(1)
    lz = pbm.shape[0]
    rows, cols = pbm.shape[1], pbm.shape[2]
    wide = cpc.shape[1]
    rext = yn.shape[1]
    lane = lax.broadcasted_iota(jnp.int32, (rext, strip), 1)

    def coef(ref, k):
        return jnp.full((1, wide), ref[k], jnp.float32)

    def ystrip(j, off, wn, wp):
        n = jnp.concatenate([yn[j], jnp.zeros((rext, strip - yn.shape[2]), jnp.float32)], axis=1)
        p = jnp.concatenate([yp[j], jnp.zeros((rext, strip - yp.shape[2]), jnp.float32)], axis=1)
        n = pltpu.roll(n, (strip - off) % strip, 1)
        p = pltpu.roll(p, strip - wp - off, 1)
        return jnp.where(lane < wn, n, jnp.where(lane >= strip - wp, p, 0.0))

    def press_ext(j, k):
        xr = jnp.concatenate([pbm[j], xn[:, k, :][0:4], xp[:, k, :][0:4]], axis=0)
        return jnp.concatenate([xr, ystrip(j, 0, 4, 4)], axis=1)

    @pl.when(phase == 0)
    def _():
        @pl.when(blk == 0)
        def _():
            car_a[...] = jnp.zeros(car_a.shape, jnp.float32)
            cpc[...] = jnp.zeros(cpc.shape, jnp.float32)

        def body(j, c):
            k = blk * lz + j
            ak = coef(lo_ref, k)
            r = 1.0 / (coef(mid_ref, k) - ak * cpc[...])
            cp = coef(up_ref, k) * r
            cpc[...] = cp
            cp1[k] = cp
            d = press_ext(j, k)
            dn = (d - ak * car_a[...]) * r
            car_a[...] = dn
            dd[k] = dn
            return c

        lax.fori_loop(0, lz, body, 0)

    @pl.when(phase == 1)
    def _():
        @pl.when(blk == 0)
        def _():
            car_a[...] = jnp.zeros(car_a.shape, jnp.float32)
            car_b[...] = jnp.zeros(car_b.shape, jnp.float32)
            cpc[...] = jnp.zeros(cpc.shape, jnp.float32)

        def body(j, c):
            k = (nblk - 1 - blk) * lz + (lz - 1 - j)
            x = dd[k] - cp1[k] * car_a[...]
            car_a[...] = x
            qa[k] = x
            pb1 = (x + diffusion * laplace(x)) * mask[...]
            ck = coef(up_ref, k)
            s = 1.0 / (coef(mid_ref, k) - ck * cpc[...])
            cq = coef(lo_ref, k) * s
            cpc[...] = cq
            cq2[k] = cq
            e = (pb1 - ck * car_b[...]) * s
            car_b[...] = e
            dd[k] = e
            return c

        lax.fori_loop(0, lz, body, 0)

    @pl.when(phase == 2)
    def _():
        @pl.when(blk == 0)
        def _():
            car_a[...] = jnp.zeros(car_a.shape, jnp.float32)

        def field_ext(i):
            xr = jnp.concatenate(
                [f4[i], x8n[8 + i], jnp.zeros((2, cols), jnp.float32), x8p[8 + i]], axis=0
            )
            ys = jnp.concatenate(
                [lane_strip(y8n[8 + i], y8p[8 + i], 3), jnp.zeros((halo_rows, strip), jnp.float32)], axis=0
            )
            return jnp.concatenate([xr, ys], axis=1)

        def level(j, canopy, acc):
            k = blk * lz + j
            qb = dd[k] - cq2[k] * car_a[...]
            car_a[...] = qb
            pg = qb + diffusion * laplace(qb)
            pg_out[j] = pg[:rows, :cols]
            xnj, xpj = xn[:, k, :], xp[:, k, :]
            tbx = jnp.concatenate([tbm[j], xnj[4:7], jnp.zeros((2, cols), jnp.float32), xpj[4:7]], axis=0)
            tby = ystrip(j, 4, 3, 3)
            th2b = jnp.concatenate([tbx, tby], axis=1) + buoyancy * (qa[k] + qb)
            if canopy:
                ud, cls, hb, lay = acc[2]
                prof = jnp.zeros(hb.shape, jnp.float32)
                for bb in range(bp_ref.shape[0] // canopy_levels):
                    prof = jnp.where(hb == float(bb), bp_ref[bb * canopy_levels + j], prof)
                act = jnp.where(lay > j.astype(jnp.float32), 1.0, 0.0)
                am = ud * prof * act
                th1b = (1.0 - am) * th2b
            else:
                th1b = th2b
            u0e = jnp.concatenate([u0m[j], xnj[7:9], jnp.zeros((3, cols), jnp.float32), xpj[7:10]], axis=0)
            u1e = jnp.concatenate([u1m[j], ystrip(j, 7, 2, 3)[:rows]], axis=1)
            adv = adjoint_tend(th1b[:, :cols], u0e, 0)[:rows, :] + adjoint_tend(th1b[:rows, :], u1e, 1)[:, :cols]
            tg_out[j] = th1b[:rows, :cols] + adv
            if canopy:
                th = thm[j]
                thx = jnp.concatenate([th, x8n[j], jnp.zeros((2, cols), jnp.float32), x8p[j]], axis=0)
                thy = jnp.concatenate([th, lane_strip(y8n[j], y8p[j], 3)], axis=1)
                fx = forward_tend(thx, u0e, 0)[:rows, :]
                fy = forward_tend(thy, u1e, 1)[:, :cols]
                first = th + (fx + fy)
                sb = th2b[:rows, :cols]
                fg, wg, fields, drag = acc
                dpa = drag * prof[:rows, :cols] * act[:rows, :cols]
                fg = fg + dpa * (wall[...] - first) * sb
                wg = wg + am[:rows, :cols] * sb
                acc = (fg, wg, fields, drag)
            return acc

        @pl.when(blk == 0)
        def _():
            zero = jnp.zeros((rows, cols), jnp.float32)
            cls = field_ext(1)
            drag = jnp.zeros(cls.shape, jnp.float32)
            for c in range(cd_ref.shape[0]):
                drag = jnp.where(cls == float(c), cd_ref[c], drag)
            ud = field_ext(0) * drag
            fields = (ud, cls, field_ext(2), field_ext(3))
            fg, wg, _, _ = lax.fori_loop(
                0, canopy_levels, lambda j, a: level(j, True, a), (zero, zero, fields, drag[:rows, :cols])
            )
            fg_out[...] = fg
            wg_out[...] = wg
            lax.fori_loop(canopy_levels, lz, lambda j, a: level(j, False, a), 0)

        @pl.when(blk > 0)
        def _():
            lax.fori_loop(0, lz, lambda j, a: level(j, False, a), 0)


def per_device(
    theta, winds, theta_bar, press_bar, urban_frac, wall_temp, urban_class, canopy_layers,
    height_bin, class_drag, bin_profile, sound_coef,
):
    levels, rows, cols = theta.shape
    rext, cext = rows + halo_rows, cols + strip
    lz = block_levels
    nblk = levels // lz
    kc = canopy_levels
    rb, cb = rows // 8 - 1, cols // strip - 1

    lvl = lambda b: (b, 0, 0)
    lz, nblk_main = pack_levels, nblk
    nblk = levels // lz
    pack_rows = pl.pallas_call(
        pack_rows_kernel,
        grid=(nblk,),
        in_specs=[
            pl.BlockSpec((lz, 8, cols), lvl),
            pl.BlockSpec((lz, 8, cols), lambda b: (b, rb, 0)),
            pl.BlockSpec((lz, 8, cols), lvl),
            pl.BlockSpec((lz, 8, cols), lambda b: (b, rb, 0)),
            pl.BlockSpec((None, lz, 8, cols), lambda b: (0, b, 0, 0)),
            pl.BlockSpec((None, lz, 8, cols), lambda b: (0, b, rb, 0)),
        ],
        out_specs=[pl.BlockSpec((9, levels, cols), lambda b: (0, 0, 0)), pl.BlockSpec((10, levels, cols), lambda b: (0, 0, 0))],
        out_shape=[jax.ShapeDtypeStruct((9, levels, cols), jnp.float32), jax.ShapeDtypeStruct((10, levels, cols), jnp.float32)],
        compiler_params=pltpu.CompilerParams(dimension_semantics=("arbitrary",)),
    )
    pack_cols = pl.pallas_call(
        pack_cols_kernel,
        grid=(nblk,),
        in_specs=[
            pl.BlockSpec((lz, rows, strip), lvl),
            pl.BlockSpec((lz, rows, strip), lambda b: (b, 0, cb)),
            pl.BlockSpec((lz, rows, strip), lvl),
            pl.BlockSpec((lz, rows, strip), lambda b: (b, 0, cb)),
            pl.BlockSpec((None, lz, rows, strip), lambda b: (1, b, 0, 0)),
            pl.BlockSpec((None, lz, rows, strip), lambda b: (1, b, 0, cb)),
        ],
        out_specs=[pl.BlockSpec((lz, rows, 9), lvl), pl.BlockSpec((lz, rows, 10), lvl)],
        out_shape=[jax.ShapeDtypeStruct((levels, rows, 9), jnp.float32), jax.ShapeDtypeStruct((levels, rows, 10), jnp.float32)],
        compiler_params=pltpu.CompilerParams(dimension_semantics=("arbitrary",)),
    )
    xf, xl = pack_rows(press_bar, press_bar, theta_bar, theta_bar, winds, winds)
    yf, yl = pack_cols(press_bar, press_bar, theta_bar, theta_bar, winds, winds)
    lz, nblk = block_levels, nblk_main

    f4 = jnp.stack(
        [urban_frac, urban_class.astype(jnp.float32), height_bin.astype(jnp.float32), canopy_layers.astype(jnp.float32)]
    )
    small = jnp.concatenate([theta[:kc], f4], axis=0)
    n_small = small.shape[0]
    n_items = n_small * 3

    def item_rows(sel):
        e = small[:, sel, :].reshape(n_items, cols)
        return jnp.pad(e, ((0, levels - n_items), (0, 0)))[None]

    def item_cols(sel):
        e = jnp.swapaxes(small[:, :, sel], 1, 2).reshape(n_items, rows)
        return jnp.pad(e, ((0, levels - n_items), (0, 0)))[:, :, None]

    xn = from_side(jnp.concatenate([xf, item_rows(slice(0, 3))], axis=0), "gx", 1)
    xp = from_side(jnp.concatenate([xl, item_rows(slice(rows - 3, rows))], axis=0), "gx", -1)

    def corner_block(sel, width):
        c = jnp.concatenate([xn[0:4, :, sel], xp[0:4, :, sel]], axis=0)
        c = jnp.swapaxes(c, 0, 1)
        return jnp.pad(c, ((0, 0), (0, 0), (0, width - 4)))

    yfe = jnp.concatenate([yf, item_cols(slice(0, 3))], axis=2)
    yle = jnp.concatenate([yl, item_cols(slice(cols - 3, cols))], axis=2)
    yfe = jnp.concatenate([yfe, corner_block(slice(0, 4), yfe.shape[2])], axis=1)
    yle = jnp.concatenate([yle, corner_block(slice(cols - 4, cols), yle.shape[2])], axis=1)
    yn = from_side(yfe, "gy", 1)
    yp = from_side(yle, "gy", -1)
    x8n = xn[9, :n_items].reshape(n_small, 3, cols)
    x8p = xp[10, :n_items].reshape(n_small, 3, cols)
    y8n = jnp.swapaxes(yn[:n_items, :rows, 9].reshape(n_small, 3, rows), 1, 2)
    y8p = jnp.swapaxes(yp[:n_items, :rows, 10].reshape(n_small, 3, rows), 1, 2)

    ix = lax.axis_index("gx")
    iy = lax.axis_index("gy")
    nx, ny = lax.axis_size("gx"), lax.axis_size("gy")
    r = jnp.arange(rext, dtype=jnp.int32)[:, None]
    cc = jnp.arange(cext, dtype=jnp.int32)[None, :]
    row_ok = (r < rows) | ((r < rows + 4) & (ix < nx - 1)) | ((r >= rext - 4) & (ix > 0))
    col_ok = (cc < cols) | ((cc < cols + 4) & (iy < ny - 1)) | ((cc >= cext - 4) & (iy > 0))
    mask = (row_ok & col_ok).astype(jnp.float32)
    bp8 = bin_profile[:, :kc].reshape(-1)

    zero1 = jnp.zeros((1,), jnp.float32)
    lower = jnp.concatenate([zero1, -sound_coef[:-1]])
    upper = jnp.concatenate([-sound_coef[1:], zero1])
    middle = 1.0 + 2.0 * sound_coef

    ph0 = lambda p, b: (jnp.where(p == 0, b, nblk - 1), 0, 0)
    ph2 = lambda p, b: (jnp.where(p == 2, b, 0), 0, 0)
    ph02 = lambda p, b: (jnp.where(p == 1, nblk - 1, b), 0, 0)
    const3 = lambda p, b: (0, 0, 0)
    const2 = lambda p, b: (0, 0)
    smem = pl.BlockSpec(memory_space=pltpu.SMEM)
    in_specs = [
        smem, smem, smem, smem, smem,
        pl.BlockSpec((lz, rows, cols), ph0),
        pl.BlockSpec((lz, rows, cols), ph2),
        pl.BlockSpec((None, lz, rows, cols), lambda p, b: (0, jnp.where(p == 2, b, 0), 0, 0)),
        pl.BlockSpec((None, lz, rows, cols), lambda p, b: (1, jnp.where(p == 2, b, 0), 0, 0)),
        pl.BlockSpec((10, levels, cols), const3),
        pl.BlockSpec((11, levels, cols), const3),
        pl.BlockSpec((lz, rext, 10), ph02),
        pl.BlockSpec((lz, rext, 11), ph02),
        pl.BlockSpec((kc, rows, cols), const3),
        pl.BlockSpec((n_small, 3, cols), const3),
        pl.BlockSpec((n_small, 3, cols), const3),
        pl.BlockSpec((n_small, rows, 3), const3),
        pl.BlockSpec((n_small, rows, 3), const3),
        pl.BlockSpec((4, rows, cols), const3),
        pl.BlockSpec((rows, cols), const2),
        pl.BlockSpec((rext, cext), const2),
    ]
    out_specs = [
        pl.BlockSpec((lz, rows, cols), ph2),
        pl.BlockSpec((lz, rows, cols), ph2),
        pl.BlockSpec((rows, cols), const2),
        pl.BlockSpec((rows, cols), const2),
    ]
    out_shape = [
        jax.ShapeDtypeStruct((levels, rows, cols), jnp.float32),
        jax.ShapeDtypeStruct((levels, rows, cols), jnp.float32),
        jax.ShapeDtypeStruct((rows, cols), jnp.float32),
        jax.ShapeDtypeStruct((rows, cols), jnp.float32),
    ]
    scratch = [
        pltpu.VMEM((levels, rext, cext), jnp.float32),
        pltpu.VMEM((levels, rext, cext), jnp.float32),
        pltpu.VMEM((rext, cext), jnp.float32),
        pltpu.VMEM((rext, cext), jnp.float32),
        pltpu.VMEM((1, cext), jnp.float32),
        pltpu.VMEM((levels, 1, cext), jnp.float32),
        pltpu.VMEM((levels, 1, cext), jnp.float32),
    ]
    call = pl.pallas_call(
        kernel,
        grid=(3, nblk),
        in_specs=in_specs,
        out_specs=out_specs,
        out_shape=out_shape,
        scratch_shapes=scratch,
        compiler_params=pltpu.CompilerParams(
            dimension_semantics=("arbitrary", "arbitrary"),
            vmem_limit_bytes=56 * 1024 * 1024,
        ),
    )
    tg, pg, fg, wg = call(
        lower, middle, upper, bp8, class_drag,
        press_bar, theta_bar, winds, winds, xn, xp, yn, yp,
        theta, x8n, x8p, y8n, y8p, f4, wall_temp, mask,
    )
    return tg, pg, fg, wg


def extend_xla(main, rows, cols, corner):
    levels = main.shape[0]
    if corner is None:
        corner = jnp.zeros((levels, rows.shape[1], cols.shape[2]), main.dtype)
    return jnp.concatenate(
        [jnp.concatenate([main, rows], axis=1), jnp.concatenate([cols, corner], axis=1)], axis=2
    )


def solution(mesh):
    in_specs = (
        P(None, "gx", "gy"),
        P(None, None, "gx", "gy"),
        P(None, "gx", "gy"),
        P(None, "gx", "gy"),
        P("gx", "gy"),
        P("gx", "gy"),
        P("gx", "gy"),
        P("gx", "gy"),
        P("gx", "gy"),
        P(),
        P(),
        P(),
    )
    out_specs = (P(None, "gx", "gy"), P(None, "gx", "gy"), P("gx", "gy"), P("gx", "gy"))
    return jax.shard_map(
        per_device, mesh=mesh, in_specs=in_specs, out_specs=out_specs, check_vma=False
    )
```
